32 devices in a mesh: groups: 2 (over y), bricks: 4 (over z), heads: 4 (over x, core).
Axes of the slice: x: 2, y: 2, z: 4, core: 2. Of those that a mesh axis runs over, the one named last changes fastest.
Arguments:
- voxel_feats: bfloat16 [4096, 1024], P(('groups', 'bricks'), 'heads'), parts along dimension 0, may hold values from -6 to 6
- face_open: int32 [8], P('groups'), parts along dimension 0, may hold values from 0 to 1
- pattern: int32 [8, 4], P('groups'), parts along dimension 0, may hold values from 0 to 1, as said below
- conv_weight: bfloat16 [27, 1024], P(None, 'heads'), may hold values from -1.25 to 1.25
- conv_bias: bfloat16 [1024], P('heads'), may hold values from -0.5 to 0.5
- gain_one: bfloat16 [1024], replicated, may hold values from 0.099609375 to 1.8984375
- query_weight: bfloat16 [1024, 1024], P(None, 'heads'), may hold values from -3 to 3
- key_weight: bfloat16 [1024, 1024], P(None, 'heads'), may hold values from -3 to 3
- value_weight: bfloat16 [1024, 1024], P(None, 'heads'), may hold values from -0.1875 to 0.1875
- out_weight: bfloat16 [1024, 1024], P('heads'), may hold values from -0.1875 to 0.1875
- gain_two: bfloat16 [1024], replicated, may hold values from 0.099609375 to 1.8984375
- up_weight: bfloat16 [1024, 4096], P(None, 'heads'), may hold values from -0.1875 to 0.1875
- down_weight: bfloat16 [4096, 1024], P('heads'), may hold values from -0.09375 to 0.09375
Outputs:
- block_out: bfloat16 [4096, 1024], P(('groups', 'bricks'), 'heads'), parts along dimension 0
The draws below stay inside these ranges and needn't reach their ends.
There are 2 independent parts, one for each index of `groups`. The reference program is written for one: setup_inputs(seed, part) draws one part's arguments, and reference() takes and returns one part's arrays. A program takes and returns all parts, laid end to end along the dimension named above; an argument that names none is the same for every part. Nothing has to cross between parts.
Inputs may be any that keep to these rules, and one draw needn't show every extreme that they name: pattern is 0 or 1; every brick attends to itself; each query brick attends to 3 or more key bricks, and some query brick to all 4.
All inputs are finite; a program needn't handle non-finite values.
Results may differ from the reference program's by a relative error of at most 0.012.
Values may be sent and summed in bfloat16 or wider, within the bound.
No kernel may reach another device: no remote copies, remote signals or barrier semaphores. Data moves between devices by JAX's collectives and lax.ppermute only.
A program may use at most 64 MiB of HBM per device.

```python
import jax
import jax.numpy as jnp
from jax import lax

EDGE = 8
HEAD_DIM = 64
HEADS = 16
FF = 4096
VOX = 512
D = 1024
BRICKS = 4
NVOX = 2048


def draw_face_open(key, part):
    levels = jax.random.randint(jax.random.fold_in(key, 7), (BRICKS,), 0, 4)
    opened = (levels < 3).astype(jnp.int32)
    positions = jnp.arange(BRICKS)
    closed_at = (part + 1) % BRICKS
    forced_at = (part + 2) % BRICKS
    opened = jnp.where(positions == closed_at, 0, opened)
    opened = jnp.where(positions == forced_at, 1, opened)
    return opened.astype(jnp.int32)


def draw_pattern(key, part):
    split_keys = jax.random.split(key, 3)
    lowest = 3 * BRICKS // 4 - 1
    extra = jax.random.randint(split_keys[0], (BRICKS,), lowest, BRICKS)
    chosen_row = jax.random.randint(split_keys[1], (), 0, BRICKS)
    extra = jnp.where(jnp.arange(BRICKS) == chosen_row, BRICKS - 1, extra)
    ranking = jax.vmap(lambda row_key: jax.random.permutation(row_key, BRICKS - 1))(jax.random.split(split_keys[2], BRICKS))
    row_ids = jnp.arange(BRICKS)[:, None]
    col_ids = jnp.arange(BRICKS)[None, :]
    offset = (col_ids - row_ids) % BRICKS
    rank_of = jnp.take_along_axis(ranking, jnp.maximum(offset - 1, 0), axis=1)
    linked = (offset == 0) | (rank_of < extra[:, None])
    return linked.astype(jnp.int32)


def base_weight(key, salt):
    noise = jax.random.normal(jax.random.fold_in(key, salt), (D, D), jnp.float32)
    return jnp.clip(noise, -6.0, 6.0) / jnp.sqrt(jnp.float32(D))


def draw_query_weight(key, part):
    matrix = base_weight(key, 1)
    return matrix.astype(jnp.bfloat16)


def draw_key_weight(key, part):
    matrix = base_weight(key, 2)
    return matrix.astype(jnp.bfloat16)


def level_of(own_key, extent, cuts, smallest, high):
    factor_of, own = 1.0, jax.random.fold_in(own_key, 6)
    for axis_at, parts in cuts:
        heights = jnp.exp(jax.random.uniform(jax.random.fold_in(own, axis_at), (parts,), jnp.float32, smallest / len(cuts), high / len(cuts)))
        factor_of = factor_of * jnp.repeat(heights, extent[axis_at] // parts).reshape([-1 if axis == axis_at else 1 for axis in range(len(extent))])
    return factor_of


def bell_draw(own_key, shape, deviation, reach, cuts=(), kind=jnp.bfloat16):
    values = deviation * jax.random.normal(own_key, shape, jnp.float32)
    if cuts:
        values = values * level_of(own_key, shape, cuts, -0.22, 0.18)
    return jnp.clip(values, -reach, reach).astype(kind)


def setup_inputs(seed: int = 0, part: int = 0) -> dict:
    seeds = jax.random.split(jax.random.key(seed), 14)
    part_keys = jax.random.split(jax.random.fold_in(seeds[13], part), 14)
    voxel_feats = bell_draw(part_keys[0], (NVOX, D), 1.0, 6.0, ((0, 4), (1, 4)))
    face_open = draw_face_open(jax.random.fold_in(jax.random.fold_in(seeds[13], part), 71), part)
    pattern = draw_pattern(jax.random.fold_in(jax.random.fold_in(seeds[13], part), 71), part)
    conv_weight = bell_draw(seeds[3], (27, D), 27 ** -0.5, 1.25, ((1, 4),))
    conv_bias = jnp.clip(jax.random.uniform(seeds[4], (D,), jnp.float32, -0.5, 0.5) * level_of(seeds[4], (D,), ((0, 4),), -0.4, 0.0), -0.5, 0.5).astype(jnp.bfloat16)
    gain_one = jnp.clip(1.0 + 0.18 * jax.random.normal(seeds[5], (D,), jnp.float32), 0.099609375, 1.8984375).astype(jnp.bfloat16)
    query_weight = draw_query_weight(jax.random.fold_in(seeds[13], 71), part)
    key_weight = draw_key_weight(jax.random.fold_in(seeds[13], 71), part)
    value_weight = bell_draw(seeds[8], (D, D), D ** -0.5, 0.1875, ((1, 4),))
    out_weight = bell_draw(seeds[9], (D, D), D ** -0.5, 0.1875, ((0, 4),))
    gain_two = jnp.clip(1.0 + 0.18 * jax.random.normal(seeds[10], (D,), jnp.float32), 0.099609375, 1.8984375).astype(jnp.bfloat16)
    up_weight = bell_draw(seeds[11], (D, FF), D ** -0.5, 0.1875, ((1, 4),))
    down_weight = bell_draw(seeds[12], (FF, D), FF ** -0.5, 0.09375, ((0, 4),))
    return dict(voxel_feats=voxel_feats, face_open=face_open, pattern=pattern, conv_weight=conv_weight, conv_bias=conv_bias, gain_one=gain_one, query_weight=query_weight, key_weight=key_weight, value_weight=value_weight, out_weight=out_weight, gain_two=gain_two, up_weight=up_weight, down_weight=down_weight)


epsilon = 1e-05

def layer_norm(inputs, gain_vec):
    values = inputs.astype(jnp.float32)
    center = values - lax.optimization_barrier(jnp.mean(values, axis=-1, keepdims=True))
    spread = lax.optimization_barrier(jnp.mean(center * center, axis=-1, keepdims=True))
    return center * lax.rsqrt(spread + epsilon) * gain_vec.astype(jnp.float32)

def depthwise(brick_vals, lower_face, upper_face, conv_weight, conv_bias):
    brick_count = brick_vals.shape[0]
    edge_len = brick_vals.shape[1]
    channels = brick_vals.shape[3]
    layers = jnp.concatenate([lower_face[:, None], brick_vals, upper_face[:, None]], axis=1)
    layers = layers.reshape(brick_count, edge_len + 2, edge_len, edge_len, channels)
    padded = jnp.pad(layers, ((0, 0), (0, 0), (1, 1), (1, 1), (0, 0)))
    weights = conv_weight.astype(jnp.float32)
    summed = jnp.zeros((brick_count, edge_len, edge_len, edge_len, channels), jnp.float32)
    for step_x in range(3):
        for step_y in range(3):
            for step_z in range(3):
                window = padded[:, step_x:step_x + edge_len, step_y:step_y + edge_len, step_z:step_z + edge_len]
                summed = summed + weights[step_x * 9 + step_y * 3 + step_z] * window
    return summed.reshape(brick_count * edge_len ** 3, channels) + conv_bias.astype(jnp.float32)

def reference(voxel_feats, face_open, pattern, conv_weight, conv_bias, gain_one, query_weight, key_weight, value_weight, out_weight, gain_two, up_weight, down_weight):
    face_rows = EDGE * EDGE
    brick_vals = voxel_feats.astype(jnp.float32).reshape(BRICKS, EDGE, face_rows, D)
    brick_ids = jnp.arange(BRICKS).astype(jnp.int32)
    lower_open = jnp.where(brick_ids >= 1, face_open, 0).astype(jnp.float32)
    upper_open = jnp.where(brick_ids + 1 < BRICKS, jnp.roll(face_open, -1), 0).astype(jnp.float32)
    zero_face = jnp.zeros((1, face_rows, D), jnp.float32)
    lower_face = jnp.concatenate([zero_face, brick_vals[:-1, EDGE - 1]], axis=0) * lower_open[:, None, None]
    upper_face = jnp.concatenate([brick_vals[1:, 0], zero_face], axis=0) * upper_open[:, None, None]
    conv_out = depthwise(brick_vals, lower_face, upper_face, conv_weight, conv_bias)
    stream = (voxel_feats.astype(jnp.float32) + conv_out).astype(jnp.bfloat16)
    normed = layer_norm(stream, gain_one).astype(jnp.bfloat16)
    queries = jnp.dot(normed, query_weight, preferred_element_type=jnp.float32).astype(jnp.bfloat16)
    keys_all = jnp.dot(normed, key_weight, preferred_element_type=jnp.float32).astype(jnp.bfloat16)
    values_all = jnp.dot(normed, value_weight, preferred_element_type=jnp.float32).astype(jnp.bfloat16)
    query_cube = queries.astype(jnp.float32).reshape(BRICKS, VOX, HEADS, HEAD_DIM)
    key_heads = jnp.transpose(keys_all.astype(jnp.float32).reshape(NVOX, HEADS, HEAD_DIM), (1, 0, 2))
    value_heads = jnp.transpose(values_all.astype(jnp.float32).reshape(NVOX, HEADS, HEAD_DIM), (1, 0, 2))
    score_scale = HEAD_DIM ** (-0.5)

    def one_brick(brick):
        keep_mask = jnp.repeat(pattern[brick] > 0, VOX, total_repeat_length=NVOX)
        query_one = lax.dynamic_index_in_dim(query_cube, brick, 0, keepdims=False)
        query_heads = jnp.transpose(query_one, (1, 0, 2))

        def one_head(packed):
            query_h, key_h, value_h = packed
            scores = jnp.dot(query_h, jnp.transpose(key_h)) * score_scale
            scores = jnp.where(keep_mask[None, :], scores, -1e+30)
            row_max = lax.optimization_barrier(jnp.max(scores, axis=-1, keepdims=True))
            weights = jnp.exp(scores - row_max)
            row_mass = lax.optimization_barrier(jnp.sum(weights, axis=-1, keepdims=True))
            rounded = lax.optimization_barrier(weights.astype(jnp.bfloat16)).astype(jnp.float32)
            return jnp.dot(rounded, value_h) / row_mass
        per_head = lax.map(one_head, (query_heads, key_heads, value_heads))
        return jnp.transpose(per_head, (1, 0, 2)).astype(jnp.bfloat16).reshape(VOX, D)
    attended = lax.map(one_brick, jnp.arange(BRICKS).astype(jnp.int32)).reshape(NVOX, D)
    projected = jnp.dot(attended, out_weight, preferred_element_type=jnp.float32)
    stream_two = (stream.astype(jnp.float32) + projected).astype(jnp.bfloat16)
    normed_two = layer_norm(stream_two, gain_two).astype(jnp.bfloat16)
    hidden = jax.nn.gelu(jnp.dot(normed_two, up_weight, preferred_element_type=jnp.float32), approximate=True).astype(jnp.bfloat16)
    lowered = jnp.dot(hidden, down_weight, preferred_element_type=jnp.float32)
    return (stream_two.astype(jnp.float32) + lowered).astype(jnp.bfloat16)
```

```python
import functools

import jax
import jax.numpy as jnp
from jax import lax
from jax.experimental import pallas as pl
from jax.experimental.pallas import tpu as pltpu
from jax.sharding import PartitionSpec as P

EDGE = 8
HEAD_DIM = 64


epsilon = 1e-05


def extended_2(value, sides, width):
    for axis, dim in sides:
        size, length = (lax.axis_size(axis), value.shape[dim])
        up = [(i, (i + 1) % size) for i in range(size - 1)]
        down = [(j, i) for i, j in up]
        last = lax.slice_in_dim(value, length - width, length, axis=dim)
        first = lax.slice_in_dim(value, 0, width, axis=dim)
        before = lax.ppermute(last, axis, up)
        after = lax.ppermute(first, axis, down)
        value = jnp.concatenate([before, value, after], axis=dim)
    return value


def layer_norm(inputs, gain_vec):
    values = inputs.astype(jnp.float32)
    center = values - jnp.mean(values, axis=-1, keepdims=True)
    spread = jnp.mean(center * center, axis=-1, keepdims=True)
    return center * lax.rsqrt(spread + epsilon) * gain_vec.astype(jnp.float32)


def depthwise(brick_vals, lower_face, upper_face, conv_weight, conv_bias):
    brick_count = brick_vals.shape[0]
    edge_len = brick_vals.shape[1]
    channels = brick_vals.shape[3]
    layers = jnp.concatenate([lower_face[:, None], brick_vals, upper_face[:, None]], axis=1)
    layers = layers.reshape(brick_count, edge_len + 2, edge_len, edge_len, channels)
    padded = jnp.pad(layers, ((0, 0), (0, 0), (1, 1), (1, 1), (0, 0)))
    weights = conv_weight.astype(jnp.float32)
    summed = jnp.zeros((brick_count, edge_len, edge_len, edge_len, channels), jnp.float32)
    for step_x in range(3):
        for step_y in range(3):
            for step_z in range(3):
                window = padded[
                    :,
                    step_x : step_x + edge_len,
                    step_y : step_y + edge_len,
                    step_z : step_z + edge_len,
                ]
                summed = summed + weights[step_x * 9 + step_y * 3 + step_z] * window
    return summed.reshape(brick_count * edge_len**3, channels) + conv_bias.astype(jnp.float32)


def attention_body(linked_ref, query_ref, key_ref, value_ref, out_ref, max_ref, mass_ref, sum_ref,
                   *, head_count, key_count):
    key_id = pl.program_id(1)
    score_scale = HEAD_DIM ** (-0.5)

    @pl.when(key_id == 0)
    def _start():
        max_ref[...] = jnp.full(max_ref.shape, -1e30, jnp.float32)
        mass_ref[...] = jnp.zeros(mass_ref.shape, jnp.float32)
        sum_ref[...] = jnp.zeros(sum_ref.shape, jnp.float32)

    linked = linked_ref[pl.program_id(0) * key_count + key_id]

    @pl.when(linked > 0)
    def _absorb():
        for head in range(head_count):
            cols = slice(head * HEAD_DIM, (head + 1) * HEAD_DIM)
            query_h = query_ref[:, cols]
            key_h = key_ref[:, cols]
            value_h = value_ref[:, cols]
            scores = lax.dot_general(
                query_h, key_h, (((1,), (1,)), ((), ())), preferred_element_type=jnp.float32
            ) * score_scale
            max_old = max_ref[head]
            max_new = jnp.maximum(max_old, jnp.max(scores, axis=-1, keepdims=True))
            factor = jnp.exp(max_old - max_new)
            weights = jnp.exp(scores - max_new)
            mass_ref[head] = mass_ref[head] * factor + jnp.sum(weights, axis=-1, keepdims=True)
            sum_ref[head] = sum_ref[head] * factor + jnp.dot(
                weights.astype(jnp.bfloat16), value_h, preferred_element_type=jnp.float32
            )
            max_ref[head] = max_new

    @pl.when(key_id == key_count - 1)
    def _finish():
        for head in range(head_count):
            cols = slice(head * HEAD_DIM, (head + 1) * HEAD_DIM)
            out_ref[:, cols] = (sum_ref[head] / mass_ref[head]).astype(out_ref.dtype)


def brick_attention(linked_rows, queries, pair_piece, head_count, key_count, brick_rows):
    row_count, width = queries.shape
    body = functools.partial(attention_body, head_count=head_count, key_count=key_count)
    grid_spec = pltpu.PrefetchScalarGridSpec(
        num_scalar_prefetch=1,
        grid=(row_count // brick_rows, key_count),
        in_specs=[
            pl.BlockSpec((brick_rows, width), lambda i, k, linked: (i, 0)),
            pl.BlockSpec((brick_rows, width), lambda i, k, linked: (k, 0)),
            pl.BlockSpec((brick_rows, width), lambda i, k, linked: (k, 1)),
        ],
        out_specs=pl.BlockSpec((brick_rows, width), lambda i, k, linked: (i, 0)),
        scratch_shapes=[
            pltpu.VMEM((head_count, brick_rows, 1), jnp.float32),
            pltpu.VMEM((head_count, brick_rows, 1), jnp.float32),
            pltpu.VMEM((head_count, brick_rows, HEAD_DIM), jnp.float32),
        ],
    )
    return pl.pallas_call(
        body,
        grid_spec=grid_spec,
        out_shape=jax.ShapeDtypeStruct((row_count, width), jnp.bfloat16),
        compiler_params=pltpu.CompilerParams(dimension_semantics=("arbitrary", "arbitrary")),
    )(linked_rows, queries, pair_piece, pair_piece)


def shards(
    voxel_feats,
    face_open,
    pattern,
    conv_weight,
    conv_bias,
    gain_one,
    query_weight,
    key_weight,
    value_weight,
    out_weight,
    gain_two,
    up_weight,
    down_weight,
):
    row_count = voxel_feats.shape[0]
    local_width = voxel_feats.shape[1]
    face_rows = EDGE * EDGE
    brick_rows = EDGE * face_rows
    local_bricks = row_count // brick_rows
    brick_total = pattern.shape[0]
    first_brick = lax.axis_index("bricks") * local_bricks
    extended = extended_2(voxel_feats, (("bricks", 0),), face_rows)
    brick_vals = extended[face_rows : face_rows + row_count].astype(jnp.float32)
    brick_vals = brick_vals.reshape(local_bricks, EDGE, face_rows, local_width)
    lower_face = jnp.concatenate(
        [extended[:face_rows].astype(jnp.float32)[None], brick_vals[:-1, EDGE - 1]], axis=0
    )
    upper_face = jnp.concatenate(
        [brick_vals[1:, 0], extended[face_rows + row_count :].astype(jnp.float32)[None]], axis=0
    )
    brick_ids = first_brick + jnp.arange(local_bricks, dtype=jnp.int32)
    lower_open = jnp.where(brick_ids >= 1, jnp.take(face_open, brick_ids), 0)
    upper_open = jnp.where(
        brick_ids + 1 < brick_total,
        jnp.take(face_open, jnp.minimum(brick_ids + 1, brick_total - 1)),
        0,
    )
    lower_face = lower_face * lower_open.astype(jnp.float32)[:, None, None]
    upper_face = upper_face * upper_open.astype(jnp.float32)[:, None, None]
    conv_out = depthwise(brick_vals, lower_face, upper_face, conv_weight, conv_bias)
    stream = (voxel_feats.astype(jnp.float32) + conv_out).astype(jnp.bfloat16)
    stream_full = lax.all_gather(stream, "heads", axis=1, tiled=True)
    normed = layer_norm(stream_full, gain_one).astype(jnp.bfloat16)
    queries = jnp.dot(normed, query_weight, preferred_element_type=jnp.float32).astype(jnp.bfloat16)
    head_count = local_width // HEAD_DIM
    keys_all = jnp.dot(normed, key_weight, preferred_element_type=jnp.float32).astype(jnp.bfloat16)
    values_all = jnp.dot(normed, value_weight, preferred_element_type=jnp.float32).astype(
        jnp.bfloat16
    )
    pair_local = jnp.concatenate([keys_all, values_all], axis=1)
    pair_piece = lax.all_gather(pair_local, "bricks", axis=0, tiled=True)
    key_count = pair_piece.shape[0] // brick_rows
    linked_rows = lax.dynamic_slice_in_dim(pattern, first_brick, local_bricks, 0).reshape(-1)
    attended = brick_attention(linked_rows, queries, pair_piece, head_count, key_count, brick_rows)
    attended = attended.reshape(row_count, local_width)
    partial_out = jnp.dot(attended, out_weight, preferred_element_type=jnp.float32)
    full_sum = lax.psum(partial_out.astype(jnp.bfloat16), "heads").astype(jnp.float32)
    stream_two_full = (stream_full.astype(jnp.float32) + full_sum).astype(jnp.bfloat16)
    stream_two = lax.dynamic_slice_in_dim(
        stream_two_full, lax.axis_index("heads") * local_width, local_width, 1
    )
    normed_two = layer_norm(stream_two_full, gain_two).astype(jnp.bfloat16)
    hidden = jax.nn.gelu(
        jnp.dot(normed_two, up_weight, preferred_element_type=jnp.float32), approximate=True
    ).astype(jnp.bfloat16)
    lowered = jnp.dot(hidden, down_weight, preferred_element_type=jnp.float32)
    mixed = lax.psum_scatter(
        lowered.astype(jnp.bfloat16), "heads", scatter_dimension=1, tiled=True
    ).astype(jnp.float32)
    return (stream_two.astype(jnp.float32) + mixed).astype(jnp.bfloat16)


def solution(mesh):
    return jax.shard_map(
        shards,
        mesh=mesh,
        in_specs=(
            P(("groups", "bricks"), "heads"),
            P("groups"),
            P("groups", None),
            P(None, "heads"),
            P("heads"),
            P(),
            P(None, "heads"),
            P(None, "heads"),
            P(None, "heads"),
            P("heads", None),
            P(),
            P(None, "heads"),
            P("heads", None),
        ),
        out_specs=P(("groups", "bricks"), "heads"),
        check_vma=False,
    )
```

```python
import jax
import jax.numpy as jnp
from jax import lax
from jax.sharding import PartitionSpec as P

EDGE = 8
HEAD_DIM = 64


epsilon = 1e-05


def extended_2(value, sides, width):
    for axis, dim in sides:
        size, length = (lax.axis_size(axis), value.shape[dim])
        up = [(i, (i + 1) % size) for i in range(size - 1)]
        down = [(j, i) for i, j in up]
        last = lax.slice_in_dim(value, length - width, length, axis=dim)
        first = lax.slice_in_dim(value, 0, width, axis=dim)
        before = lax.ppermute(last, axis, up)
        after = lax.ppermute(first, axis, down)
        value = jnp.concatenate([before, value, after], axis=dim)
    return value


def layer_norm(inputs, gain_vec):
    values = inputs.astype(jnp.float32)
    center = values - jnp.mean(values, axis=-1, keepdims=True)
    spread = jnp.mean(center * center, axis=-1, keepdims=True)
    return center * lax.rsqrt(spread + epsilon) * gain_vec.astype(jnp.float32)


def depthwise(brick_vals, lower_face, upper_face, conv_weight, conv_bias):
    brick_count = brick_vals.shape[0]
    edge_len = brick_vals.shape[1]
    channels = brick_vals.shape[3]
    layers = jnp.concatenate([lower_face[:, None], brick_vals, upper_face[:, None]], axis=1)
    layers = layers.reshape(brick_count, edge_len + 2, edge_len, edge_len, channels)
    padded = jnp.pad(layers, ((0, 0), (0, 0), (1, 1), (1, 1), (0, 0)))
    weights = conv_weight.astype(jnp.float32)
    summed = jnp.zeros((brick_count, edge_len, edge_len, edge_len, channels), jnp.float32)
    for step_x in range(3):
        for step_y in range(3):
            for step_z in range(3):
                window = padded[
                    :,
                    step_x : step_x + edge_len,
                    step_y : step_y + edge_len,
                    step_z : step_z + edge_len,
                ]
                summed = summed + weights[step_x * 9 + step_y * 3 + step_z] * window
    return summed.reshape(brick_count * edge_len**3, channels) + conv_bias.astype(jnp.float32)


def level_count(total):
    levels = total.bit_length() - 1
    assert 1 << levels == total
    return levels


def scatter_heads(partial, head_id, head_total):
    levels = level_count(head_total)
    rows = partial.shape[0]
    width = partial.shape[1] // head_total
    current = partial.reshape((rows,) + (2,) * levels + (width,))
    for level in range(levels):
        bit = 1 << level
        axis = levels - level
        mine = (head_id >> level) & 1
        keep = lax.dynamic_index_in_dim(current, mine, axis, keepdims=False)
        give = lax.dynamic_index_in_dim(current, 1 - mine, axis, keepdims=False)
        got = lax.ppermute(
            give.astype(jnp.bfloat16), "heads", [(i, i ^ bit) for i in range(head_total)]
        )
        current = keep + got.astype(jnp.float32)
    return current.reshape(rows, width)


def gather_heads(piece, head_id, head_total):
    levels = level_count(head_total)
    rows, width = piece.shape
    current = piece
    for level in reversed(range(levels)):
        bit = 1 << level
        mine = (head_id >> level) & 1
        got = lax.ppermute(current, "heads", [(i, i ^ bit) for i in range(head_total)])
        low = jnp.where(mine == 0, current, got)
        high = jnp.where(mine == 0, got, current)
        current = jnp.stack([low, high], axis=current.ndim - 1)
    return current.reshape(rows, head_total * width)


def absorb_block(state, query_heads, block, linked, head_count, brick_rows, local_width):
    row_max, row_mass, weighted = state
    key_rows = block[:, :local_width].reshape(-1, head_count, HEAD_DIM)
    value_rows = block[:, local_width:].reshape(-1, head_count, HEAD_DIM)
    scores = (
        jnp.einsum("bqhd,khd->bhqk", query_heads, key_rows, preferred_element_type=jnp.float32)
        * HEAD_DIM ** (-0.5)
    )
    keep = jnp.repeat(linked, brick_rows, axis=1, total_repeat_length=key_rows.shape[0])
    scores = jnp.where(keep[:, None, None, :], scores, -1e30)
    max_new = jnp.maximum(row_max, jnp.max(scores, axis=-1))
    factor = jnp.exp(row_max - max_new)
    weights = jnp.exp(scores - max_new[..., None])
    mass_new = row_mass * factor + jnp.sum(weights, axis=-1)
    sum_new = weighted * jnp.transpose(factor, (0, 2, 1))[..., None] + jnp.einsum(
        "bhqk,khd->bqhd", weights.astype(jnp.bfloat16), value_rows,
        preferred_element_type=jnp.float32,
    )
    return max_new, mass_new, sum_new


def shards(
    voxel_feats,
    face_open,
    pattern,
    conv_weight,
    conv_bias,
    gain_one,
    query_weight,
    key_weight,
    value_weight,
    out_weight,
    gain_two,
    up_weight,
    down_weight,
):
    row_count = voxel_feats.shape[0]
    local_width = voxel_feats.shape[1]
    face_rows = EDGE * EDGE
    brick_rows = EDGE * face_rows
    local_bricks = row_count // brick_rows
    brick_total = pattern.shape[0]
    first_brick = lax.axis_index("bricks") * local_bricks
    extended = extended_2(voxel_feats, (("bricks", 0),), face_rows)
    brick_vals = extended[face_rows : face_rows + row_count].astype(jnp.float32)
    brick_vals = brick_vals.reshape(local_bricks, EDGE, face_rows, local_width)
    lower_face = jnp.concatenate(
        [extended[:face_rows].astype(jnp.float32)[None], brick_vals[:-1, EDGE - 1]], axis=0
    )
    upper_face = jnp.concatenate(
        [brick_vals[1:, 0], extended[face_rows + row_count :].astype(jnp.float32)[None]], axis=0
    )
    brick_ids = first_brick + jnp.arange(local_bricks, dtype=jnp.int32)
    lower_open = jnp.where(brick_ids >= 1, jnp.take(face_open, brick_ids), 0)
    upper_open = jnp.where(
        brick_ids + 1 < brick_total,
        jnp.take(face_open, jnp.minimum(brick_ids + 1, brick_total - 1)),
        0,
    )
    lower_face = lower_face * lower_open.astype(jnp.float32)[:, None, None]
    upper_face = upper_face * upper_open.astype(jnp.float32)[:, None, None]
    conv_out = depthwise(brick_vals, lower_face, upper_face, conv_weight, conv_bias)
    stream = (voxel_feats.astype(jnp.float32) + conv_out).astype(jnp.bfloat16)
    head_total = lax.axis_size("heads")
    head_id = lax.axis_index("heads")
    stream_full = gather_heads(stream, head_id, head_total)
    normed = layer_norm(stream_full, gain_one).astype(jnp.bfloat16)
    queries = jnp.dot(normed, query_weight, preferred_element_type=jnp.float32).astype(jnp.bfloat16)
    head_count = local_width // HEAD_DIM
    keys_all = jnp.dot(normed, key_weight, preferred_element_type=jnp.float32).astype(jnp.bfloat16)
    values_all = jnp.dot(normed, value_weight, preferred_element_type=jnp.float32).astype(
        jnp.bfloat16
    )
    pair_local = jnp.concatenate([keys_all, values_all], axis=1)
    brick_dev = lax.axis_index("bricks")
    dev_total = lax.axis_size("bricks")
    key_total = pattern.shape[1]
    query_heads = queries.reshape(local_bricks, brick_rows, head_count, HEAD_DIM)
    linked_rows = lax.dynamic_slice_in_dim(pattern, first_brick, local_bricks, 0)
    state = (
        jnp.full((local_bricks, head_count, brick_rows), -1e30, jnp.float32),
        jnp.zeros((local_bricks, head_count, brick_rows), jnp.float32),
        jnp.zeros((local_bricks, brick_rows, head_count, HEAD_DIM), jnp.float32),
    )
    ring = [(i, (i + 1) % dev_total) for i in range(dev_total)]
    block = pair_local
    for step in range(dev_total):
        if step > 0:
            block = lax.ppermute(block, "bricks", ring)
        source = (brick_dev - step) % dev_total
        key_ids = source * local_bricks + jnp.arange(local_bricks, dtype=jnp.int32)
        linked = jnp.take(linked_rows, key_ids, axis=1) > 0
        state = absorb_block(state, query_heads, block, linked, head_count, brick_rows, local_width)
    row_max, row_mass, weighted = state
    attended = (weighted / jnp.transpose(row_mass, (0, 2, 1))[:, :, :, None]).astype(jnp.bfloat16)
    attended = attended.reshape(row_count, local_width)
    partial_out = jnp.dot(attended, out_weight, preferred_element_type=jnp.float32)
    out_sum = scatter_heads(partial_out, head_id, head_total)
    stream_two = (stream.astype(jnp.float32) + out_sum).astype(jnp.bfloat16)
    stream_two_full = gather_heads(stream_two, head_id, head_total)
    normed_two = layer_norm(stream_two_full, gain_two).astype(jnp.bfloat16)
    hidden = jax.nn.gelu(
        jnp.dot(normed_two, up_weight, preferred_element_type=jnp.float32), approximate=True
    ).astype(jnp.bfloat16)
    lowered = jnp.dot(hidden, down_weight, preferred_element_type=jnp.float32)
    mixed = scatter_heads(lowered, head_id, head_total)
    return (stream_two.astype(jnp.float32) + mixed).astype(jnp.bfloat16)


def solution(mesh):
    return jax.shard_map(
        shards,
        mesh=mesh,
        in_specs=(
            P(("groups", "bricks"), "heads"),
            P("groups"),
            P("groups", None),
            P(None, "heads"),
            P("heads"),
            P(),
            P(None, "heads"),
            P(None, "heads"),
            P(None, "heads"),
            P("heads", None),
            P(),
            P(None, "heads"),
            P("heads", None),
        ),
        out_specs=P(("groups", "bricks"), "heads"),
        check_vma=False,
    )
```

```python
import jax
import jax.numpy as jnp
from jax import lax
from jax.sharding import PartitionSpec as P

EDGE = 8
HEAD_DIM = 64


epsilon = 1e-05


def extended_2(value, sides, width):
    for axis, dim in sides:
        size, length = (lax.axis_size(axis), value.shape[dim])
        up = [(i, (i + 1) % size) for i in range(size - 1)]
        down = [(j, i) for i, j in up]
        last = lax.slice_in_dim(value, length - width, length, axis=dim)
        first = lax.slice_in_dim(value, 0, width, axis=dim)
        before = lax.ppermute(last, axis, up)
        after = lax.ppermute(first, axis, down)
        value = jnp.concatenate([before, value, after], axis=dim)
    return value


def layer_norm(inputs, gain_vec):
    values = inputs.astype(jnp.float32)
    center = values - jnp.mean(values, axis=-1, keepdims=True)
    spread = jnp.mean(center * center, axis=-1, keepdims=True)
    return center * lax.rsqrt(spread + epsilon) * gain_vec.astype(jnp.float32)


def depthwise(brick_vals, lower_face, upper_face, conv_weight, conv_bias):
    brick_count = brick_vals.shape[0]
    edge_len = brick_vals.shape[1]
    channels = brick_vals.shape[3]
    layers = jnp.concatenate([lower_face[:, None], brick_vals, upper_face[:, None]], axis=1)
    layers = layers.reshape(brick_count, edge_len + 2, edge_len, edge_len, channels)
    padded = jnp.pad(layers, ((0, 0), (0, 0), (1, 1), (1, 1), (0, 0)))
    weights = conv_weight.astype(jnp.float32)
    summed = jnp.zeros((brick_count, edge_len, edge_len, edge_len, channels), jnp.float32)
    for step_x in range(3):
        for step_y in range(3):
            for step_z in range(3):
                window = padded[
                    :,
                    step_x : step_x + edge_len,
                    step_y : step_y + edge_len,
                    step_z : step_z + edge_len,
                ]
                summed = summed + weights[step_x * 9 + step_y * 3 + step_z] * window
    return summed.reshape(brick_count * edge_len**3, channels) + conv_bias.astype(jnp.float32)


def level_count(total):
    levels = total.bit_length() - 1
    assert 1 << levels == total
    return levels


def scatter_heads(partial, head_id, head_total):
    levels = level_count(head_total)
    rows = partial.shape[0]
    width = partial.shape[1] // head_total
    current = partial.reshape((rows,) + (2,) * levels + (width,))
    for level in range(levels):
        bit = 1 << level
        axis = levels - level
        mine = (head_id >> level) & 1
        keep = lax.dynamic_index_in_dim(current, mine, axis, keepdims=False)
        give = lax.dynamic_index_in_dim(current, 1 - mine, axis, keepdims=False)
        got = lax.ppermute(
            give.astype(jnp.bfloat16), "heads", [(i, i ^ bit) for i in range(head_total)]
        )
        current = keep + got.astype(jnp.float32)
    return current.reshape(rows, width)


def gather_heads(piece, head_id, head_total):
    levels = level_count(head_total)
    rows, width = piece.shape
    current = piece
    for level in reversed(range(levels)):
        bit = 1 << level
        mine = (head_id >> level) & 1
        got = lax.ppermute(current, "heads", [(i, i ^ bit) for i in range(head_total)])
        low = jnp.where(mine == 0, current, got)
        high = jnp.where(mine == 0, got, current)
        current = jnp.stack([low, high], axis=current.ndim - 1)
    return current.reshape(rows, head_total * width)


def absorb_block(state, query_heads, block, linked, head_count, brick_rows, local_width):
    row_max, row_mass, weighted = state
    key_rows = block[:, :local_width].reshape(-1, head_count, HEAD_DIM)
    value_rows = block[:, local_width:].reshape(-1, head_count, HEAD_DIM)
    scores = (
        jnp.einsum("bqhd,khd->bhqk", query_heads, key_rows, preferred_element_type=jnp.float32)
        * HEAD_DIM ** (-0.5)
    )
    keep = jnp.repeat(linked, brick_rows, axis=1, total_repeat_length=key_rows.shape[0])
    scores = jnp.where(keep[:, None, None, :], scores, -1e30)
    max_new = jnp.maximum(row_max, jnp.max(scores, axis=-1))
    factor = jnp.exp(row_max - max_new)
    weights = jnp.exp(scores - max_new[..., None])
    mass_new = row_mass * factor + jnp.sum(weights, axis=-1)
    sum_new = weighted * jnp.transpose(factor, (0, 2, 1))[..., None] + jnp.einsum(
        "bhqk,khd->bqhd", weights.astype(jnp.bfloat16), value_rows,
        preferred_element_type=jnp.float32,
    )
    return max_new, mass_new, sum_new


def shards(
    voxel_feats,
    face_open,
    pattern,
    conv_weight,
    conv_bias,
    gain_one,
    query_weight,
    key_weight,
    value_weight,
    out_weight,
    gain_two,
    up_weight,
    down_weight,
):
    row_count = voxel_feats.shape[0]
    local_width = voxel_feats.shape[1]
    face_rows = EDGE * EDGE
    brick_rows = EDGE * face_rows
    local_bricks = row_count // brick_rows
    brick_total = pattern.shape[0]
    first_brick = lax.axis_index("bricks") * local_bricks
    extended = extended_2(voxel_feats, (("bricks", 0),), face_rows)
    brick_vals = extended[face_rows : face_rows + row_count].astype(jnp.float32)
    brick_vals = brick_vals.reshape(local_bricks, EDGE, face_rows, local_width)
    lower_face = jnp.concatenate(
        [extended[:face_rows].astype(jnp.float32)[None], brick_vals[:-1, EDGE - 1]], axis=0
    )
    upper_face = jnp.concatenate(
        [brick_vals[1:, 0], extended[face_rows + row_count :].astype(jnp.float32)[None]], axis=0
    )
    brick_ids = first_brick + jnp.arange(local_bricks, dtype=jnp.int32)
    lower_open = jnp.where(brick_ids >= 1, jnp.take(face_open, brick_ids), 0)
    upper_open = jnp.where(
        brick_ids + 1 < brick_total,
        jnp.take(face_open, jnp.minimum(brick_ids + 1, brick_total - 1)),
        0,
    )
    lower_face = lower_face * lower_open.astype(jnp.float32)[:, None, None]
    upper_face = upper_face * upper_open.astype(jnp.float32)[:, None, None]
    conv_out = depthwise(brick_vals, lower_face, upper_face, conv_weight, conv_bias)
    stream = (voxel_feats.astype(jnp.float32) + conv_out).astype(jnp.bfloat16)
    head_total = lax.axis_size("heads")
    head_id = lax.axis_index("heads")
    stream_full = gather_heads(stream, head_id, head_total)
    normed = layer_norm(stream_full, gain_one).astype(jnp.bfloat16)
    queries = jnp.dot(normed, query_weight, preferred_element_type=jnp.float32).astype(jnp.bfloat16)
    head_count = local_width // HEAD_DIM
    keys_all = jnp.dot(normed, key_weight, preferred_element_type=jnp.float32).astype(jnp.bfloat16)
    values_all = jnp.dot(normed, value_weight, preferred_element_type=jnp.float32).astype(
        jnp.bfloat16
    )
    pair_local = jnp.concatenate([keys_all, values_all], axis=1)
    brick_dev = lax.axis_index("bricks")
    dev_total = lax.axis_size("bricks")
    key_total = pattern.shape[1]
    query_heads = queries.reshape(local_bricks, brick_rows, head_count, HEAD_DIM)
    linked_rows = lax.dynamic_slice_in_dim(pattern, first_brick, local_bricks, 0)
    state = (
        jnp.full((local_bricks, head_count, brick_rows), -1e30, jnp.float32),
        jnp.zeros((local_bricks, head_count, brick_rows), jnp.float32),
        jnp.zeros((local_bricks, brick_rows, head_count, HEAD_DIM), jnp.float32),
    )
    ring = [(i, (i + 1) % dev_total) for i in range(dev_total)]
    block = pair_local
    for step in range(dev_total):
        if step + 1 < dev_total:
            arriving = lax.ppermute(block, "bricks", ring)
        source = (brick_dev - step) % dev_total
        key_ids = source * local_bricks + jnp.arange(local_bricks, dtype=jnp.int32)
        linked = jnp.take(linked_rows, key_ids, axis=1) > 0
        state = absorb_block(state, query_heads, block, linked, head_count, brick_rows, local_width)
        if step + 1 < dev_total:
            state, block = lax.optimization_barrier((state, arriving))
    row_max, row_mass, weighted = state
    attended = (weighted / jnp.transpose(row_mass, (0, 2, 1))[:, :, :, None]).astype(jnp.bfloat16)
    attended = attended.reshape(row_count, local_width)
    partial_out = jnp.dot(attended, out_weight, preferred_element_type=jnp.float32)
    out_sum = scatter_heads(partial_out, head_id, head_total)
    stream_two = (stream.astype(jnp.float32) + out_sum).astype(jnp.bfloat16)
    stream_two_full = gather_heads(stream_two, head_id, head_total)
    normed_two = layer_norm(stream_two_full, gain_two).astype(jnp.bfloat16)
    hidden = jax.nn.gelu(
        jnp.dot(normed_two, up_weight, preferred_element_type=jnp.float32), approximate=True
    ).astype(jnp.bfloat16)
    lowered = jnp.dot(hidden, down_weight, preferred_element_type=jnp.float32)
    mixed = scatter_heads(lowered, head_id, head_total)
    return (stream_two.astype(jnp.float32) + mixed).astype(jnp.bfloat16)


def solution(mesh):
    return jax.shard_map(
        shards,
        mesh=mesh,
        in_specs=(
            P(("groups", "bricks"), "heads"),
            P("groups"),
            P("groups", None),
            P(None, "heads"),
            P("heads"),
            P(),
            P(None, "heads"),
            P(None, "heads"),
            P(None, "heads"),
            P("heads", None),
            P(),
            P(None, "heads"),
            P("heads", None),
        ),
        out_specs=P(("groups", "bricks"), "heads"),
        check_vma=False,
    )
```

```python
import jax
import jax.numpy as jnp
from jax import lax
from jax.sharding import PartitionSpec as P

EDGE = 8
HEAD_DIM = 64


epsilon = 1e-05


def extended_2(value, sides, width):
    for axis, dim in sides:
        size, length = (lax.axis_size(axis), value.shape[dim])
        up = [(i, (i + 1) % size) for i in range(size - 1)]
        down = [(j, i) for i, j in up]
        last = lax.slice_in_dim(value, length - width, length, axis=dim)
        first = lax.slice_in_dim(value, 0, width, axis=dim)
        before = lax.ppermute(last, axis, up)
        after = lax.ppermute(first, axis, down)
        value = jnp.concatenate([before, value, after], axis=dim)
    return value


def layer_norm(inputs, gain_vec):
    values = inputs.astype(jnp.float32)
    center = values - jnp.mean(values, axis=-1, keepdims=True)
    spread = jnp.mean(center * center, axis=-1, keepdims=True)
    return center * lax.rsqrt(spread + epsilon) * gain_vec.astype(jnp.float32)


def depthwise(brick_vals, lower_face, upper_face, conv_weight, conv_bias):
    brick_count = brick_vals.shape[0]
    edge_len = brick_vals.shape[1]
    channels = brick_vals.shape[3]
    layers = jnp.concatenate([lower_face[:, None], brick_vals, upper_face[:, None]], axis=1)
    layers = layers.reshape(brick_count, edge_len + 2, edge_len, edge_len, channels)
    padded = jnp.pad(layers, ((0, 0), (0, 0), (1, 1), (1, 1), (0, 0)))
    weights = conv_weight.astype(jnp.float32)
    summed = jnp.zeros((brick_count, edge_len, edge_len, edge_len, channels), jnp.float32)
    for step_x in range(3):
        for step_y in range(3):
            for step_z in range(3):
                window = padded[
                    :,
                    step_x : step_x + edge_len,
                    step_y : step_y + edge_len,
                    step_z : step_z + edge_len,
                ]
                summed = summed + weights[step_x * 9 + step_y * 3 + step_z] * window
    return summed.reshape(brick_count * edge_len**3, channels) + conv_bias.astype(jnp.float32)


def level_count(total):
    levels = total.bit_length() - 1
    assert 1 << levels == total
    return levels


def scatter_heads(partial, head_id, head_total):
    levels = level_count(head_total)
    rows = partial.shape[0]
    width = partial.shape[1] // head_total
    current = partial.reshape((rows,) + (2,) * levels + (width,))
    for level in range(levels):
        bit = 1 << level
        axis = levels - level
        mine = (head_id >> level) & 1
        keep = lax.dynamic_index_in_dim(current, mine, axis, keepdims=False)
        give = lax.dynamic_index_in_dim(current, 1 - mine, axis, keepdims=False)
        got = lax.ppermute(
            give.astype(jnp.bfloat16), "heads", [(i, i ^ bit) for i in range(head_total)]
        )
        current = keep + got.astype(jnp.float32)
    return current.reshape(rows, width)


def gather_heads(piece, head_id, head_total):
    levels = level_count(head_total)
    rows, width = piece.shape
    current = piece
    for level in reversed(range(levels)):
        bit = 1 << level
        mine = (head_id >> level) & 1
        got = lax.ppermute(current, "heads", [(i, i ^ bit) for i in range(head_total)])
        low = jnp.where(mine == 0, current, got)
        high = jnp.where(mine == 0, got, current)
        current = jnp.stack([low, high], axis=current.ndim - 1)
    return current.reshape(rows, head_total * width)


def absorb_block(state, query_heads, block, linked, head_count, brick_rows, local_width):
    row_max, row_mass, weighted = state
    key_rows = block[:, :local_width].reshape(-1, head_count, HEAD_DIM)
    value_rows = block[:, local_width:].reshape(-1, head_count, HEAD_DIM)
    scores = (
        jnp.einsum("bqhd,khd->bhqk", query_heads, key_rows, preferred_element_type=jnp.float32)
        * HEAD_DIM ** (-0.5)
    )
    keep = jnp.repeat(linked, brick_rows, axis=1, total_repeat_length=key_rows.shape[0])
    scores = jnp.where(keep[:, None, None, :], scores, -1e30)
    max_new = jnp.maximum(row_max, jnp.max(scores, axis=-1))
    factor = jnp.exp(row_max - max_new)
    weights = jnp.exp(scores - max_new[..., None])
    mass_new = row_mass * factor + jnp.sum(weights, axis=-1)
    sum_new = weighted * jnp.transpose(factor, (0, 2, 1))[..., None] + jnp.einsum(
        "bhqk,khd->bqhd", weights.astype(jnp.bfloat16), value_rows,
        preferred_element_type=jnp.float32,
    )
    return max_new, mass_new, sum_new


def shards(
    voxel_feats,
    face_open,
    pattern,
    conv_weight,
    conv_bias,
    gain_one,
    query_weight,
    key_weight,
    value_weight,
    out_weight,
    gain_two,
    up_weight,
    down_weight,
):
    row_count = voxel_feats.shape[0]
    local_width = voxel_feats.shape[1]
    face_rows = EDGE * EDGE
    brick_rows = EDGE * face_rows
    local_bricks = row_count // brick_rows
    brick_total = pattern.shape[0]
    first_brick = lax.axis_index("bricks") * local_bricks
    extended = extended_2(voxel_feats, (("bricks", 0),), face_rows)
    brick_vals = extended[face_rows : face_rows + row_count].astype(jnp.float32)
    brick_vals = brick_vals.reshape(local_bricks, EDGE, face_rows, local_width)
    lower_face = jnp.concatenate(
        [extended[:face_rows].astype(jnp.float32)[None], brick_vals[:-1, EDGE - 1]], axis=0
    )
    upper_face = jnp.concatenate(
        [brick_vals[1:, 0], extended[face_rows + row_count :].astype(jnp.float32)[None]], axis=0
    )
    brick_ids = first_brick + jnp.arange(local_bricks, dtype=jnp.int32)
    lower_open = jnp.where(brick_ids >= 1, jnp.take(face_open, brick_ids), 0)
    upper_open = jnp.where(
        brick_ids + 1 < brick_total,
        jnp.take(face_open, jnp.minimum(brick_ids + 1, brick_total - 1)),
        0,
    )
    lower_face = lower_face * lower_open.astype(jnp.float32)[:, None, None]
    upper_face = upper_face * upper_open.astype(jnp.float32)[:, None, None]
    conv_out = depthwise(brick_vals, lower_face, upper_face, conv_weight, conv_bias)
    stream = (voxel_feats.astype(jnp.float32) + conv_out).astype(jnp.bfloat16)
    head_total = lax.axis_size("heads")
    head_id = lax.axis_index("heads")
    stream_full = gather_heads(stream, head_id, head_total)
    normed = layer_norm(stream_full, gain_one).astype(jnp.bfloat16)
    queries = jnp.dot(normed, query_weight, preferred_element_type=jnp.float32).astype(jnp.bfloat16)
    head_count = local_width // HEAD_DIM
    keys_all = jnp.dot(normed, key_weight, preferred_element_type=jnp.float32).astype(jnp.bfloat16)
    values_all = jnp.dot(normed, value_weight, preferred_element_type=jnp.float32).astype(
        jnp.bfloat16
    )
    pair_local = jnp.concatenate([keys_all, values_all], axis=1)
    brick_dev = lax.axis_index("bricks")
    dev_total = lax.axis_size("bricks")
    key_total = pattern.shape[1]
    query_heads = queries.reshape(local_bricks, brick_rows, head_count, HEAD_DIM)
    linked_rows = lax.dynamic_slice_in_dim(pattern, first_brick, local_bricks, 0)
    state = (
        jnp.full((local_bricks, head_count, brick_rows), -1e30, jnp.float32),
        jnp.zeros((local_bricks, head_count, brick_rows), jnp.float32),
        jnp.zeros((local_bricks, brick_rows, head_count, HEAD_DIM), jnp.float32),
    )
    def take_block(state_now, block, source, valid):
        key_ids = jnp.clip(source, 0, dev_total - 1) * local_bricks + jnp.arange(
            local_bricks, dtype=jnp.int32
        )
        linked = (jnp.take(linked_rows, key_ids, axis=1) > 0) & valid
        return absorb_block(
            state_now, query_heads, block, linked, head_count, brick_rows, local_width
        )

    upward, downward = pair_local, pair_local
    pending = [(pair_local, brick_dev, jnp.bool_(True))]
    for step in range(1, dev_total):
        up_pairs = [(i, i + 1) for i in range(step - 1, dev_total - 1)]
        down_pairs = [(i, i - 1) for i in range(1, dev_total - step + 1)]
        upward_next = lax.ppermute(upward, "bricks", up_pairs)
        downward_next = lax.ppermute(downward, "bricks", down_pairs)
        for block, source, valid in pending:
            state = take_block(state, block, source, valid)
        state, upward, downward = lax.optimization_barrier((state, upward_next, downward_next))
        from_below = brick_dev >= step
        from_above = brick_dev + step <= dev_total - 1
        if 2 * step > dev_total - 1:
            pending = [(
                jnp.where(from_below, upward, downward),
                jnp.where(from_below, brick_dev - step, brick_dev + step),
                from_below | from_above,
            )]
        else:
            pending = [
                (upward, brick_dev - step, from_below),
                (downward, brick_dev + step, from_above),
            ]
    for block, source, valid in pending:
        state = take_block(state, block, source, valid)
    row_max, row_mass, weighted = state
    attended = (weighted / jnp.transpose(row_mass, (0, 2, 1))[:, :, :, None]).astype(jnp.bfloat16)
    attended = attended.reshape(row_count, local_width)
    partial_out = jnp.dot(attended, out_weight, preferred_element_type=jnp.float32)
    out_sum = scatter_heads(partial_out, head_id, head_total)
    stream_two = (stream.astype(jnp.float32) + out_sum).astype(jnp.bfloat16)
    stream_two_full = gather_heads(stream_two, head_id, head_total)
    normed_two = layer_norm(stream_two_full, gain_two).astype(jnp.bfloat16)
    hidden = jax.nn.gelu(
        jnp.dot(normed_two, up_weight, preferred_element_type=jnp.float32), approximate=True
    ).astype(jnp.bfloat16)
    lowered = jnp.dot(hidden, down_weight, preferred_element_type=jnp.float32)
    mixed = scatter_heads(lowered, head_id, head_total)
    return (stream_two.astype(jnp.float32) + mixed).astype(jnp.bfloat16)


def solution(mesh):
    return jax.shard_map(
        shards,
        mesh=mesh,
        in_specs=(
            P(("groups", "bricks"), "heads"),
            P("groups"),
            P("groups", None),
            P(None, "heads"),
            P("heads"),
            P(),
            P(None, "heads"),
            P(None, "heads"),
            P(None, "heads"),
            P("heads", None),
            P(),
            P(None, "heads"),
            P("heads", None),
        ),
        out_specs=P(("groups", "bricks"), "heads"),
        check_vma=False,
    )
```

```python
import jax
import jax.numpy as jnp
from jax import lax
from jax.sharding import PartitionSpec as P

EDGE = 8
HEAD_DIM = 64


epsilon = 1e-05


def extended_2(value, sides, width):
    for axis, dim in sides:
        size, length = (lax.axis_size(axis), value.shape[dim])
        up = [(i, (i + 1) % size) for i in range(size - 1)]
        down = [(j, i) for i, j in up]
        last = lax.slice_in_dim(value, length - width, length, axis=dim)
        first = lax.slice_in_dim(value, 0, width, axis=dim)
        before = lax.ppermute(last, axis, up)
        after = lax.ppermute(first, axis, down)
        value = jnp.concatenate([before, value, after], axis=dim)
    return value


def layer_norm(inputs, gain_vec):
    values = inputs.astype(jnp.float32)
    center = values - jnp.mean(values, axis=-1, keepdims=True)
    spread = jnp.mean(center * center, axis=-1, keepdims=True)
    return center * lax.rsqrt(spread + epsilon) * gain_vec.astype(jnp.float32)


def depthwise(brick_vals, lower_face, upper_face, conv_weight, conv_bias):
    brick_count = brick_vals.shape[0]
    edge_len = brick_vals.shape[1]
    channels = brick_vals.shape[3]
    layers = jnp.concatenate([lower_face[:, None], brick_vals, upper_face[:, None]], axis=1)
    layers = layers.reshape(brick_count, edge_len + 2, edge_len, edge_len, channels)
    padded = jnp.pad(layers, ((0, 0), (0, 0), (1, 1), (1, 1), (0, 0)))
    weights = conv_weight.astype(jnp.float32)
    summed = jnp.zeros((brick_count, edge_len, edge_len, edge_len, channels), jnp.float32)
    for step_x in range(3):
        for step_y in range(3):
            for step_z in range(3):
                window = padded[
                    :,
                    step_x : step_x + edge_len,
                    step_y : step_y + edge_len,
                    step_z : step_z + edge_len,
                ]
                summed = summed + weights[step_x * 9 + step_y * 3 + step_z] * window
    return summed.reshape(brick_count * edge_len**3, channels) + conv_bias.astype(jnp.float32)


def level_count(total):
    levels = total.bit_length() - 1
    assert 1 << levels == total
    return levels


def scatter_heads(partial, head_id, head_total):
    levels = level_count(head_total)
    rows = partial.shape[0]
    width = partial.shape[1] // head_total
    current = partial.reshape((rows,) + (2,) * levels + (width,))
    for level in range(levels):
        bit = 1 << level
        axis = levels - level
        mine = (head_id >> level) & 1
        keep = lax.dynamic_index_in_dim(current, mine, axis, keepdims=False)
        give = lax.dynamic_index_in_dim(current, 1 - mine, axis, keepdims=False)
        got = lax.ppermute(
            give.astype(jnp.bfloat16), "heads", [(i, i ^ bit) for i in range(head_total)]
        )
        current = keep + got.astype(jnp.float32)
    return current.reshape(rows, width)


def gather_heads(piece, head_id, head_total):
    levels = level_count(head_total)
    rows, width = piece.shape
    current = piece
    for level in reversed(range(levels)):
        bit = 1 << level
        mine = (head_id >> level) & 1
        got = lax.ppermute(current, "heads", [(i, i ^ bit) for i in range(head_total)])
        low = jnp.where(mine == 0, current, got)
        high = jnp.where(mine == 0, got, current)
        current = jnp.stack([low, high], axis=current.ndim - 1)
    return current.reshape(rows, head_total * width)


def absorb_block(state, query_heads, block, linked, head_count, brick_rows, local_width):
    row_max, row_mass, weighted = state
    key_rows = block[:, :local_width].reshape(-1, head_count, HEAD_DIM)
    value_rows = block[:, local_width:].reshape(-1, head_count, HEAD_DIM)
    scores = (
        jnp.einsum("bqhd,khd->bhqk", query_heads, key_rows, preferred_element_type=jnp.float32)
        * HEAD_DIM ** (-0.5)
    )
    keep = jnp.repeat(linked, brick_rows, axis=1, total_repeat_length=key_rows.shape[0])
    scores = jnp.where(keep[:, None, None, :], scores, -1e30)
    max_new = jnp.maximum(row_max, jnp.max(scores, axis=-1))
    factor = jnp.exp(row_max - max_new)
    weights = jnp.exp(scores - max_new[..., None])
    mass_new = row_mass * factor + jnp.sum(weights, axis=-1)
    sum_new = weighted * jnp.transpose(factor, (0, 2, 1))[..., None] + jnp.einsum(
        "bhqk,khd->bqhd", weights.astype(jnp.bfloat16), value_rows,
        preferred_element_type=jnp.float32,
    )
    return max_new, mass_new, sum_new


def shards(
    voxel_feats,
    face_open,
    pattern,
    conv_weight,
    conv_bias,
    gain_one,
    query_weight,
    key_weight,
    value_weight,
    out_weight,
    gain_two,
    up_weight,
    down_weight,
):
    row_count = voxel_feats.shape[0]
    local_width = voxel_feats.shape[1]
    face_rows = EDGE * EDGE
    brick_rows = EDGE * face_rows
    local_bricks = row_count // brick_rows
    brick_total = pattern.shape[0]
    first_brick = lax.axis_index("bricks") * local_bricks
    extended = extended_2(voxel_feats, (("bricks", 0),), face_rows)
    brick_vals = extended[face_rows : face_rows + row_count].astype(jnp.float32)
    brick_vals = brick_vals.reshape(local_bricks, EDGE, face_rows, local_width)
    lower_face = jnp.concatenate(
        [extended[:face_rows].astype(jnp.float32)[None], brick_vals[:-1, EDGE - 1]], axis=0
    )
    upper_face = jnp.concatenate(
        [brick_vals[1:, 0], extended[face_rows + row_count :].astype(jnp.float32)[None]], axis=0
    )
    brick_ids = first_brick + jnp.arange(local_bricks, dtype=jnp.int32)
    lower_open = jnp.where(brick_ids >= 1, jnp.take(face_open, brick_ids), 0)
    upper_open = jnp.where(
        brick_ids + 1 < brick_total,
        jnp.take(face_open, jnp.minimum(brick_ids + 1, brick_total - 1)),
        0,
    )
    lower_face = lower_face * lower_open.astype(jnp.float32)[:, None, None]
    upper_face = upper_face * upper_open.astype(jnp.float32)[:, None, None]
    conv_out = depthwise(brick_vals, lower_face, upper_face, conv_weight, conv_bias)
    stream = (voxel_feats.astype(jnp.float32) + conv_out).astype(jnp.bfloat16)
    head_total = lax.axis_size("heads")
    head_id = lax.axis_index("heads")
    stream_full = gather_heads(stream, head_id, head_total)
    normed = layer_norm(stream_full, gain_one).astype(jnp.bfloat16)
    queries = jnp.dot(normed, query_weight, preferred_element_type=jnp.float32).astype(jnp.bfloat16)
    head_count = local_width // HEAD_DIM
    keys_all = jnp.dot(normed, key_weight, preferred_element_type=jnp.float32).astype(jnp.bfloat16)
    values_all = jnp.dot(normed, value_weight, preferred_element_type=jnp.float32).astype(
        jnp.bfloat16
    )
    pair_local = jnp.concatenate([keys_all, values_all], axis=1)
    brick_dev = lax.axis_index("bricks")
    dev_total = lax.axis_size("bricks")
    key_total = pattern.shape[1]
    query_heads = queries.reshape(local_bricks, brick_rows, head_count, HEAD_DIM)
    linked_rows = lax.dynamic_slice_in_dim(pattern, first_brick, local_bricks, 0)
    state = (
        jnp.full((local_bricks, head_count, brick_rows), -1e30, jnp.float32),
        jnp.zeros((local_bricks, head_count, brick_rows), jnp.float32),
        jnp.zeros((local_bricks, brick_rows, head_count, HEAD_DIM), jnp.float32),
    )
    ring = [(i, (i + 1) % dev_total) for i in range(dev_total)]
    block = pair_local
    for step in range(dev_total):
        if step + 1 < dev_total:
            arriving = lax.ppermute(block, "bricks", ring)
        source = (brick_dev - step) % dev_total
        key_ids = source * local_bricks + jnp.arange(local_bricks, dtype=jnp.int32)
        linked = jnp.take(linked_rows, key_ids, axis=1) > 0
        state = absorb_block(state, query_heads, block, linked, head_count, brick_rows, local_width)
        if step + 1 < dev_total:
            state, block = lax.optimization_barrier((state, arriving))
    row_max, row_mass, weighted = state
    attended = (weighted / jnp.transpose(row_mass, (0, 2, 1))[:, :, :, None]).astype(jnp.bfloat16)
    attended = attended.reshape(row_count, local_width)
    chunk_count = 2 if row_count % 16 == 0 else 1
    chunk_rows = row_count // chunk_count
    outputs = []
    for chunk in range(chunk_count):
        rows = slice(chunk * chunk_rows, (chunk + 1) * chunk_rows)
        partial_out = jnp.dot(attended[rows], out_weight, preferred_element_type=jnp.float32)
        out_sum = scatter_heads(partial_out, head_id, head_total)
        stream_two = (stream[rows].astype(jnp.float32) + out_sum).astype(jnp.bfloat16)
        stream_two_full = gather_heads(stream_two, head_id, head_total)
        normed_two = layer_norm(stream_two_full, gain_two).astype(jnp.bfloat16)
        hidden = jax.nn.gelu(
            jnp.dot(normed_two, up_weight, preferred_element_type=jnp.float32), approximate=True
        ).astype(jnp.bfloat16)
        lowered = jnp.dot(hidden, down_weight, preferred_element_type=jnp.float32)
        mixed = scatter_heads(lowered, head_id, head_total)
        outputs.append((stream_two.astype(jnp.float32) + mixed).astype(jnp.bfloat16))
    return jnp.concatenate(outputs, axis=0)

def solution(mesh):
    return jax.shard_map(
        shards,
        mesh=mesh,
        in_specs=(
            P(("groups", "bricks"), "heads"),
            P("groups"),
            P("groups", None),
            P(None, "heads"),
            P("heads"),
            P(),
            P(None, "heads"),
            P(None, "heads"),
            P(None, "heads"),
            P("heads", None),
            P(),
            P(None, "heads"),
            P("heads", None),
        ),
        out_specs=P(("groups", "bricks"), "heads"),
        check_vma=False,
    )
```

```python
import jax
import jax.numpy as jnp
from jax import lax
from jax.sharding import PartitionSpec as P

EDGE = 8
HEAD_DIM = 64


epsilon = 1e-05


def extended_2(value, sides, width):
    for axis, dim in sides:
        size, length = (lax.axis_size(axis), value.shape[dim])
        up = [(i, (i + 1) % size) for i in range(size - 1)]
        down = [(j, i) for i, j in up]
        last = lax.slice_in_dim(value, length - width, length, axis=dim)
        first = lax.slice_in_dim(value, 0, width, axis=dim)
        before = lax.ppermute(last, axis, up)
        after = lax.ppermute(first, axis, down)
        value = jnp.concatenate([before, value, after], axis=dim)
    return value


def layer_norm(inputs, gain_vec):
    values = inputs.astype(jnp.float32)
    center = values - jnp.mean(values, axis=-1, keepdims=True)
    spread = jnp.mean(center * center, axis=-1, keepdims=True)
    return center * lax.rsqrt(spread + epsilon) * gain_vec.astype(jnp.float32)


def depthwise(brick_vals, lower_face, upper_face, conv_weight, conv_bias):
    brick_count = brick_vals.shape[0]
    edge_len = brick_vals.shape[1]
    channels = brick_vals.shape[3]
    layers = jnp.concatenate([lower_face[:, None], brick_vals, upper_face[:, None]], axis=1)
    layers = layers.reshape(brick_count, edge_len + 2, edge_len, edge_len, channels)
    padded = jnp.pad(layers, ((0, 0), (0, 0), (1, 1), (1, 1), (0, 0)))
    weights = conv_weight.astype(jnp.float32)
    summed = jnp.zeros((brick_count, edge_len, edge_len, edge_len, channels), jnp.float32)
    for step_x in range(3):
        for step_y in range(3):
            for step_z in range(3):
                window = padded[
                    :,
                    step_x : step_x + edge_len,
                    step_y : step_y + edge_len,
                    step_z : step_z + edge_len,
                ]
                summed = summed + weights[step_x * 9 + step_y * 3 + step_z] * window
    return summed.reshape(brick_count * edge_len**3, channels) + conv_bias.astype(jnp.float32)


def level_count(total):
    levels = total.bit_length() - 1
    assert 1 << levels == total
    return levels


def scatter_heads(partial, head_id, head_total):
    levels = level_count(head_total)
    rows = partial.shape[0]
    width = partial.shape[1] // head_total
    current = partial.reshape((rows,) + (2,) * levels + (width,))
    for level in range(levels):
        bit = 1 << level
        axis = levels - level
        mine = (head_id >> level) & 1
        keep = lax.dynamic_index_in_dim(current, mine, axis, keepdims=False)
        give = lax.dynamic_index_in_dim(current, 1 - mine, axis, keepdims=False)
        got = lax.ppermute(
            give.astype(jnp.bfloat16), "heads", [(i, i ^ bit) for i in range(head_total)]
        )
        current = keep + got.astype(jnp.float32)
    return current.reshape(rows, width)


def gather_heads(piece, head_id, head_total):
    levels = level_count(head_total)
    rows, width = piece.shape
    current = piece
    for level in reversed(range(levels)):
        bit = 1 << level
        mine = (head_id >> level) & 1
        got = lax.ppermute(current, "heads", [(i, i ^ bit) for i in range(head_total)])
        low = jnp.where(mine == 0, current, got)
        high = jnp.where(mine == 0, got, current)
        current = jnp.stack([low, high], axis=current.ndim - 1)
    return current.reshape(rows, head_total * width)


def absorb_block(state, query_heads, block, linked, head_count, brick_rows, local_width):
    row_max, row_mass, weighted = state
    key_rows = block[:, :local_width].reshape(-1, head_count, HEAD_DIM)
    value_rows = block[:, local_width:].reshape(-1, head_count, HEAD_DIM)
    scores = (
        jnp.einsum("bqhd,khd->bhqk", query_heads, key_rows, preferred_element_type=jnp.float32)
        * HEAD_DIM ** (-0.5)
    )
    keep = jnp.repeat(linked, brick_rows, axis=1, total_repeat_length=key_rows.shape[0])
    scores = jnp.where(keep[:, None, None, :], scores, -1e30)
    max_new = jnp.maximum(row_max, jnp.max(scores, axis=-1))
    factor = jnp.exp(row_max - max_new)
    weights = jnp.exp(scores - max_new[..., None])
    mass_new = row_mass * factor + jnp.sum(weights, axis=-1)
    sum_new = weighted * jnp.transpose(factor, (0, 2, 1))[..., None] + jnp.einsum(
        "bhqk,khd->bqhd", weights.astype(jnp.bfloat16), value_rows,
        preferred_element_type=jnp.float32,
    )
    return max_new, mass_new, sum_new


def shards(
    voxel_feats,
    face_open,
    pattern,
    conv_weight,
    conv_bias,
    gain_one,
    query_weight,
    key_weight,
    value_weight,
    out_weight,
    gain_two,
    up_weight,
    down_weight,
):
    row_count = voxel_feats.shape[0]
    local_width = voxel_feats.shape[1]
    face_rows = EDGE * EDGE
    brick_rows = EDGE * face_rows
    local_bricks = row_count // brick_rows
    brick_total = pattern.shape[0]
    first_brick = lax.axis_index("bricks") * local_bricks
    extended = extended_2(voxel_feats, (("bricks", 0),), face_rows)
    brick_vals = extended[face_rows : face_rows + row_count].astype(jnp.float32)
    brick_vals = brick_vals.reshape(local_bricks, EDGE, face_rows, local_width)
    lower_face = jnp.concatenate(
        [extended[:face_rows].astype(jnp.float32)[None], brick_vals[:-1, EDGE - 1]], axis=0
    )
    upper_face = jnp.concatenate(
        [brick_vals[1:, 0], extended[face_rows + row_count :].astype(jnp.float32)[None]], axis=0
    )
    brick_ids = first_brick + jnp.arange(local_bricks, dtype=jnp.int32)
    lower_open = jnp.where(brick_ids >= 1, jnp.take(face_open, brick_ids), 0)
    upper_open = jnp.where(
        brick_ids + 1 < brick_total,
        jnp.take(face_open, jnp.minimum(brick_ids + 1, brick_total - 1)),
        0,
    )
    lower_face = lower_face * lower_open.astype(jnp.float32)[:, None, None]
    upper_face = upper_face * upper_open.astype(jnp.float32)[:, None, None]
    conv_out = depthwise(brick_vals, lower_face, upper_face, conv_weight, conv_bias)
    stream = (voxel_feats.astype(jnp.float32) + conv_out).astype(jnp.bfloat16)
    head_total = lax.axis_size("heads")
    head_id = lax.axis_index("heads")
    head_count = local_width // HEAD_DIM
    brick_dev = lax.axis_index("bricks")
    dev_total = lax.axis_size("bricks")
    ring = [(i, (i + 1) % dev_total) for i in range(dev_total)]
    pair_weight = jnp.concatenate([key_weight, value_weight], axis=1)
    linked_rows = lax.dynamic_slice_in_dim(pattern, first_brick, local_bricks, 0)
    state = (
        jnp.full((local_bricks, head_count, brick_rows), -1e30, jnp.float32),
        jnp.zeros((local_bricks, head_count, brick_rows), jnp.float32),
        jnp.zeros((local_bricks, brick_rows, head_count, HEAD_DIM), jnp.float32),
    )
    if dev_total > 1:
        ring_block = lax.ppermute(stream, "bricks", ring)
    full_now = gather_heads(stream, head_id, head_total)
    query_heads = None
    for step in range(dev_total):
        normed_now = layer_norm(full_now, gain_one).astype(jnp.bfloat16)
        if step == 0:
            queries = jnp.dot(normed_now, query_weight, preferred_element_type=jnp.float32).astype(
                jnp.bfloat16
            )
            query_heads = queries.reshape(local_bricks, brick_rows, head_count, HEAD_DIM)
        pair_block = jnp.dot(normed_now, pair_weight, preferred_element_type=jnp.float32).astype(
            jnp.bfloat16
        )
        source = (brick_dev - step) % dev_total
        key_ids = source * local_bricks + jnp.arange(local_bricks, dtype=jnp.int32)
        linked = jnp.take(linked_rows, key_ids, axis=1) > 0
        state = absorb_block(
            state, query_heads, pair_block, linked, head_count, brick_rows, local_width
        )
        if step + 1 < dev_total:
            arrived = ring_block
            if step + 2 < dev_total:
                ring_block = lax.ppermute(arrived, "bricks", ring)
            full_next = gather_heads(arrived, head_id, head_total)
            if step + 2 < dev_total:
                state, full_now, ring_block = lax.optimization_barrier(
                    (state, full_next, ring_block)
                )
            else:
                state, full_now = lax.optimization_barrier((state, full_next))
    row_max, row_mass, weighted = state
    attended = (weighted / jnp.transpose(row_mass, (0, 2, 1))[:, :, :, None]).astype(jnp.bfloat16)
    attended = attended.reshape(row_count, local_width)
    chunk_count = 2 if row_count % 16 == 0 else 1
    chunk_rows = row_count // chunk_count
    outputs = []
    for chunk in range(chunk_count):
        rows = slice(chunk * chunk_rows, (chunk + 1) * chunk_rows)
        partial_out = jnp.dot(attended[rows], out_weight, preferred_element_type=jnp.float32)
        out_sum = scatter_heads(partial_out, head_id, head_total)
        stream_two = (stream[rows].astype(jnp.float32) + out_sum).astype(jnp.bfloat16)
        stream_two_full = gather_heads(stream_two, head_id, head_total)
        normed_two = layer_norm(stream_two_full, gain_two).astype(jnp.bfloat16)
        hidden = jax.nn.gelu(
            jnp.dot(normed_two, up_weight, preferred_element_type=jnp.float32), approximate=True
        ).astype(jnp.bfloat16)
        lowered = jnp.dot(hidden, down_weight, preferred_element_type=jnp.float32)
        mixed = scatter_heads(lowered, head_id, head_total)
        outputs.append((stream_two.astype(jnp.float32) + mixed).astype(jnp.bfloat16))
    return jnp.concatenate(outputs, axis=0)

def solution(mesh):
    return jax.shard_map(
        shards,
        mesh=mesh,
        in_specs=(
            P(("groups", "bricks"), "heads"),
            P("groups"),
            P("groups", None),
            P(None, "heads"),
            P("heads"),
            P(),
            P(None, "heads"),
            P(None, "heads"),
            P(None, "heads"),
            P("heads", None),
            P(),
            P(None, "heads"),
            P("heads", None),
        ),
        out_specs=P(("groups", "bricks"), "heads"),
        check_vma=False,
    )
```

```python
import jax
import jax.numpy as jnp
from jax import lax
from jax.sharding import PartitionSpec as P

EDGE = 8
HEAD_DIM = 64


epsilon = 1e-05


def extended_2(value, sides, width):
    for axis, dim in sides:
        size, length = (lax.axis_size(axis), value.shape[dim])
        up = [(i, (i + 1) % size) for i in range(size - 1)]
        down = [(j, i) for i, j in up]
        last = lax.slice_in_dim(value, length - width, length, axis=dim)
        first = lax.slice_in_dim(value, 0, width, axis=dim)
        before = lax.ppermute(last, axis, up)
        after = lax.ppermute(first, axis, down)
        value = jnp.concatenate([before, value, after], axis=dim)
    return value


def layer_norm(inputs, gain_vec):
    values = inputs.astype(jnp.float32)
    center = values - jnp.mean(values, axis=-1, keepdims=True)
    spread = jnp.mean(center * center, axis=-1, keepdims=True)
    return center * lax.rsqrt(spread + epsilon) * gain_vec.astype(jnp.float32)


def depthwise(brick_vals, lower_face, upper_face, conv_weight, conv_bias):
    brick_count = brick_vals.shape[0]
    edge_len = brick_vals.shape[1]
    channels = brick_vals.shape[3]
    layers = jnp.concatenate([lower_face[:, None], brick_vals, upper_face[:, None]], axis=1)
    layers = layers.reshape(brick_count, edge_len + 2, edge_len, edge_len, channels)
    padded = jnp.pad(layers, ((0, 0), (0, 0), (1, 1), (1, 1), (0, 0)))
    weights = conv_weight.astype(jnp.float32)
    summed = jnp.zeros((brick_count, edge_len, edge_len, edge_len, channels), jnp.float32)
    for step_x in range(3):
        for step_y in range(3):
            for step_z in range(3):
                window = padded[
                    :,
                    step_x : step_x + edge_len,
                    step_y : step_y + edge_len,
                    step_z : step_z + edge_len,
                ]
                summed = summed + weights[step_x * 9 + step_y * 3 + step_z] * window
    return summed.reshape(brick_count * edge_len**3, channels) + conv_bias.astype(jnp.float32)


def level_count(total):
    levels = total.bit_length() - 1
    assert 1 << levels == total
    return levels


def scatter_heads(partial, head_id, head_total):
    levels = level_count(head_total)
    rows = partial.shape[0]
    width = partial.shape[1] // head_total
    current = partial.reshape((rows,) + (2,) * levels + (width,))
    for level in range(levels):
        bit = 1 << level
        axis = levels - level
        mine = (head_id >> level) & 1
        keep = lax.dynamic_index_in_dim(current, mine, axis, keepdims=False)
        give = lax.dynamic_index_in_dim(current, 1 - mine, axis, keepdims=False)
        got = lax.ppermute(
            give.astype(jnp.bfloat16), "heads", [(i, i ^ bit) for i in range(head_total)]
        )
        current = keep + got.astype(jnp.float32)
    return current.reshape(rows, width)


def gather_heads(piece, head_id, head_total):
    levels = level_count(head_total)
    rows, width = piece.shape
    current = piece
    for level in reversed(range(levels)):
        bit = 1 << level
        mine = (head_id >> level) & 1
        got = lax.ppermute(current, "heads", [(i, i ^ bit) for i in range(head_total)])
        low = jnp.where(mine == 0, current, got)
        high = jnp.where(mine == 0, got, current)
        current = jnp.stack([low, high], axis=current.ndim - 1)
    return current.reshape(rows, head_total * width)


def absorb_block(state, query_heads, block, linked, head_count, brick_rows, local_width):
    row_max, row_mass, weighted = state
    key_rows = block[:, :local_width].reshape(-1, head_count, HEAD_DIM)
    value_rows = block[:, local_width:].reshape(-1, head_count, HEAD_DIM)
    scores = (
        jnp.einsum("bqhd,khd->bhqk", query_heads, key_rows, preferred_element_type=jnp.float32)
        * HEAD_DIM ** (-0.5)
    )
    keep = jnp.repeat(linked, brick_rows, axis=1, total_repeat_length=key_rows.shape[0])
    scores = jnp.where(keep[:, None, None, :], scores, -1e30)
    max_new = jnp.maximum(row_max, jnp.max(scores, axis=-1))
    factor = jnp.exp(row_max - max_new)
    weights = jnp.exp(scores - max_new[..., None])
    mass_new = row_mass * factor + jnp.sum(weights, axis=-1)
    sum_new = weighted * jnp.transpose(factor, (0, 2, 1))[..., None] + jnp.einsum(
        "bhqk,khd->bqhd", weights.astype(jnp.bfloat16), value_rows,
        preferred_element_type=jnp.float32,
    )
    return max_new, mass_new, sum_new


def shifted_depthwise(brick_vals, lower_face, upper_face, conv_weight, conv_bias):
    brick_count, edge_len, face_rows, channels = brick_vals.shape
    brick_rows = edge_len * face_rows
    layers = jnp.concatenate([lower_face[:, None], brick_vals, upper_face[:, None]], axis=1)
    flat = layers.reshape(brick_count, (edge_len + 2) * face_rows, channels)
    reach = face_rows + edge_len + 1
    flat = jnp.pad(flat, ((0, 0), (reach, reach), (0, 0)))
    row_ids = jnp.arange(brick_rows, dtype=jnp.int32)[:, None]
    y_ids = (row_ids // edge_len) % edge_len
    z_ids = row_ids % edge_len
    weights = conv_weight.astype(jnp.float32)
    summed = jnp.zeros((brick_count, brick_rows, channels), jnp.float32)
    for step_x in range(3):
        for step_y in range(3):
            for step_z in range(3):
                offset = (step_x - 1) * face_rows + (step_y - 1) * edge_len + (step_z - 1)
                begin = reach + face_rows + offset
                window = flat[:, begin : begin + brick_rows]
                inside = (
                    (y_ids + step_y - 1 >= 0)
                    & (y_ids + step_y - 1 < edge_len)
                    & (z_ids + step_z - 1 >= 0)
                    & (z_ids + step_z - 1 < edge_len)
                )
                window = jnp.where(inside[None], window, 0.0)
                summed = summed + weights[step_x * 9 + step_y * 3 + step_z] * window
    return summed.reshape(brick_count * brick_rows, channels) + conv_bias.astype(jnp.float32)


def shards(
    voxel_feats,
    face_open,
    pattern,
    conv_weight,
    conv_bias,
    gain_one,
    query_weight,
    key_weight,
    value_weight,
    out_weight,
    gain_two,
    up_weight,
    down_weight,
):
    row_count = voxel_feats.shape[0]
    local_width = voxel_feats.shape[1]
    face_rows = EDGE * EDGE
    brick_rows = EDGE * face_rows
    local_bricks = row_count // brick_rows
    brick_total = pattern.shape[0]
    first_brick = lax.axis_index("bricks") * local_bricks
    extended = extended_2(voxel_feats, (("bricks", 0),), face_rows)
    brick_vals = extended[face_rows : face_rows + row_count].astype(jnp.float32)
    brick_vals = brick_vals.reshape(local_bricks, EDGE, face_rows, local_width)
    lower_face = jnp.concatenate(
        [extended[:face_rows].astype(jnp.float32)[None], brick_vals[:-1, EDGE - 1]], axis=0
    )
    upper_face = jnp.concatenate(
        [brick_vals[1:, 0], extended[face_rows + row_count :].astype(jnp.float32)[None]], axis=0
    )
    brick_ids = first_brick + jnp.arange(local_bricks, dtype=jnp.int32)
    lower_open = jnp.where(brick_ids >= 1, jnp.take(face_open, brick_ids), 0)
    upper_open = jnp.where(
        brick_ids + 1 < brick_total,
        jnp.take(face_open, jnp.minimum(brick_ids + 1, brick_total - 1)),
        0,
    )
    lower_face = lower_face * lower_open.astype(jnp.float32)[:, None, None]
    upper_face = upper_face * upper_open.astype(jnp.float32)[:, None, None]
    conv_out = shifted_depthwise(brick_vals, lower_face, upper_face, conv_weight, conv_bias)
    stream = (voxel_feats.astype(jnp.float32) + conv_out).astype(jnp.bfloat16)
    head_total = lax.axis_size("heads")
    head_id = lax.axis_index("heads")
    head_count = local_width // HEAD_DIM
    brick_dev = lax.axis_index("bricks")
    dev_total = lax.axis_size("bricks")
    ring = [(i, (i + 1) % dev_total) for i in range(dev_total)]
    pair_weight = jnp.concatenate([key_weight, value_weight], axis=1)
    linked_rows = lax.dynamic_slice_in_dim(pattern, first_brick, local_bricks, 0)
    state = (
        jnp.full((local_bricks, head_count, brick_rows), -1e30, jnp.float32),
        jnp.zeros((local_bricks, head_count, brick_rows), jnp.float32),
        jnp.zeros((local_bricks, brick_rows, head_count, HEAD_DIM), jnp.float32),
    )
    if dev_total > 1:
        ring_block = lax.ppermute(stream, "bricks", ring)
    full_now = gather_heads(stream, head_id, head_total)
    query_heads = None
    for step in range(dev_total):
        normed_now = layer_norm(full_now, gain_one).astype(jnp.bfloat16)
        if step == 0:
            queries = jnp.dot(normed_now, query_weight, preferred_element_type=jnp.float32).astype(
                jnp.bfloat16
            )
            query_heads = queries.reshape(local_bricks, brick_rows, head_count, HEAD_DIM)
        pair_block = jnp.dot(normed_now, pair_weight, preferred_element_type=jnp.float32).astype(
            jnp.bfloat16
        )
        source = (brick_dev - step) % dev_total
        key_ids = source * local_bricks + jnp.arange(local_bricks, dtype=jnp.int32)
        linked = jnp.take(linked_rows, key_ids, axis=1) > 0
        state = absorb_block(
            state, query_heads, pair_block, linked, head_count, brick_rows, local_width
        )
        if step + 1 < dev_total:
            arrived = ring_block
            if step + 2 < dev_total:
                ring_block = lax.ppermute(arrived, "bricks", ring)
            full_next = gather_heads(arrived, head_id, head_total)
            if step + 2 < dev_total:
                state, full_now, ring_block = lax.optimization_barrier(
                    (state, full_next, ring_block)
                )
            else:
                state, full_now = lax.optimization_barrier((state, full_next))
    row_max, row_mass, weighted = state
    attended = (weighted / jnp.transpose(row_mass, (0, 2, 1))[:, :, :, None]).astype(jnp.bfloat16)
    attended = attended.reshape(row_count, local_width)
    chunk_count = 2 if row_count % 16 == 0 else 1
    chunk_rows = row_count // chunk_count
    outputs = []
    for chunk in range(chunk_count):
        rows = slice(chunk * chunk_rows, (chunk + 1) * chunk_rows)
        partial_out = jnp.dot(attended[rows], out_weight, preferred_element_type=jnp.float32)
        out_sum = scatter_heads(partial_out, head_id, head_total)
        stream_two = (stream[rows].astype(jnp.float32) + out_sum).astype(jnp.bfloat16)
        stream_two_full = gather_heads(stream_two, head_id, head_total)
        normed_two = layer_norm(stream_two_full, gain_two).astype(jnp.bfloat16)
        hidden = jax.nn.gelu(
            jnp.dot(normed_two, up_weight, preferred_element_type=jnp.float32), approximate=True
        ).astype(jnp.bfloat16)
        lowered = jnp.dot(hidden, down_weight, preferred_element_type=jnp.float32)
        mixed = scatter_heads(lowered, head_id, head_total)
        outputs.append((stream_two.astype(jnp.float32) + mixed).astype(jnp.bfloat16))
    return jnp.concatenate(outputs, axis=0)

def solution(mesh):
    return jax.shard_map(
        shards,
        mesh=mesh,
        in_specs=(
            P(("groups", "bricks"), "heads"),
            P("groups"),
            P("groups", None),
            P(None, "heads"),
            P("heads"),
            P(),
            P(None, "heads"),
            P(None, "heads"),
            P(None, "heads"),
            P("heads", None),
            P(),
            P(None, "heads"),
            P("heads", None),
        ),
        out_specs=P(("groups", "bricks"), "heads"),
        check_vma=False,
    )
```

```python
import jax
import jax.numpy as jnp
from jax import lax
from jax.sharding import PartitionSpec as P

EDGE = 8
HEAD_DIM = 64


epsilon = 1e-05


def extended_2(value, sides, width):
    for axis, dim in sides:
        size, length = (lax.axis_size(axis), value.shape[dim])
        up = [(i, (i + 1) % size) for i in range(size - 1)]
        down = [(j, i) for i, j in up]
        last = lax.slice_in_dim(value, length - width, length, axis=dim)
        first = lax.slice_in_dim(value, 0, width, axis=dim)
        before = lax.ppermute(last, axis, up)
        after = lax.ppermute(first, axis, down)
        value = jnp.concatenate([before, value, after], axis=dim)
    return value


def layer_norm(inputs, gain_vec):
    values = inputs.astype(jnp.float32)
    center = values - jnp.mean(values, axis=-1, keepdims=True)
    spread = jnp.mean(center * center, axis=-1, keepdims=True)
    return center * lax.rsqrt(spread + epsilon) * gain_vec.astype(jnp.float32)


def depthwise(brick_vals, lower_face, upper_face, conv_weight, conv_bias):
    brick_count = brick_vals.shape[0]
    edge_len = brick_vals.shape[1]
    channels = brick_vals.shape[3]
    layers = jnp.concatenate([lower_face[:, None], brick_vals, upper_face[:, None]], axis=1)
    layers = layers.reshape(brick_count, edge_len + 2, edge_len, edge_len, channels)
    padded = jnp.pad(layers, ((0, 0), (0, 0), (1, 1), (1, 1), (0, 0)))
    weights = conv_weight.astype(jnp.float32)
    summed = jnp.zeros((brick_count, edge_len, edge_len, edge_len, channels), jnp.float32)
    for step_x in range(3):
        for step_y in range(3):
            for step_z in range(3):
                window = padded[
                    :,
                    step_x : step_x + edge_len,
                    step_y : step_y + edge_len,
                    step_z : step_z + edge_len,
                ]
                summed = summed + weights[step_x * 9 + step_y * 3 + step_z] * window
    return summed.reshape(brick_count * edge_len**3, channels) + conv_bias.astype(jnp.float32)


def level_count(total):
    levels = total.bit_length() - 1
    assert 1 << levels == total
    return levels


def scatter_heads(partial, head_id, head_total):
    levels = level_count(head_total)
    rows = partial.shape[0]
    width = partial.shape[1] // head_total
    current = partial.reshape((rows,) + (2,) * levels + (width,))
    for level in range(levels):
        bit = 1 << level
        axis = levels - level
        mine = (head_id >> level) & 1
        keep = lax.dynamic_index_in_dim(current, mine, axis, keepdims=False)
        give = lax.dynamic_index_in_dim(current, 1 - mine, axis, keepdims=False)
        got = lax.ppermute(
            give.astype(jnp.bfloat16), "heads", [(i, i ^ bit) for i in range(head_total)]
        )
        current = keep + got.astype(jnp.float32)
    return current.reshape(rows, width)


def gather_heads(piece, head_id, head_total):
    levels = level_count(head_total)
    rows, width = piece.shape
    current = piece
    for level in reversed(range(levels)):
        bit = 1 << level
        mine = (head_id >> level) & 1
        got = lax.ppermute(current, "heads", [(i, i ^ bit) for i in range(head_total)])
        low = jnp.where(mine == 0, current, got)
        high = jnp.where(mine == 0, got, current)
        current = jnp.stack([low, high], axis=current.ndim - 1)
    return current.reshape(rows, head_total * width)


def absorb_block(state, query_heads, block, linked, head_count, brick_rows, local_width):
    row_max, row_mass, weighted = state
    key_rows = block[:, :local_width].reshape(-1, head_count, HEAD_DIM)
    value_rows = block[:, local_width:].reshape(-1, head_count, HEAD_DIM)
    scores = (
        jnp.einsum("bqhd,khd->bhqk", query_heads, key_rows, preferred_element_type=jnp.float32)
        * HEAD_DIM ** (-0.5)
    )
    keep = jnp.repeat(linked, brick_rows, axis=1, total_repeat_length=key_rows.shape[0])
    scores = jnp.where(keep[:, None, None, :], scores, -1e30)
    max_new = jnp.maximum(row_max, jnp.max(scores, axis=-1))
    factor = jnp.exp(row_max - max_new)
    weights = jnp.exp(scores - max_new[..., None])
    mass_new = row_mass * factor + jnp.sum(weights, axis=-1)
    sum_new = weighted * jnp.transpose(factor, (0, 2, 1))[..., None] + jnp.einsum(
        "bhqk,khd->bqhd", weights.astype(jnp.bfloat16), value_rows,
        preferred_element_type=jnp.float32,
    )
    return max_new, mass_new, sum_new


def shards(
    voxel_feats,
    face_open,
    pattern,
    conv_weight,
    conv_bias,
    gain_one,
    query_weight,
    key_weight,
    value_weight,
    out_weight,
    gain_two,
    up_weight,
    down_weight,
):
    row_count = voxel_feats.shape[0]
    local_width = voxel_feats.shape[1]
    face_rows = EDGE * EDGE
    brick_rows = EDGE * face_rows
    local_bricks = row_count // brick_rows
    brick_total = pattern.shape[0]
    first_brick = lax.axis_index("bricks") * local_bricks
    extended = extended_2(voxel_feats, (("bricks", 0),), face_rows)
    brick_vals = extended[face_rows : face_rows + row_count].astype(jnp.float32)
    brick_vals = brick_vals.reshape(local_bricks, EDGE, face_rows, local_width)
    lower_face = jnp.concatenate(
        [extended[:face_rows].astype(jnp.float32)[None], brick_vals[:-1, EDGE - 1]], axis=0
    )
    upper_face = jnp.concatenate(
        [brick_vals[1:, 0], extended[face_rows + row_count :].astype(jnp.float32)[None]], axis=0
    )
    brick_ids = first_brick + jnp.arange(local_bricks, dtype=jnp.int32)
    lower_open = jnp.where(brick_ids >= 1, jnp.take(face_open, brick_ids), 0)
    upper_open = jnp.where(
        brick_ids + 1 < brick_total,
        jnp.take(face_open, jnp.minimum(brick_ids + 1, brick_total - 1)),
        0,
    )
    lower_face = lower_face * lower_open.astype(jnp.float32)[:, None, None]
    upper_face = upper_face * upper_open.astype(jnp.float32)[:, None, None]
    conv_out = depthwise(brick_vals, lower_face, upper_face, conv_weight, conv_bias)
    stream = (voxel_feats.astype(jnp.float32) + conv_out).astype(jnp.bfloat16)
    head_total = lax.axis_size("heads")
    head_id = lax.axis_index("heads")
    head_count = local_width // HEAD_DIM
    brick_dev = lax.axis_index("bricks")
    dev_total = lax.axis_size("bricks")
    ring = [(i, (i + 1) % dev_total) for i in range(dev_total)]
    pair_weight = jnp.concatenate([key_weight, value_weight], axis=1)
    linked_rows = lax.dynamic_slice_in_dim(pattern, first_brick, local_bricks, 0)
    state = (
        jnp.full((local_bricks, head_count, brick_rows), -1e30, jnp.float32),
        jnp.zeros((local_bricks, head_count, brick_rows), jnp.float32),
        jnp.zeros((local_bricks, brick_rows, head_count, HEAD_DIM), jnp.float32),
    )
    if dev_total > 1:
        ring_block = lax.ppermute(stream, "bricks", ring)
    full_now = gather_heads(stream, head_id, head_total)
    query_heads = None
    for step in range(dev_total):
        normed_now = layer_norm(full_now, gain_one).astype(jnp.bfloat16)
        if step == 0:
            queries = jnp.dot(normed_now, query_weight, preferred_element_type=jnp.float32).astype(
                jnp.bfloat16
            )
            query_heads = queries.reshape(local_bricks, brick_rows, head_count, HEAD_DIM)
        pair_block = jnp.dot(normed_now, pair_weight, preferred_element_type=jnp.float32).astype(
            jnp.bfloat16
        )
        source = (brick_dev - step) % dev_total
        key_ids = source * local_bricks + jnp.arange(local_bricks, dtype=jnp.int32)
        linked = jnp.take(linked_rows, key_ids, axis=1) > 0
        state = absorb_block(
            state, query_heads, pair_block, linked, head_count, brick_rows, local_width
        )
        if step + 1 < dev_total:
            arrived = ring_block
            if step + 2 < dev_total:
                ring_block = lax.ppermute(arrived, "bricks", ring)
            full_next = gather_heads(arrived, head_id, head_total)
            if step + 2 < dev_total:
                state, full_now, ring_block = lax.optimization_barrier(
                    (state, full_next, ring_block)
                )
            else:
                state, full_now = lax.optimization_barrier((state, full_next))
    row_max, row_mass, weighted = state
    attended = (weighted / jnp.transpose(row_mass, (0, 2, 1))[:, :, :, None]).astype(jnp.bfloat16)
    attended = attended.reshape(row_count, local_width)
    chunk_count = 4 if row_count % 32 == 0 else 1
    chunk_rows = row_count // chunk_count
    outputs = []
    for chunk in range(chunk_count):
        rows = slice(chunk * chunk_rows, (chunk + 1) * chunk_rows)
        partial_out = jnp.dot(attended[rows], out_weight, preferred_element_type=jnp.float32)
        out_sum = scatter_heads(partial_out, head_id, head_total)
        stream_two = (stream[rows].astype(jnp.float32) + out_sum).astype(jnp.bfloat16)
        stream_two_full = gather_heads(stream_two, head_id, head_total)
        normed_two = layer_norm(stream_two_full, gain_two).astype(jnp.bfloat16)
        hidden = jax.nn.gelu(
            jnp.dot(normed_two, up_weight, preferred_element_type=jnp.float32), approximate=True
        ).astype(jnp.bfloat16)
        lowered = jnp.dot(hidden, down_weight, preferred_element_type=jnp.float32)
        mixed = scatter_heads(lowered, head_id, head_total)
        outputs.append((stream_two.astype(jnp.float32) + mixed).astype(jnp.bfloat16))
    return jnp.concatenate(outputs, axis=0)

def solution(mesh):
    return jax.shard_map(
        shards,
        mesh=mesh,
        in_specs=(
            P(("groups", "bricks"), "heads"),
            P("groups"),
            P("groups", None),
            P(None, "heads"),
            P("heads"),
            P(),
            P(None, "heads"),
            P(None, "heads"),
            P(None, "heads"),
            P("heads", None),
            P(),
            P(None, "heads"),
            P("heads", None),
        ),
        out_specs=P(("groups", "bricks"), "heads"),
        check_vma=False,
    )
```

```python
import jax
import jax.numpy as jnp
from jax import lax
from jax.sharding import PartitionSpec as P

EDGE = 8
HEAD_DIM = 64


epsilon = 1e-05


def extended_2(value, sides, width):
    for axis, dim in sides:
        size, length = (lax.axis_size(axis), value.shape[dim])
        up = [(i, (i + 1) % size) for i in range(size - 1)]
        down = [(j, i) for i, j in up]
        last = lax.slice_in_dim(value, length - width, length, axis=dim)
        first = lax.slice_in_dim(value, 0, width, axis=dim)
        before = lax.ppermute(last, axis, up)
        after = lax.ppermute(first, axis, down)
        value = jnp.concatenate([before, value, after], axis=dim)
    return value


def layer_norm(inputs, gain_vec):
    values = inputs.astype(jnp.float32)
    center = values - jnp.mean(values, axis=-1, keepdims=True)
    spread = jnp.mean(center * center, axis=-1, keepdims=True)
    return center * lax.rsqrt(spread + epsilon) * gain_vec.astype(jnp.float32)


def depthwise(brick_vals, lower_face, upper_face, conv_weight, conv_bias):
    brick_count = brick_vals.shape[0]
    edge_len = brick_vals.shape[1]
    channels = brick_vals.shape[3]
    layers = jnp.concatenate([lower_face[:, None], brick_vals, upper_face[:, None]], axis=1)
    layers = layers.reshape(brick_count, edge_len + 2, edge_len, edge_len, channels)
    padded = jnp.pad(layers, ((0, 0), (0, 0), (1, 1), (1, 1), (0, 0)))
    weights = conv_weight.astype(jnp.float32)
    summed = jnp.zeros((brick_count, edge_len, edge_len, edge_len, channels), jnp.float32)
    for step_x in range(3):
        for step_y in range(3):
            for step_z in range(3):
                window = padded[
                    :,
                    step_x : step_x + edge_len,
                    step_y : step_y + edge_len,
                    step_z : step_z + edge_len,
                ]
                summed = summed + weights[step_x * 9 + step_y * 3 + step_z] * window
    return summed.reshape(brick_count * edge_len**3, channels) + conv_bias.astype(jnp.float32)


def level_count(total):
    levels = total.bit_length() - 1
    assert 1 << levels == total
    return levels


def scatter_heads(partial, head_id, head_total):
    levels = level_count(head_total)
    rows = partial.shape[0]
    width = partial.shape[1] // head_total
    current = partial.reshape((rows,) + (2,) * levels + (width,))
    for level in range(levels):
        bit = 1 << level
        axis = levels - level
        mine = (head_id >> level) & 1
        keep = lax.dynamic_index_in_dim(current, mine, axis, keepdims=False)
        give = lax.dynamic_index_in_dim(current, 1 - mine, axis, keepdims=False)
        got = lax.ppermute(
            give.astype(jnp.bfloat16), "heads", [(i, i ^ bit) for i in range(head_total)]
        )
        current = keep + got.astype(jnp.float32)
    return current.reshape(rows, width)


def gather_heads(piece, head_id, head_total):
    levels = level_count(head_total)
    rows, width = piece.shape
    current = piece
    for level in reversed(range(levels)):
        bit = 1 << level
        mine = (head_id >> level) & 1
        got = lax.ppermute(current, "heads", [(i, i ^ bit) for i in range(head_total)])
        low = jnp.where(mine == 0, current, got)
        high = jnp.where(mine == 0, got, current)
        current = jnp.stack([low, high], axis=current.ndim - 1)
    return current.reshape(rows, head_total * width)


def gather_levels(current, head_id, head_total, level_list):
    for level in level_list:
        bit = 1 << level
        mine = (head_id >> level) & 1
        got = lax.ppermute(current, "heads", [(i, i ^ bit) for i in range(head_total)])
        low = jnp.where(mine == 0, current, got)
        high = jnp.where(mine == 0, got, current)
        current = jnp.stack([low, high], axis=current.ndim - 1)
    return current


def absorb_block(state, query_heads, block, linked, head_count, brick_rows, local_width):
    row_max, row_mass, weighted = state
    key_rows = block[:, :local_width].reshape(-1, head_count, HEAD_DIM)
    value_rows = block[:, local_width:].reshape(-1, head_count, HEAD_DIM)
    scores = (
        jnp.einsum("bqhd,khd->bhqk", query_heads, key_rows, preferred_element_type=jnp.float32)
        * HEAD_DIM ** (-0.5)
    )
    keep = jnp.repeat(linked, brick_rows, axis=1, total_repeat_length=key_rows.shape[0])
    scores = jnp.where(keep[:, None, None, :], scores, -1e30)
    max_new = jnp.maximum(row_max, jnp.max(scores, axis=-1))
    factor = jnp.exp(row_max - max_new)
    weights = jnp.exp(scores - max_new[..., None])
    mass_new = row_mass * factor + jnp.sum(weights, axis=-1)
    sum_new = weighted * jnp.transpose(factor, (0, 2, 1))[..., None] + jnp.einsum(
        "bhqk,khd->bqhd", weights.astype(jnp.bfloat16), value_rows,
        preferred_element_type=jnp.float32,
    )
    return max_new, mass_new, sum_new


def shards(
    voxel_feats,
    face_open,
    pattern,
    conv_weight,
    conv_bias,
    gain_one,
    query_weight,
    key_weight,
    value_weight,
    out_weight,
    gain_two,
    up_weight,
    down_weight,
):
    row_count = voxel_feats.shape[0]
    local_width = voxel_feats.shape[1]
    face_rows = EDGE * EDGE
    brick_rows = EDGE * face_rows
    local_bricks = row_count // brick_rows
    brick_total = pattern.shape[0]
    first_brick = lax.axis_index("bricks") * local_bricks
    extended = extended_2(voxel_feats, (("bricks", 0),), face_rows)
    brick_vals = extended[face_rows : face_rows + row_count].astype(jnp.float32)
    brick_vals = brick_vals.reshape(local_bricks, EDGE, face_rows, local_width)
    lower_face = jnp.concatenate(
        [extended[:face_rows].astype(jnp.float32)[None], brick_vals[:-1, EDGE - 1]], axis=0
    )
    upper_face = jnp.concatenate(
        [brick_vals[1:, 0], extended[face_rows + row_count :].astype(jnp.float32)[None]], axis=0
    )
    brick_ids = first_brick + jnp.arange(local_bricks, dtype=jnp.int32)
    lower_open = jnp.where(brick_ids >= 1, jnp.take(face_open, brick_ids), 0)
    upper_open = jnp.where(
        brick_ids + 1 < brick_total,
        jnp.take(face_open, jnp.minimum(brick_ids + 1, brick_total - 1)),
        0,
    )
    lower_face = lower_face * lower_open.astype(jnp.float32)[:, None, None]
    upper_face = upper_face * upper_open.astype(jnp.float32)[:, None, None]
    conv_out = depthwise(brick_vals, lower_face, upper_face, conv_weight, conv_bias)
    stream = (voxel_feats.astype(jnp.float32) + conv_out).astype(jnp.bfloat16)
    head_total = lax.axis_size("heads")
    head_id = lax.axis_index("heads")
    head_count = local_width // HEAD_DIM
    brick_dev = lax.axis_index("bricks")
    dev_total = lax.axis_size("bricks")
    ring = [(i, (i + 1) % dev_total) for i in range(dev_total)]
    pair_weight = jnp.concatenate([key_weight, value_weight], axis=1)
    linked_rows = lax.dynamic_slice_in_dim(pattern, first_brick, local_bricks, 0)
    state = (
        jnp.full((local_bricks, head_count, brick_rows), -1e30, jnp.float32),
        jnp.zeros((local_bricks, head_count, brick_rows), jnp.float32),
        jnp.zeros((local_bricks, brick_rows, head_count, HEAD_DIM), jnp.float32),
    )
    levels = level_count(head_total)
    cross_levels = list(reversed(range(1, levels)))
    chip_levels = list(range(min(levels, 1)))
    ringed = {0: stream}
    crossed = {}
    gathered = {}
    query_heads = None
    for slot in range(dev_total + 2):
        made = []
        if 1 <= slot + 1 < dev_total:
            ringed[slot + 1] = lax.ppermute(ringed[slot], "bricks", ring)
            made.append((ringed, slot + 1))
        if slot < dev_total:
            crossed[slot] = gather_levels(ringed[slot], head_id, head_total, cross_levels)
            made.append((crossed, slot))
        if 0 <= slot - 1 < dev_total:
            gathered[slot - 1] = gather_levels(
                crossed[slot - 1], head_id, head_total, chip_levels
            ).reshape(row_count, head_total * local_width)
            made.append((gathered, slot - 1))
        step = slot - 2
        if 0 <= step < dev_total:
            normed_now = layer_norm(gathered[step], gain_one).astype(jnp.bfloat16)
            if step == 0:
                queries = jnp.dot(
                    normed_now, query_weight, preferred_element_type=jnp.float32
                ).astype(jnp.bfloat16)
                query_heads = queries.reshape(local_bricks, brick_rows, head_count, HEAD_DIM)
            pair_block = jnp.dot(
                normed_now, pair_weight, preferred_element_type=jnp.float32
            ).astype(jnp.bfloat16)
            source = (brick_dev - step) % dev_total
            key_ids = source * local_bricks + jnp.arange(local_bricks, dtype=jnp.int32)
            linked = jnp.take(linked_rows, key_ids, axis=1) > 0
            state = absorb_block(
                state, query_heads, pair_block, linked, head_count, brick_rows, local_width
            )
        if slot < dev_total + 1:
            packed = lax.optimization_barrier((state, [table[key] for table, key in made]))
            state = packed[0]
            for (table, key), value in zip(made, packed[1]):
                table[key] = value
    row_max, row_mass, weighted = state
    attended = (weighted / jnp.transpose(row_mass, (0, 2, 1))[:, :, :, None]).astype(jnp.bfloat16)
    attended = attended.reshape(row_count, local_width)
    chunk_count = 2 if row_count % 16 == 0 else 1
    chunk_rows = row_count // chunk_count
    outputs = []
    for chunk in range(chunk_count):
        rows = slice(chunk * chunk_rows, (chunk + 1) * chunk_rows)
        partial_out = jnp.dot(attended[rows], out_weight, preferred_element_type=jnp.float32)
        out_sum = scatter_heads(partial_out, head_id, head_total)
        stream_two = (stream[rows].astype(jnp.float32) + out_sum).astype(jnp.bfloat16)
        stream_two_full = gather_heads(stream_two, head_id, head_total)
        normed_two = layer_norm(stream_two_full, gain_two).astype(jnp.bfloat16)
        hidden = jax.nn.gelu(
            jnp.dot(normed_two, up_weight, preferred_element_type=jnp.float32), approximate=True
        ).astype(jnp.bfloat16)
        lowered = jnp.dot(hidden, down_weight, preferred_element_type=jnp.float32)
        mixed = scatter_heads(lowered, head_id, head_total)
        outputs.append((stream_two.astype(jnp.float32) + mixed).astype(jnp.bfloat16))
    return jnp.concatenate(outputs, axis=0)

def solution(mesh):
    return jax.shard_map(
        shards,
        mesh=mesh,
        in_specs=(
            P(("groups", "bricks"), "heads"),
            P("groups"),
            P("groups", None),
            P(None, "heads"),
            P("heads"),
            P(),
            P(None, "heads"),
            P(None, "heads"),
            P(None, "heads"),
            P("heads", None),
            P(),
            P(None, "heads"),
            P("heads", None),
        ),
        out_specs=P(("groups", "bricks"), "heads"),
        check_vma=False,
    )
```

```python
import jax
import jax.numpy as jnp
from jax import lax
from jax.sharding import PartitionSpec as P

EDGE = 8
HEAD_DIM = 64


epsilon = 1e-05


def extended_2(value, sides, width):
    for axis, dim in sides:
        size, length = (lax.axis_size(axis), value.shape[dim])
        up = [(i, (i + 1) % size) for i in range(size - 1)]
        down = [(j, i) for i, j in up]
        last = lax.slice_in_dim(value, length - width, length, axis=dim)
        first = lax.slice_in_dim(value, 0, width, axis=dim)
        before = lax.ppermute(last, axis, up)
        after = lax.ppermute(first, axis, down)
        value = jnp.concatenate([before, value, after], axis=dim)
    return value


def layer_norm(inputs, gain_vec):
    values = inputs.astype(jnp.float32)
    center = values - jnp.mean(values, axis=-1, keepdims=True)
    spread = jnp.mean(center * center, axis=-1, keepdims=True)
    return center * lax.rsqrt(spread + epsilon) * gain_vec.astype(jnp.float32)


def depthwise(brick_vals, lower_face, upper_face, conv_weight, conv_bias):
    brick_count = brick_vals.shape[0]
    edge_len = brick_vals.shape[1]
    channels = brick_vals.shape[3]
    layers = jnp.concatenate([lower_face[:, None], brick_vals, upper_face[:, None]], axis=1)
    layers = layers.reshape(brick_count, edge_len + 2, edge_len, edge_len, channels)
    padded = jnp.pad(layers, ((0, 0), (0, 0), (1, 1), (1, 1), (0, 0)))
    weights = conv_weight.astype(jnp.float32)
    summed = jnp.zeros((brick_count, edge_len, edge_len, edge_len, channels), jnp.float32)
    for step_x in range(3):
        for step_y in range(3):
            for step_z in range(3):
                window = padded[
                    :,
                    step_x : step_x + edge_len,
                    step_y : step_y + edge_len,
                    step_z : step_z + edge_len,
                ]
                summed = summed + weights[step_x * 9 + step_y * 3 + step_z] * window
    return summed.reshape(brick_count * edge_len**3, channels) + conv_bias.astype(jnp.float32)


def level_count(total):
    levels = total.bit_length() - 1
    assert 1 << levels == total
    return levels


def scatter_heads(partial, head_id, head_total):
    levels = level_count(head_total)
    rows = partial.shape[0]
    width = partial.shape[1] // head_total
    current = partial.reshape((rows,) + (2,) * levels + (width,))
    for level in range(levels):
        bit = 1 << level
        axis = levels - level
        mine = (head_id >> level) & 1
        keep = lax.dynamic_index_in_dim(current, mine, axis, keepdims=False)
        give = lax.dynamic_index_in_dim(current, 1 - mine, axis, keepdims=False)
        got = lax.ppermute(
            give.astype(jnp.bfloat16), "heads", [(i, i ^ bit) for i in range(head_total)]
        )
        current = keep + got.astype(jnp.float32)
    return current.reshape(rows, width)


def gather_heads(piece, head_id, head_total):
    levels = level_count(head_total)
    rows, width = piece.shape
    current = piece
    for level in reversed(range(levels)):
        bit = 1 << level
        mine = (head_id >> level) & 1
        got = lax.ppermute(current, "heads", [(i, i ^ bit) for i in range(head_total)])
        low = jnp.where(mine == 0, current, got)
        high = jnp.where(mine == 0, got, current)
        current = jnp.stack([low, high], axis=current.ndim - 1)
    return current.reshape(rows, head_total * width)


def gather_levels(current, head_id, head_total, level_list):
    for level in level_list:
        bit = 1 << level
        mine = (head_id >> level) & 1
        got = lax.ppermute(current, "heads", [(i, i ^ bit) for i in range(head_total)])
        low = jnp.where(mine == 0, current, got)
        high = jnp.where(mine == 0, got, current)
        current = jnp.stack([low, high], axis=current.ndim - 1)
    return current


def absorb_block(state, query_heads, key_block, value_block, linked, head_count, brick_rows):
    row_max, row_mass, weighted = state
    key_rows = key_block.reshape(-1, head_count, HEAD_DIM)
    value_rows = value_block.reshape(-1, head_count, HEAD_DIM)
    scores = (
        jnp.einsum("bqhd,khd->bhqk", query_heads, key_rows, preferred_element_type=jnp.float32)
        * HEAD_DIM ** (-0.5)
    )
    keep = jnp.repeat(linked, brick_rows, axis=1, total_repeat_length=key_rows.shape[0])
    scores = jnp.where(keep[:, None, None, :], scores, -1e30)
    max_new = jnp.maximum(row_max, jnp.max(scores, axis=-1))
    factor = jnp.exp(row_max - max_new)
    weights = jnp.exp(scores - max_new[..., None])
    mass_new = row_mass * factor + jnp.sum(weights, axis=-1)
    sum_new = weighted * jnp.transpose(factor, (0, 2, 1))[..., None] + jnp.einsum(
        "bhqk,khd->bqhd", weights.astype(jnp.bfloat16), value_rows,
        preferred_element_type=jnp.float32,
    )
    return max_new, mass_new, sum_new


def shards(
    voxel_feats,
    face_open,
    pattern,
    conv_weight,
    conv_bias,
    gain_one,
    query_weight,
    key_weight,
    value_weight,
    out_weight,
    gain_two,
    up_weight,
    down_weight,
):
    row_count = voxel_feats.shape[0]
    local_width = voxel_feats.shape[1]
    face_rows = EDGE * EDGE
    brick_rows = EDGE * face_rows
    local_bricks = row_count // brick_rows
    brick_total = pattern.shape[0]
    first_brick = lax.axis_index("bricks") * local_bricks
    extended = extended_2(voxel_feats, (("bricks", 0),), face_rows)
    brick_vals = extended[face_rows : face_rows + row_count].astype(jnp.float32)
    brick_vals = brick_vals.reshape(local_bricks, EDGE, face_rows, local_width)
    lower_face = jnp.concatenate(
        [extended[:face_rows].astype(jnp.float32)[None], brick_vals[:-1, EDGE - 1]], axis=0
    )
    upper_face = jnp.concatenate(
        [brick_vals[1:, 0], extended[face_rows + row_count :].astype(jnp.float32)[None]], axis=0
    )
    brick_ids = first_brick + jnp.arange(local_bricks, dtype=jnp.int32)
    lower_open = jnp.where(brick_ids >= 1, jnp.take(face_open, brick_ids), 0)
    upper_open = jnp.where(
        brick_ids + 1 < brick_total,
        jnp.take(face_open, jnp.minimum(brick_ids + 1, brick_total - 1)),
        0,
    )
    lower_face = lower_face * lower_open.astype(jnp.float32)[:, None, None]
    upper_face = upper_face * upper_open.astype(jnp.float32)[:, None, None]
    conv_out = depthwise(brick_vals, lower_face, upper_face, conv_weight, conv_bias)
    stream = (voxel_feats.astype(jnp.float32) + conv_out).astype(jnp.bfloat16)
    head_total = lax.axis_size("heads")
    head_id = lax.axis_index("heads")
    head_count = local_width // HEAD_DIM
    brick_dev = lax.axis_index("bricks")
    dev_total = lax.axis_size("bricks")
    ring = [(i, (i + 1) % dev_total) for i in range(dev_total)]
    linked_rows = lax.dynamic_slice_in_dim(pattern, first_brick, local_bricks, 0)
    state = (
        jnp.full((local_bricks, head_count, brick_rows), -1e30, jnp.float32),
        jnp.zeros((local_bricks, head_count, brick_rows), jnp.float32),
        jnp.zeros((local_bricks, brick_rows, head_count, HEAD_DIM), jnp.float32),
    )
    levels = level_count(head_total)
    cross_levels = list(reversed(range(1, levels)))
    chip_levels = list(range(min(levels, 1)))
    ringed = {0: stream}
    crossed = {}
    gathered = {}
    query_heads = None
    for slot in range(dev_total + 2):
        made = []
        if 1 <= slot + 1 < dev_total:
            ringed[slot + 1] = lax.ppermute(ringed[slot], "bricks", ring)
            made.append((ringed, slot + 1))
        if slot < dev_total:
            crossed[slot] = gather_levels(ringed[slot], head_id, head_total, cross_levels)
            made.append((crossed, slot))
        if 0 <= slot - 1 < dev_total:
            gathered[slot - 1] = gather_levels(
                crossed[slot - 1], head_id, head_total, chip_levels
            ).reshape(row_count, head_total * local_width)
            made.append((gathered, slot - 1))
        step = slot - 2
        if 0 <= step < dev_total:
            normed_now = layer_norm(gathered[step], gain_one).astype(jnp.bfloat16)
            if step == 0:
                queries = jnp.dot(
                    normed_now, query_weight, preferred_element_type=jnp.float32
                ).astype(jnp.bfloat16)
                query_heads = queries.reshape(local_bricks, brick_rows, head_count, HEAD_DIM)
            key_block = jnp.dot(
                normed_now, key_weight, preferred_element_type=jnp.float32
            ).astype(jnp.bfloat16)
            value_block = jnp.dot(
                normed_now, value_weight, preferred_element_type=jnp.float32
            ).astype(jnp.bfloat16)
            source = (brick_dev - step) % dev_total
            key_ids = source * local_bricks + jnp.arange(local_bricks, dtype=jnp.int32)
            linked = jnp.take(linked_rows, key_ids, axis=1) > 0
            state = absorb_block(
                state, query_heads, key_block, value_block, linked, head_count, brick_rows
            )
        if slot < dev_total + 1:
            packed = lax.optimization_barrier((state, [table[key] for table, key in made]))
            state = packed[0]
            for (table, key), value in zip(made, packed[1]):
                table[key] = value
    row_max, row_mass, weighted = state
    attended = (weighted / jnp.transpose(row_mass, (0, 2, 1))[:, :, :, None]).astype(jnp.bfloat16)
    attended = attended.reshape(row_count, local_width)
    chunk_count = 2 if row_count % 16 == 0 else 1
    chunk_rows = row_count // chunk_count
    outputs = []
    for chunk in range(chunk_count):
        rows = slice(chunk * chunk_rows, (chunk + 1) * chunk_rows)
        partial_out = jnp.dot(attended[rows], out_weight, preferred_element_type=jnp.float32)
        out_sum = scatter_heads(partial_out, head_id, head_total)
        stream_two = (stream[rows].astype(jnp.float32) + out_sum).astype(jnp.bfloat16)
        stream_two_full = gather_heads(stream_two, head_id, head_total)
        normed_two = layer_norm(stream_two_full, gain_two).astype(jnp.bfloat16)
        hidden = jax.nn.gelu(
            jnp.dot(normed_two, up_weight, preferred_element_type=jnp.float32), approximate=True
        ).astype(jnp.bfloat16)
        lowered = jnp.dot(hidden, down_weight, preferred_element_type=jnp.float32)
        mixed = scatter_heads(lowered, head_id, head_total)
        outputs.append((stream_two.astype(jnp.float32) + mixed).astype(jnp.bfloat16))
    return jnp.concatenate(outputs, axis=0)

def solution(mesh):
    return jax.shard_map(
        shards,
        mesh=mesh,
        in_specs=(
            P(("groups", "bricks"), "heads"),
            P("groups"),
            P("groups", None),
            P(None, "heads"),
            P("heads"),
            P(),
            P(None, "heads"),
            P(None, "heads"),
            P(None, "heads"),
            P("heads", None),
            P(),
            P(None, "heads"),
            P("heads", None),
        ),
        out_specs=P(("groups", "bricks"), "heads"),
        check_vma=False,
    )
```

```python
import jax
import jax.numpy as jnp
from jax import lax
from jax.sharding import PartitionSpec as P

EDGE = 8
HEAD_DIM = 64


epsilon = 1e-05


def extended_2(value, sides, width):
    for axis, dim in sides:
        size, length = (lax.axis_size(axis), value.shape[dim])
        up = [(i, (i + 1) % size) for i in range(size - 1)]
        down = [(j, i) for i, j in up]
        last = lax.slice_in_dim(value, length - width, length, axis=dim)
        first = lax.slice_in_dim(value, 0, width, axis=dim)
        before = lax.ppermute(last, axis, up)
        after = lax.ppermute(first, axis, down)
        value = jnp.concatenate([before, value, after], axis=dim)
    return value


def layer_norm(inputs, gain_vec):
    values = inputs.astype(jnp.float32)
    center = values - jnp.mean(values, axis=-1, keepdims=True)
    spread = jnp.mean(center * center, axis=-1, keepdims=True)
    return center * lax.rsqrt(spread + epsilon) * gain_vec.astype(jnp.float32)


def depthwise(brick_vals, lower_face, upper_face, conv_weight, conv_bias):
    brick_count = brick_vals.shape[0]
    edge_len = brick_vals.shape[1]
    channels = brick_vals.shape[3]
    layers = jnp.concatenate([lower_face[:, None], brick_vals, upper_face[:, None]], axis=1)
    layers = layers.reshape(brick_count, edge_len + 2, edge_len, edge_len, channels)
    padded = jnp.pad(layers, ((0, 0), (0, 0), (1, 1), (1, 1), (0, 0)))
    weights = conv_weight.astype(jnp.float32)
    summed = jnp.zeros((brick_count, edge_len, edge_len, edge_len, channels), jnp.float32)
    for step_x in range(3):
        for step_y in range(3):
            for step_z in range(3):
                window = padded[
                    :,
                    step_x : step_x + edge_len,
                    step_y : step_y + edge_len,
                    step_z : step_z + edge_len,
                ]
                summed = summed + weights[step_x * 9 + step_y * 3 + step_z] * window
    return summed.reshape(brick_count * edge_len**3, channels) + conv_bias.astype(jnp.float32)


def level_count(total):
    levels = total.bit_length() - 1
    assert 1 << levels == total
    return levels


def scatter_heads(partial, head_id, head_total):
    levels = level_count(head_total)
    rows = partial.shape[0]
    width = partial.shape[1] // head_total
    current = partial.reshape((rows,) + (2,) * levels + (width,))
    for level in range(levels):
        bit = 1 << level
        axis = levels - level
        mine = (head_id >> level) & 1
        keep = lax.dynamic_index_in_dim(current, mine, axis, keepdims=False)
        give = lax.dynamic_index_in_dim(current, 1 - mine, axis, keepdims=False)
        got = lax.ppermute(
            give.astype(jnp.bfloat16), "heads", [(i, i ^ bit) for i in range(head_total)]
        )
        current = keep + got.astype(jnp.float32)
    return current.reshape(rows, width)


def gather_heads(piece, head_id, head_total):
    levels = level_count(head_total)
    rows, width = piece.shape
    current = piece
    for level in reversed(range(levels)):
        bit = 1 << level
        mine = (head_id >> level) & 1
        got = lax.ppermute(current, "heads", [(i, i ^ bit) for i in range(head_total)])
        low = jnp.where(mine == 0, current, got)
        high = jnp.where(mine == 0, got, current)
        current = jnp.stack([low, high], axis=current.ndim - 1)
    return current.reshape(rows, head_total * width)


def gather_levels(current, head_id, head_total, level_list, by_rows=False, first_axis=0):
    for done, level in enumerate(level_list, first_axis):
        bit = 1 << level
        mine = (head_id >> level) & 1
        got = lax.ppermute(current, "heads", [(i, i ^ bit) for i in range(head_total)])
        low = jnp.where(mine == 0, current, got)
        high = jnp.where(mine == 0, got, current)
        current = jnp.stack([low, high], axis=done if by_rows else current.ndim - 1)
    return current


def absorb_block(state, query_heads, key_block, value_block, linked, head_count, brick_rows):
    row_max, row_mass, weighted = state
    key_rows = key_block.reshape(-1, head_count, HEAD_DIM)
    value_rows = value_block.reshape(-1, head_count, HEAD_DIM)
    scores = (
        jnp.einsum("bqhd,khd->bhqk", query_heads, key_rows, preferred_element_type=jnp.float32)
        * HEAD_DIM ** (-0.5)
    )
    keep = jnp.repeat(linked, brick_rows, axis=1, total_repeat_length=key_rows.shape[0])
    scores = jnp.where(keep[:, None, None, :], scores, -1e30)
    max_new = jnp.maximum(row_max, jnp.max(scores, axis=-1))
    factor = jnp.exp(row_max - max_new)
    weights = jnp.exp(scores - max_new[..., None])
    mass_new = row_mass * factor + jnp.sum(weights, axis=-1)
    sum_new = weighted * jnp.transpose(factor, (0, 2, 1))[..., None] + jnp.einsum(
        "bhqk,khd->bqhd", weights.astype(jnp.bfloat16), value_rows,
        preferred_element_type=jnp.float32,
    )
    return max_new, mass_new, sum_new


def shards(
    voxel_feats,
    face_open,
    pattern,
    conv_weight,
    conv_bias,
    gain_one,
    query_weight,
    key_weight,
    value_weight,
    out_weight,
    gain_two,
    up_weight,
    down_weight,
):
    head_total = lax.axis_size("heads")
    head_id = lax.axis_index("heads")
    row_count = voxel_feats.shape[0]
    local_width = voxel_feats.shape[1]
    face_rows = EDGE * EDGE
    brick_rows = EDGE * face_rows
    local_bricks = row_count // brick_rows
    brick_total = pattern.shape[0]
    first_brick = lax.axis_index("bricks") * local_bricks
    extended = extended_2(voxel_feats, (("bricks", 0),), face_rows)
    brick_vals = extended[face_rows : face_rows + row_count].astype(jnp.float32)
    brick_vals = brick_vals.reshape(local_bricks, EDGE, face_rows, local_width)
    lower_face = jnp.concatenate(
        [extended[:face_rows].astype(jnp.float32)[None], brick_vals[:-1, EDGE - 1]], axis=0
    )
    upper_face = jnp.concatenate(
        [brick_vals[1:, 0], extended[face_rows + row_count :].astype(jnp.float32)[None]], axis=0
    )
    brick_ids = first_brick + jnp.arange(local_bricks, dtype=jnp.int32)
    lower_open = jnp.where(brick_ids >= 1, jnp.take(face_open, brick_ids), 0)
    upper_open = jnp.where(
        brick_ids + 1 < brick_total,
        jnp.take(face_open, jnp.minimum(brick_ids + 1, brick_total - 1)),
        0,
    )
    lower_face = lower_face * lower_open.astype(jnp.float32)[:, None, None]
    upper_face = upper_face * upper_open.astype(jnp.float32)[:, None, None]
    conv_out = depthwise(brick_vals, lower_face, upper_face, conv_weight, conv_bias)
    stream = (voxel_feats.astype(jnp.float32) + conv_out).astype(jnp.bfloat16)
    head_count = local_width // HEAD_DIM
    brick_dev = lax.axis_index("bricks")
    dev_total = lax.axis_size("bricks")
    ring = [(i, (i + 1) % dev_total) for i in range(dev_total)]
    linked_rows = lax.dynamic_slice_in_dim(pattern, first_brick, local_bricks, 0)
    state = (
        jnp.full((local_bricks, head_count, brick_rows), -1e30, jnp.float32),
        jnp.zeros((local_bricks, head_count, brick_rows), jnp.float32),
        jnp.zeros((local_bricks, brick_rows, head_count, HEAD_DIM), jnp.float32),
    )
    levels = level_count(head_total)
    cross_levels = list(reversed(range(1, levels)))
    chip_levels = list(range(min(levels, 1)))
    ringed = {0: stream}
    crossed = {}
    gathered = {}
    query_heads = None
    weights = {"out": out_weight}
    for slot in range(dev_total + 2):
        made = []
        if slot == dev_total - 1:
            made.append((weights, "out"))
        if slot == dev_total:
            weights["out"] = gather_levels(
                weights["out"], head_id, head_total, cross_levels, True
            )
        if slot == dev_total + 1:
            made.append((weights, "out"))
        if 1 <= slot + 1 < dev_total:
            ringed[slot + 1] = lax.ppermute(ringed[slot], "bricks", ring)
            made.append((ringed, slot + 1))
        if slot < dev_total:
            crossed[slot] = gather_levels(ringed[slot], head_id, head_total, cross_levels)
            made.append((crossed, slot))
        if 0 <= slot - 1 < dev_total:
            gathered[slot - 1] = gather_levels(
                crossed[slot - 1], head_id, head_total, chip_levels
            ).reshape(row_count, head_total * local_width)
            made.append((gathered, slot - 1))
        step = slot - 2
        if 0 <= step < dev_total:
            normed_now = layer_norm(gathered[step], gain_one).astype(jnp.bfloat16)
            if step == 0:
                queries = jnp.dot(
                    normed_now, query_weight, preferred_element_type=jnp.float32
                ).astype(jnp.bfloat16)
                query_heads = queries.reshape(local_bricks, brick_rows, head_count, HEAD_DIM)
            key_block = jnp.dot(
                normed_now, key_weight, preferred_element_type=jnp.float32
            ).astype(jnp.bfloat16)
            value_block = jnp.dot(
                normed_now, value_weight, preferred_element_type=jnp.float32
            ).astype(jnp.bfloat16)
            source = (brick_dev - step) % dev_total
            key_ids = source * local_bricks + jnp.arange(local_bricks, dtype=jnp.int32)
            linked = jnp.take(linked_rows, key_ids, axis=1) > 0
            state = absorb_block(
                state, query_heads, key_block, value_block, linked, head_count, brick_rows
            )
        if made:
            packed = lax.optimization_barrier((state, [table[key] for table, key in made]))
            state = packed[0]
            for (table, key), value in zip(made, packed[1]):
                table[key] = value
    out_weight_full = gather_levels(
        weights["out"], head_id, head_total, chip_levels, True, len(cross_levels)
    ).reshape(head_total * out_weight.shape[0], out_weight.shape[1])
    row_max, row_mass, weighted = state
    attended = (weighted / jnp.transpose(row_mass, (0, 2, 1))[:, :, :, None]).astype(jnp.bfloat16)
    attended = attended.reshape(row_count, local_width)
    chunk_count = 2 if row_count % 16 == 0 else 1
    chunk_rows = row_count // chunk_count
    outputs = []
    for chunk in range(chunk_count):
        rows = slice(chunk * chunk_rows, (chunk + 1) * chunk_rows)
        attended_full = gather_heads(attended[rows], head_id, head_total)
        projected = jnp.dot(attended_full, out_weight_full, preferred_element_type=jnp.float32)
        stream_two_full = (gathered[0][rows].astype(jnp.float32) + projected).astype(jnp.bfloat16)
        stream_two = lax.dynamic_slice_in_dim(
            stream_two_full, head_id * local_width, local_width, 1
        )
        normed_two = layer_norm(stream_two_full, gain_two).astype(jnp.bfloat16)
        hidden = jax.nn.gelu(
            jnp.dot(normed_two, up_weight, preferred_element_type=jnp.float32), approximate=True
        ).astype(jnp.bfloat16)
        lowered = jnp.dot(hidden, down_weight, preferred_element_type=jnp.float32)
        mixed = scatter_heads(lowered, head_id, head_total)
        outputs.append((stream_two.astype(jnp.float32) + mixed).astype(jnp.bfloat16))
    return jnp.concatenate(outputs, axis=0)

def solution(mesh):
    return jax.shard_map(
        shards,
        mesh=mesh,
        in_specs=(
            P(("groups", "bricks"), "heads"),
            P("groups"),
            P("groups", None),
            P(None, "heads"),
            P("heads"),
            P(),
            P(None, "heads"),
            P(None, "heads"),
            P(None, "heads"),
            P("heads", None),
            P(),
            P(None, "heads"),
            P("heads", None),
        ),
        out_specs=P(("groups", "bricks"), "heads"),
        check_vma=False,
    )
```

```python
import jax
import jax.numpy as jnp
from jax import lax
from jax.sharding import PartitionSpec as P

EDGE = 8
HEAD_DIM = 64


epsilon = 1e-05


def extended_2(value, sides, width):
    for axis, dim in sides:
        size, length = (lax.axis_size(axis), value.shape[dim])
        up = [(i, (i + 1) % size) for i in range(size - 1)]
        down = [(j, i) for i, j in up]
        last = lax.slice_in_dim(value, length - width, length, axis=dim)
        first = lax.slice_in_dim(value, 0, width, axis=dim)
        before = lax.ppermute(last, axis, up)
        after = lax.ppermute(first, axis, down)
        value = jnp.concatenate([before, value, after], axis=dim)
    return value


def layer_norm(inputs, gain_vec):
    values = inputs.astype(jnp.float32)
    center = values - jnp.mean(values, axis=-1, keepdims=True)
    spread = jnp.mean(center * center, axis=-1, keepdims=True)
    return center * lax.rsqrt(spread + epsilon) * gain_vec.astype(jnp.float32)


def depthwise(brick_vals, lower_face, upper_face, conv_weight, conv_bias):
    brick_count = brick_vals.shape[0]
    edge_len = brick_vals.shape[1]
    channels = brick_vals.shape[3]
    layers = jnp.concatenate([lower_face[:, None], brick_vals, upper_face[:, None]], axis=1)
    layers = layers.reshape(brick_count, edge_len + 2, edge_len, edge_len, channels)
    padded = jnp.pad(layers, ((0, 0), (0, 0), (1, 1), (1, 1), (0, 0)))
    weights = conv_weight.astype(jnp.float32)
    summed = jnp.zeros((brick_count, edge_len, edge_len, edge_len, channels), jnp.float32)
    for step_x in range(3):
        for step_y in range(3):
            for step_z in range(3):
                window = padded[
                    :,
                    step_x : step_x + edge_len,
                    step_y : step_y + edge_len,
                    step_z : step_z + edge_len,
                ]
                summed = summed + weights[step_x * 9 + step_y * 3 + step_z] * window
    return summed.reshape(brick_count * edge_len**3, channels) + conv_bias.astype(jnp.float32)


def level_count(total):
    levels = total.bit_length() - 1
    assert 1 << levels == total
    return levels


def scatter_heads(partial, head_id, head_total):
    levels = level_count(head_total)
    rows = partial.shape[0]
    width = partial.shape[1] // head_total
    current = partial.reshape((rows,) + (2,) * levels + (width,))
    for level in range(levels):
        bit = 1 << level
        axis = levels - level
        mine = (head_id >> level) & 1
        keep = lax.dynamic_index_in_dim(current, mine, axis, keepdims=False)
        give = lax.dynamic_index_in_dim(current, 1 - mine, axis, keepdims=False)
        got = lax.ppermute(
            give.astype(jnp.bfloat16), "heads", [(i, i ^ bit) for i in range(head_total)]
        )
        current = keep + got.astype(jnp.float32)
    return current.reshape(rows, width)


def gather_heads(piece, head_id, head_total):
    order = list(reversed(range(level_count(head_total))))
    return join_parts(gather_parts([piece], head_id, head_total, order), order)


def gather_levels(current, head_id, head_total, level_list, by_rows=False, first_axis=0):
    for done, level in enumerate(level_list, first_axis):
        bit = 1 << level
        mine = (head_id >> level) & 1
        got = lax.ppermute(current, "heads", [(i, i ^ bit) for i in range(head_total)])
        low = jnp.where(mine == 0, current, got)
        high = jnp.where(mine == 0, got, current)
        current = jnp.stack([low, high], axis=done if by_rows else current.ndim - 1)
    return current


def gather_parts(parts, head_id, head_total, level_list):
    width = parts[0].shape[-1]
    for level in level_list:
        bit = 1 << level
        mine = (head_id >> level) & 1
        sent = parts[0] if len(parts) == 1 else jnp.concatenate(parts, axis=-1)
        got = lax.ppermute(sent, "heads", [(i, i ^ bit) for i in range(head_total)])
        got_parts = [got[..., k * width : (k + 1) * width] for k in range(len(parts))]
        low = [jnp.where(mine == 0, a, b) for a, b in zip(parts, got_parts)]
        high = [jnp.where(mine == 0, b, a) for a, b in zip(parts, got_parts)]
        parts = low + high
    return parts


def join_parts(parts, level_order):
    ordered = []
    for head in range(len(parts)):
        slot = sum(((head >> level) & 1) << t for t, level in enumerate(level_order))
        ordered.append(parts[slot])
    return ordered[0] if len(ordered) == 1 else jnp.concatenate(ordered, axis=-1)


def absorb_block(state, query_heads, key_block, value_block, linked, head_count, brick_rows):
    row_max, row_mass, weighted = state
    key_rows = key_block.reshape(-1, head_count, HEAD_DIM)
    value_rows = value_block.reshape(-1, head_count, HEAD_DIM)
    scores = (
        jnp.einsum("bqhd,khd->bhqk", query_heads, key_rows, preferred_element_type=jnp.float32)
        * HEAD_DIM ** (-0.5)
    )
    keep = jnp.repeat(linked, brick_rows, axis=1, total_repeat_length=key_rows.shape[0])
    scores = jnp.where(keep[:, None, None, :], scores, -1e30)
    max_new = jnp.maximum(row_max, jnp.max(scores, axis=-1))
    factor = jnp.exp(row_max - max_new)
    weights = jnp.exp(scores - max_new[..., None])
    mass_new = row_mass * factor + jnp.sum(weights, axis=-1)
    sum_new = weighted * jnp.transpose(factor, (0, 2, 1))[..., None] + jnp.einsum(
        "bhqk,khd->bqhd", weights.astype(jnp.bfloat16), value_rows,
        preferred_element_type=jnp.float32,
    )
    return max_new, mass_new, sum_new


def shards(
    voxel_feats,
    face_open,
    pattern,
    conv_weight,
    conv_bias,
    gain_one,
    query_weight,
    key_weight,
    value_weight,
    out_weight,
    gain_two,
    up_weight,
    down_weight,
):
    head_total = lax.axis_size("heads")
    head_id = lax.axis_index("heads")
    row_count = voxel_feats.shape[0]
    local_width = voxel_feats.shape[1]
    face_rows = EDGE * EDGE
    brick_rows = EDGE * face_rows
    local_bricks = row_count // brick_rows
    brick_total = pattern.shape[0]
    first_brick = lax.axis_index("bricks") * local_bricks
    extended = extended_2(voxel_feats, (("bricks", 0),), face_rows)
    brick_vals = extended[face_rows : face_rows + row_count].astype(jnp.float32)
    brick_vals = brick_vals.reshape(local_bricks, EDGE, face_rows, local_width)
    lower_face = jnp.concatenate(
        [extended[:face_rows].astype(jnp.float32)[None], brick_vals[:-1, EDGE - 1]], axis=0
    )
    upper_face = jnp.concatenate(
        [brick_vals[1:, 0], extended[face_rows + row_count :].astype(jnp.float32)[None]], axis=0
    )
    brick_ids = first_brick + jnp.arange(local_bricks, dtype=jnp.int32)
    lower_open = jnp.where(brick_ids >= 1, jnp.take(face_open, brick_ids), 0)
    upper_open = jnp.where(
        brick_ids + 1 < brick_total,
        jnp.take(face_open, jnp.minimum(brick_ids + 1, brick_total - 1)),
        0,
    )
    lower_face = lower_face * lower_open.astype(jnp.float32)[:, None, None]
    upper_face = upper_face * upper_open.astype(jnp.float32)[:, None, None]
    conv_out = depthwise(brick_vals, lower_face, upper_face, conv_weight, conv_bias)
    stream = (voxel_feats.astype(jnp.float32) + conv_out).astype(jnp.bfloat16)
    head_count = local_width // HEAD_DIM
    brick_dev = lax.axis_index("bricks")
    dev_total = lax.axis_size("bricks")
    ring = [(i, (i + 1) % dev_total) for i in range(dev_total)]
    linked_rows = lax.dynamic_slice_in_dim(pattern, first_brick, local_bricks, 0)
    state = (
        jnp.full((local_bricks, head_count, brick_rows), -1e30, jnp.float32),
        jnp.zeros((local_bricks, head_count, brick_rows), jnp.float32),
        jnp.zeros((local_bricks, brick_rows, head_count, HEAD_DIM), jnp.float32),
    )
    levels = level_count(head_total)
    cross_levels = list(reversed(range(1, levels)))
    chip_levels = list(range(min(levels, 1)))
    ringed = {0: stream}
    crossed = {}
    gathered = {}
    query_heads = None
    weights = {"out": out_weight}
    for slot in range(dev_total + 2):
        made = []
        if slot == dev_total - 1:
            made.append((weights, "out"))
        if slot == dev_total:
            weights["out"] = gather_levels(
                weights["out"], head_id, head_total, cross_levels, True
            )
        if slot == dev_total + 1:
            made.append((weights, "out"))
        if 1 <= slot + 1 < dev_total:
            ringed[slot + 1] = lax.ppermute(ringed[slot], "bricks", ring)
            made.append((ringed, slot + 1))
        if slot < dev_total:
            crossed[slot] = gather_parts([ringed[slot]], head_id, head_total, cross_levels)
            made.append((crossed, slot))
        if 0 <= slot - 1 < dev_total:
            gathered[slot - 1] = join_parts(
                gather_parts(crossed[slot - 1], head_id, head_total, chip_levels),
                cross_levels + chip_levels,
            )
            made.append((gathered, slot - 1))
        step = slot - 2
        if 0 <= step < dev_total:
            normed_now = layer_norm(gathered[step], gain_one).astype(jnp.bfloat16)
            if step == 0:
                queries = jnp.dot(
                    normed_now, query_weight, preferred_element_type=jnp.float32
                ).astype(jnp.bfloat16)
                query_heads = queries.reshape(local_bricks, brick_rows, head_count, HEAD_DIM)
            key_block = jnp.dot(
                normed_now, key_weight, preferred_element_type=jnp.float32
            ).astype(jnp.bfloat16)
            value_block = jnp.dot(
                normed_now, value_weight, preferred_element_type=jnp.float32
            ).astype(jnp.bfloat16)
            source = (brick_dev - step) % dev_total
            key_ids = source * local_bricks + jnp.arange(local_bricks, dtype=jnp.int32)
            linked = jnp.take(linked_rows, key_ids, axis=1) > 0
            state = absorb_block(
                state, query_heads, key_block, value_block, linked, head_count, brick_rows
            )
        if made:
            packed = lax.optimization_barrier((state, [table[key] for table, key in made]))
            state = packed[0]
            for (table, key), value in zip(made, packed[1]):
                table[key] = value
    out_weight_full = gather_levels(
        weights["out"], head_id, head_total, chip_levels, True, len(cross_levels)
    ).reshape(head_total * out_weight.shape[0], out_weight.shape[1])
    row_max, row_mass, weighted = state
    attended = (weighted / jnp.transpose(row_mass, (0, 2, 1))[:, :, :, None]).astype(jnp.bfloat16)
    attended = attended.reshape(row_count, local_width)
    chunk_count = 2 if row_count % 16 == 0 else 1
    chunk_rows = row_count // chunk_count
    outputs = []
    for chunk in range(chunk_count):
        rows = slice(chunk * chunk_rows, (chunk + 1) * chunk_rows)
        attended_full = gather_heads(attended[rows], head_id, head_total)
        projected = jnp.dot(attended_full, out_weight_full, preferred_element_type=jnp.float32)
        stream_two_full = (gathered[0][rows].astype(jnp.float32) + projected).astype(jnp.bfloat16)
        stream_two = lax.dynamic_slice_in_dim(
            stream_two_full, head_id * local_width, local_width, 1
        )
        normed_two = layer_norm(stream_two_full, gain_two).astype(jnp.bfloat16)
        hidden = jax.nn.gelu(
            jnp.dot(normed_two, up_weight, preferred_element_type=jnp.float32), approximate=True
        ).astype(jnp.bfloat16)
        lowered = jnp.dot(hidden, down_weight, preferred_element_type=jnp.float32)
        mixed = scatter_heads(lowered, head_id, head_total)
        outputs.append((stream_two.astype(jnp.float32) + mixed).astype(jnp.bfloat16))
    return jnp.concatenate(outputs, axis=0)

def solution(mesh):
    return jax.shard_map(
        shards,
        mesh=mesh,
        in_specs=(
            P(("groups", "bricks"), "heads"),
            P("groups"),
            P("groups", None),
            P(None, "heads"),
            P("heads"),
            P(),
            P(None, "heads"),
            P(None, "heads"),
            P(None, "heads"),
            P("heads", None),
            P(),
            P(None, "heads"),
            P("heads", None),
        ),
        out_specs=P(("groups", "bricks"), "heads"),
        check_vma=False,
    )
```

```python
import jax
import jax.numpy as jnp
from jax import lax
from jax.sharding import PartitionSpec as P

EDGE = 8
HEAD_DIM = 64


epsilon = 1e-05


def extended_2(value, sides, width):
    for axis, dim in sides:
        size, length = (lax.axis_size(axis), value.shape[dim])
        up = [(i, (i + 1) % size) for i in range(size - 1)]
        down = [(j, i) for i, j in up]
        last = lax.slice_in_dim(value, length - width, length, axis=dim)
        first = lax.slice_in_dim(value, 0, width, axis=dim)
        before = lax.ppermute(last, axis, up)
        after = lax.ppermute(first, axis, down)
        value = jnp.concatenate([before, value, after], axis=dim)
    return value


def layer_norm(inputs, gain_vec):
    values = inputs.astype(jnp.float32)
    center = values - jnp.mean(values, axis=-1, keepdims=True)
    spread = jnp.mean(center * center, axis=-1, keepdims=True)
    return center * lax.rsqrt(spread + epsilon) * gain_vec.astype(jnp.float32)


def depthwise(brick_vals, lower_face, upper_face, conv_weight, conv_bias):
    brick_count = brick_vals.shape[0]
    edge_len = brick_vals.shape[1]
    channels = brick_vals.shape[3]
    layers = jnp.concatenate([lower_face[:, None], brick_vals, upper_face[:, None]], axis=1)
    layers = layers.reshape(brick_count, edge_len + 2, edge_len, edge_len, channels)
    padded = jnp.pad(layers, ((0, 0), (0, 0), (1, 1), (1, 1), (0, 0)))
    weights = conv_weight.astype(jnp.float32)
    summed = jnp.zeros((brick_count, edge_len, edge_len, edge_len, channels), jnp.float32)
    for step_x in range(3):
        for step_y in range(3):
            for step_z in range(3):
                window = padded[
                    :,
                    step_x : step_x + edge_len,
                    step_y : step_y + edge_len,
                    step_z : step_z + edge_len,
                ]
                summed = summed + weights[step_x * 9 + step_y * 3 + step_z] * window
    return summed.reshape(brick_count * edge_len**3, channels) + conv_bias.astype(jnp.float32)


def level_count(total):
    levels = total.bit_length() - 1
    assert 1 << levels == total
    return levels


def scatter_heads(partial, head_id, head_total):
    levels = level_count(head_total)
    rows = partial.shape[0]
    width = partial.shape[1] // head_total
    current = partial.reshape((rows,) + (2,) * levels + (width,))
    for level in range(levels):
        bit = 1 << level
        axis = levels - level
        mine = (head_id >> level) & 1
        keep = lax.dynamic_index_in_dim(current, mine, axis, keepdims=False)
        give = lax.dynamic_index_in_dim(current, 1 - mine, axis, keepdims=False)
        got = lax.ppermute(
            give.astype(jnp.bfloat16), "heads", [(i, i ^ bit) for i in range(head_total)]
        )
        current = keep + got.astype(jnp.float32)
    return current.reshape(rows, width)


def gather_heads(piece, head_id, head_total):
    order = list(reversed(range(level_count(head_total))))
    return join_parts(gather_parts([piece], head_id, head_total, order), order)


def gather_parts(parts, head_id, head_total, level_list):
    width = parts[0].shape[-1]
    for level in level_list:
        bit = 1 << level
        mine = (head_id >> level) & 1
        sent = parts[0] if len(parts) == 1 else jnp.concatenate(parts, axis=-1)
        got = lax.ppermute(sent, "heads", [(i, i ^ bit) for i in range(head_total)])
        got_parts = [got[..., k * width : (k + 1) * width] for k in range(len(parts))]
        low = [jnp.where(mine == 0, a, b) for a, b in zip(parts, got_parts)]
        high = [jnp.where(mine == 0, b, a) for a, b in zip(parts, got_parts)]
        parts = low + high
    return parts


def join_parts(parts, level_order):
    ordered = []
    for head in range(len(parts)):
        slot = sum(((head >> level) & 1) << t for t, level in enumerate(level_order))
        ordered.append(parts[slot])
    return ordered[0] if len(ordered) == 1 else jnp.concatenate(ordered, axis=-1)


def absorb_block(state, query_heads, key_block, value_block, linked, head_count, brick_rows):
    row_max, row_mass, weighted = state
    key_rows = key_block.reshape(-1, head_count, HEAD_DIM)
    value_rows = value_block.reshape(-1, head_count, HEAD_DIM)
    scores = (
        jnp.einsum("bqhd,khd->bhqk", query_heads, key_rows, preferred_element_type=jnp.float32)
        * HEAD_DIM ** (-0.5)
    )
    keep = jnp.repeat(linked, brick_rows, axis=1, total_repeat_length=key_rows.shape[0])
    scores = jnp.where(keep[:, None, None, :], scores, -1e30)
    max_new = jnp.maximum(row_max, jnp.max(scores, axis=-1))
    factor = jnp.exp(row_max - max_new)
    weights = jnp.exp(scores - max_new[..., None])
    mass_new = row_mass * factor + jnp.sum(weights, axis=-1)
    sum_new = weighted * jnp.transpose(factor, (0, 2, 1))[..., None] + jnp.einsum(
        "bhqk,khd->bqhd", weights.astype(jnp.bfloat16), value_rows,
        preferred_element_type=jnp.float32,
    )
    return max_new, mass_new, sum_new


def shards(
    voxel_feats,
    face_open,
    pattern,
    conv_weight,
    conv_bias,
    gain_one,
    query_weight,
    key_weight,
    value_weight,
    out_weight,
    gain_two,
    up_weight,
    down_weight,
):
    row_count = voxel_feats.shape[0]
    local_width = voxel_feats.shape[1]
    face_rows = EDGE * EDGE
    brick_rows = EDGE * face_rows
    local_bricks = row_count // brick_rows
    brick_total = pattern.shape[0]
    first_brick = lax.axis_index("bricks") * local_bricks
    extended = extended_2(voxel_feats, (("bricks", 0),), face_rows)
    brick_vals = extended[face_rows : face_rows + row_count].astype(jnp.float32)
    brick_vals = brick_vals.reshape(local_bricks, EDGE, face_rows, local_width)
    lower_face = jnp.concatenate(
        [extended[:face_rows].astype(jnp.float32)[None], brick_vals[:-1, EDGE - 1]], axis=0
    )
    upper_face = jnp.concatenate(
        [brick_vals[1:, 0], extended[face_rows + row_count :].astype(jnp.float32)[None]], axis=0
    )
    brick_ids = first_brick + jnp.arange(local_bricks, dtype=jnp.int32)
    lower_open = jnp.where(brick_ids >= 1, jnp.take(face_open, brick_ids), 0)
    upper_open = jnp.where(
        brick_ids + 1 < brick_total,
        jnp.take(face_open, jnp.minimum(brick_ids + 1, brick_total - 1)),
        0,
    )
    lower_face = lower_face * lower_open.astype(jnp.float32)[:, None, None]
    upper_face = upper_face * upper_open.astype(jnp.float32)[:, None, None]
    conv_out = depthwise(brick_vals, lower_face, upper_face, conv_weight, conv_bias)
    stream = (voxel_feats.astype(jnp.float32) + conv_out).astype(jnp.bfloat16)
    head_total = lax.axis_size("heads")
    head_id = lax.axis_index("heads")
    head_count = local_width // HEAD_DIM
    brick_dev = lax.axis_index("bricks")
    dev_total = lax.axis_size("bricks")
    ring = [(i, (i + 1) % dev_total) for i in range(dev_total)]
    linked_rows = lax.dynamic_slice_in_dim(pattern, first_brick, local_bricks, 0)
    state = (
        jnp.full((local_bricks, head_count, brick_rows), -1e30, jnp.float32),
        jnp.zeros((local_bricks, head_count, brick_rows), jnp.float32),
        jnp.zeros((local_bricks, brick_rows, head_count, HEAD_DIM), jnp.float32),
    )
    levels = level_count(head_total)
    cross_levels = list(reversed(range(1, levels)))
    chip_levels = list(range(min(levels, 1)))
    ringed = {0: stream}
    crossed = {}
    gathered = {}
    query_heads = None
    for slot in range(dev_total + 2):
        made = []
        if 1 <= slot + 1 < dev_total:
            ringed[slot + 1] = lax.ppermute(ringed[slot], "bricks", ring)
            made.append((ringed, slot + 1))
        if slot < dev_total:
            crossed[slot] = gather_parts([ringed[slot]], head_id, head_total, cross_levels)
            made.append((crossed, slot))
        if 0 <= slot - 1 < dev_total:
            gathered[slot - 1] = join_parts(
                gather_parts(crossed[slot - 1], head_id, head_total, chip_levels),
                cross_levels + chip_levels,
            )
            made.append((gathered, slot - 1))
        step = slot - 2
        if 0 <= step < dev_total:
            normed_now = layer_norm(gathered[step], gain_one).astype(jnp.bfloat16)
            if step == 0:
                queries = jnp.dot(
                    normed_now, query_weight, preferred_element_type=jnp.float32
                ).astype(jnp.bfloat16)
                query_heads = queries.reshape(local_bricks, brick_rows, head_count, HEAD_DIM)
            key_block = jnp.dot(
                normed_now, key_weight, preferred_element_type=jnp.float32
            ).astype(jnp.bfloat16)
            value_block = jnp.dot(
                normed_now, value_weight, preferred_element_type=jnp.float32
            ).astype(jnp.bfloat16)
            source = (brick_dev - step) % dev_total
            key_ids = source * local_bricks + jnp.arange(local_bricks, dtype=jnp.int32)
            linked = jnp.take(linked_rows, key_ids, axis=1) > 0
            state = absorb_block(
                state, query_heads, key_block, value_block, linked, head_count, brick_rows
            )
        if slot < dev_total + 1:
            packed = lax.optimization_barrier((state, [table[key] for table, key in made]))
            state = packed[0]
            for (table, key), value in zip(made, packed[1]):
                table[key] = value
    row_max, row_mass, weighted = state
    attended = (weighted / jnp.transpose(row_mass, (0, 2, 1))[:, :, :, None]).astype(jnp.bfloat16)
    attended = attended.reshape(row_count, local_width)
    chunk_count = 2 if row_count % 16 == 0 else 1
    chunk_rows = row_count // chunk_count
    outputs = []
    for chunk in range(chunk_count):
        rows = slice(chunk * chunk_rows, (chunk + 1) * chunk_rows)
        partial_out = jnp.dot(attended[rows], out_weight, preferred_element_type=jnp.float32)
        out_sum = scatter_heads(partial_out, head_id, head_total)
        stream_two = (stream[rows].astype(jnp.float32) + out_sum).astype(jnp.bfloat16)
        stream_two_full = gather_heads(stream_two, head_id, head_total)
        normed_two = layer_norm(stream_two_full, gain_two).astype(jnp.bfloat16)
        hidden = jax.nn.gelu(
            jnp.dot(normed_two, up_weight, preferred_element_type=jnp.float32), approximate=True
        ).astype(jnp.bfloat16)
        lowered = jnp.dot(hidden, down_weight, preferred_element_type=jnp.float32)
        mixed = scatter_heads(lowered, head_id, head_total)
        outputs.append((stream_two.astype(jnp.float32) + mixed).astype(jnp.bfloat16))
    return jnp.concatenate(outputs, axis=0)

def solution(mesh):
    return jax.shard_map(
        shards,
        mesh=mesh,
        in_specs=(
            P(("groups", "bricks"), "heads"),
            P("groups"),
            P("groups", None),
            P(None, "heads"),
            P("heads"),
            P(),
            P(None, "heads"),
            P(None, "heads"),
            P(None, "heads"),
            P("heads", None),
            P(),
            P(None, "heads"),
            P("heads", None),
        ),
        out_specs=P(("groups", "bricks"), "heads"),
        check_vma=False,
    )
```

```python
import jax
import jax.numpy as jnp
from jax import lax
from jax.sharding import PartitionSpec as P

EDGE = 8
HEAD_DIM = 64


epsilon = 1e-05


def extended_2(value, sides, width):
    for axis, dim in sides:
        size, length = (lax.axis_size(axis), value.shape[dim])
        up = [(i, (i + 1) % size) for i in range(size - 1)]
        down = [(j, i) for i, j in up]
        last = lax.slice_in_dim(value, length - width, length, axis=dim)
        first = lax.slice_in_dim(value, 0, width, axis=dim)
        before = lax.ppermute(last, axis, up)
        after = lax.ppermute(first, axis, down)
        value = jnp.concatenate([before, value, after], axis=dim)
    return value


def layer_norm(inputs, gain_vec):
    values = inputs.astype(jnp.float32)
    center = values - jnp.mean(values, axis=-1, keepdims=True)
    spread = jnp.mean(center * center, axis=-1, keepdims=True)
    return center * lax.rsqrt(spread + epsilon) * gain_vec.astype(jnp.float32)


def depthwise(brick_vals, lower_face, upper_face, conv_weight, conv_bias):
    brick_count = brick_vals.shape[0]
    edge_len = brick_vals.shape[1]
    channels = brick_vals.shape[3]
    layers = jnp.concatenate([lower_face[:, None], brick_vals, upper_face[:, None]], axis=1)
    layers = layers.reshape(brick_count, edge_len + 2, edge_len, edge_len, channels)
    padded = jnp.pad(layers, ((0, 0), (0, 0), (1, 1), (1, 1), (0, 0)))
    weights = conv_weight.astype(jnp.float32)
    summed = jnp.zeros((brick_count, edge_len, edge_len, edge_len, channels), jnp.float32)
    for step_x in range(3):
        for step_y in range(3):
            for step_z in range(3):
                window = padded[
                    :,
                    step_x : step_x + edge_len,
                    step_y : step_y + edge_len,
                    step_z : step_z + edge_len,
                ]
                summed = summed + weights[step_x * 9 + step_y * 3 + step_z] * window
    return summed.reshape(brick_count * edge_len**3, channels) + conv_bias.astype(jnp.float32)


def level_count(total):
    levels = total.bit_length() - 1
    assert 1 << levels == total
    return levels


def scatter_heads(partial, head_id, head_total):
    levels = level_count(head_total)
    rows = partial.shape[0]
    width = partial.shape[1] // head_total
    current = partial.reshape((rows,) + (2,) * levels + (width,))
    for level in range(levels):
        bit = 1 << level
        axis = levels - level
        mine = (head_id >> level) & 1
        keep = lax.dynamic_index_in_dim(current, mine, axis, keepdims=False)
        give = lax.dynamic_index_in_dim(current, 1 - mine, axis, keepdims=False)
        got = lax.ppermute(
            give.astype(jnp.bfloat16), "heads", [(i, i ^ bit) for i in range(head_total)]
        )
        current = keep + got.astype(jnp.float32)
    return current.reshape(rows, width)


def gather_heads(piece, head_id, head_total):
    levels = level_count(head_total)
    rows, width = piece.shape
    current = piece
    for level in reversed(range(levels)):
        bit = 1 << level
        mine = (head_id >> level) & 1
        got = lax.ppermute(current, "heads", [(i, i ^ bit) for i in range(head_total)])
        low = jnp.where(mine == 0, current, got)
        high = jnp.where(mine == 0, got, current)
        current = jnp.stack([low, high], axis=current.ndim - 1)
    return current.reshape(rows, head_total * width)


def gather_levels(current, head_id, head_total, level_list):
    for level in level_list:
        bit = 1 << level
        mine = (head_id >> level) & 1
        got = lax.ppermute(current, "heads", [(i, i ^ bit) for i in range(head_total)])
        low = jnp.where(mine == 0, current, got)
        high = jnp.where(mine == 0, got, current)
        current = jnp.stack([low, high], axis=current.ndim - 1)
    return current


def reduce_all_heads(partial, head_id, head_total):
    levels = level_count(head_total)
    rows, cols = partial.shape
    halves = partial.reshape(rows, 2, cols // 2)
    mine = head_id & 1
    keep = lax.dynamic_index_in_dim(halves, mine, 1, keepdims=False)
    give = lax.dynamic_index_in_dim(halves, 1 - mine, 1, keepdims=False)
    got = lax.ppermute(give.astype(jnp.bfloat16), "heads", [(i, i ^ 1) for i in range(head_total)])
    current = keep + got.astype(jnp.float32)
    for level in range(1, levels):
        bit = 1 << level
        sent = current.astype(jnp.bfloat16)
        got = lax.ppermute(sent, "heads", [(i, i ^ bit) for i in range(head_total)])
        current = sent.astype(jnp.float32) + got.astype(jnp.float32)
    own = current.astype(jnp.bfloat16)
    other = lax.ppermute(own, "heads", [(i, i ^ 1) for i in range(head_total)])
    low = jnp.where(mine == 0, own, other)
    high = jnp.where(mine == 0, other, own)
    return jnp.concatenate([low, high], axis=1)


def absorb_block(state, query_heads, key_block, value_block, linked, head_count, brick_rows):
    row_max, row_mass, weighted = state
    key_rows = key_block.reshape(-1, head_count, HEAD_DIM)
    value_rows = value_block.reshape(-1, head_count, HEAD_DIM)
    scores = (
        jnp.einsum("bqhd,khd->bhqk", query_heads, key_rows, preferred_element_type=jnp.float32)
        * HEAD_DIM ** (-0.5)
    )
    keep = jnp.repeat(linked, brick_rows, axis=1, total_repeat_length=key_rows.shape[0])
    scores = jnp.where(keep[:, None, None, :], scores, -1e30)
    max_new = jnp.maximum(row_max, jnp.max(scores, axis=-1))
    factor = jnp.exp(row_max - max_new)
    weights = jnp.exp(scores - max_new[..., None])
    mass_new = row_mass * factor + jnp.sum(weights, axis=-1)
    sum_new = weighted * jnp.transpose(factor, (0, 2, 1))[..., None] + jnp.einsum(
        "bhqk,khd->bqhd", weights.astype(jnp.bfloat16), value_rows,
        preferred_element_type=jnp.float32,
    )
    return max_new, mass_new, sum_new


def shards(
    voxel_feats,
    face_open,
    pattern,
    conv_weight,
    conv_bias,
    gain_one,
    query_weight,
    key_weight,
    value_weight,
    out_weight,
    gain_two,
    up_weight,
    down_weight,
):
    row_count = voxel_feats.shape[0]
    local_width = voxel_feats.shape[1]
    face_rows = EDGE * EDGE
    brick_rows = EDGE * face_rows
    local_bricks = row_count // brick_rows
    brick_total = pattern.shape[0]
    first_brick = lax.axis_index("bricks") * local_bricks
    extended = extended_2(voxel_feats, (("bricks", 0),), face_rows)
    brick_vals = extended[face_rows : face_rows + row_count].astype(jnp.float32)
    brick_vals = brick_vals.reshape(local_bricks, EDGE, face_rows, local_width)
    lower_face = jnp.concatenate(
        [extended[:face_rows].astype(jnp.float32)[None], brick_vals[:-1, EDGE - 1]], axis=0
    )
    upper_face = jnp.concatenate(
        [brick_vals[1:, 0], extended[face_rows + row_count :].astype(jnp.float32)[None]], axis=0
    )
    brick_ids = first_brick + jnp.arange(local_bricks, dtype=jnp.int32)
    lower_open = jnp.where(brick_ids >= 1, jnp.take(face_open, brick_ids), 0)
    upper_open = jnp.where(
        brick_ids + 1 < brick_total,
        jnp.take(face_open, jnp.minimum(brick_ids + 1, brick_total - 1)),
        0,
    )
    lower_face = lower_face * lower_open.astype(jnp.float32)[:, None, None]
    upper_face = upper_face * upper_open.astype(jnp.float32)[:, None, None]
    conv_out = depthwise(brick_vals, lower_face, upper_face, conv_weight, conv_bias)
    stream = (voxel_feats.astype(jnp.float32) + conv_out).astype(jnp.bfloat16)
    head_total = lax.axis_size("heads")
    head_id = lax.axis_index("heads")
    head_count = local_width // HEAD_DIM
    brick_dev = lax.axis_index("bricks")
    dev_total = lax.axis_size("bricks")
    ring = [(i, (i + 1) % dev_total) for i in range(dev_total)]
    linked_rows = lax.dynamic_slice_in_dim(pattern, first_brick, local_bricks, 0)
    state = (
        jnp.full((local_bricks, head_count, brick_rows), -1e30, jnp.float32),
        jnp.zeros((local_bricks, head_count, brick_rows), jnp.float32),
        jnp.zeros((local_bricks, brick_rows, head_count, HEAD_DIM), jnp.float32),
    )
    levels = level_count(head_total)
    cross_levels = list(reversed(range(1, levels)))
    chip_levels = list(range(min(levels, 1)))
    ringed = {0: stream}
    crossed = {}
    gathered = {}
    query_heads = None
    for slot in range(dev_total + 2):
        made = []
        if 1 <= slot + 1 < dev_total:
            ringed[slot + 1] = lax.ppermute(ringed[slot], "bricks", ring)
            made.append((ringed, slot + 1))
        if slot < dev_total:
            crossed[slot] = gather_levels(ringed[slot], head_id, head_total, cross_levels)
            made.append((crossed, slot))
        if 0 <= slot - 1 < dev_total:
            gathered[slot - 1] = gather_levels(
                crossed[slot - 1], head_id, head_total, chip_levels
            ).reshape(row_count, head_total * local_width)
            made.append((gathered, slot - 1))
        step = slot - 2
        if 0 <= step < dev_total:
            normed_now = layer_norm(gathered[step], gain_one).astype(jnp.bfloat16)
            if step == 0:
                queries = jnp.dot(
                    normed_now, query_weight, preferred_element_type=jnp.float32
                ).astype(jnp.bfloat16)
                query_heads = queries.reshape(local_bricks, brick_rows, head_count, HEAD_DIM)
            key_block = jnp.dot(
                normed_now, key_weight, preferred_element_type=jnp.float32
            ).astype(jnp.bfloat16)
            value_block = jnp.dot(
                normed_now, value_weight, preferred_element_type=jnp.float32
            ).astype(jnp.bfloat16)
            source = (brick_dev - step) % dev_total
            key_ids = source * local_bricks + jnp.arange(local_bricks, dtype=jnp.int32)
            linked = jnp.take(linked_rows, key_ids, axis=1) > 0
            state = absorb_block(
                state, query_heads, key_block, value_block, linked, head_count, brick_rows
            )
        if slot < dev_total + 1:
            packed = lax.optimization_barrier((state, [table[key] for table, key in made]))
            state = packed[0]
            for (table, key), value in zip(made, packed[1]):
                table[key] = value
    row_max, row_mass, weighted = state
    attended = (weighted / jnp.transpose(row_mass, (0, 2, 1))[:, :, :, None]).astype(jnp.bfloat16)
    attended = attended.reshape(row_count, local_width)
    chunk_count = 2 if row_count % 16 == 0 else 1
    chunk_rows = row_count // chunk_count
    outputs = []
    for chunk in range(chunk_count):
        rows = slice(chunk * chunk_rows, (chunk + 1) * chunk_rows)
        partial_out = jnp.dot(attended[rows], out_weight, preferred_element_type=jnp.float32)
        own_cols = head_id * local_width
        partial_out = lax.dynamic_update_slice_in_dim(
            partial_out,
            lax.dynamic_slice_in_dim(partial_out, own_cols, local_width, 1)
            + stream[rows].astype(jnp.float32),
            own_cols,
            1,
        )
        stream_two_full = reduce_all_heads(partial_out, head_id, head_total)
        stream_two = lax.dynamic_slice_in_dim(stream_two_full, own_cols, local_width, 1)
        normed_two = layer_norm(stream_two_full, gain_two).astype(jnp.bfloat16)
        hidden = jax.nn.gelu(
            jnp.dot(normed_two, up_weight, preferred_element_type=jnp.float32), approximate=True
        ).astype(jnp.bfloat16)
        lowered = jnp.dot(hidden, down_weight, preferred_element_type=jnp.float32)
        mixed = scatter_heads(lowered, head_id, head_total)
        outputs.append((stream_two.astype(jnp.float32) + mixed).astype(jnp.bfloat16))
    return jnp.concatenate(outputs, axis=0)

def solution(mesh):
    return jax.shard_map(
        shards,
        mesh=mesh,
        in_specs=(
            P(("groups", "bricks"), "heads"),
            P("groups"),
            P("groups", None),
            P(None, "heads"),
            P("heads"),
            P(),
            P(None, "heads"),
            P(None, "heads"),
            P(None, "heads"),
            P("heads", None),
            P(),
            P(None, "heads"),
            P("heads", None),
        ),
        out_specs=P(("groups", "bricks"), "heads"),
        check_vma=False,
    )
```

```python
import jax
import jax.numpy as jnp
from jax import lax
from jax.sharding import PartitionSpec as P

EDGE = 8
HEAD_DIM = 64


epsilon = 1e-05


def extended_2(value, sides, width):
    for axis, dim in sides:
        size, length = (lax.axis_size(axis), value.shape[dim])
        up = [(i, (i + 1) % size) for i in range(size - 1)]
        down = [(j, i) for i, j in up]
        last = lax.slice_in_dim(value, length - width, length, axis=dim)
        first = lax.slice_in_dim(value, 0, width, axis=dim)
        before = lax.ppermute(last, axis, up)
        after = lax.ppermute(first, axis, down)
        value = jnp.concatenate([before, value, after], axis=dim)
    return value


def layer_norm(inputs, gain_vec):
    values = inputs.astype(jnp.float32)
    center = values - jnp.mean(values, axis=-1, keepdims=True)
    spread = jnp.mean(center * center, axis=-1, keepdims=True)
    return center * lax.rsqrt(spread + epsilon) * gain_vec.astype(jnp.float32)


def depthwise(brick_vals, lower_face, upper_face, conv_weight, conv_bias):
    brick_count = brick_vals.shape[0]
    edge_len = brick_vals.shape[1]
    channels = brick_vals.shape[3]
    layers = jnp.concatenate([lower_face[:, None], brick_vals, upper_face[:, None]], axis=1)
    layers = layers.reshape(brick_count, edge_len + 2, edge_len, edge_len, channels)
    padded = jnp.pad(layers, ((0, 0), (0, 0), (1, 1), (1, 1), (0, 0)))
    weights = conv_weight.astype(jnp.float32)
    summed = jnp.zeros((brick_count, edge_len, edge_len, edge_len, channels), jnp.float32)
    for step_x in range(3):
        for step_y in range(3):
            for step_z in range(3):
                window = padded[
                    :,
                    step_x : step_x + edge_len,
                    step_y : step_y + edge_len,
                    step_z : step_z + edge_len,
                ]
                summed = summed + weights[step_x * 9 + step_y * 3 + step_z] * window
    return summed.reshape(brick_count * edge_len**3, channels) + conv_bias.astype(jnp.float32)


def level_count(total):
    levels = total.bit_length() - 1
    assert 1 << levels == total
    return levels


def scatter_heads(partial, head_id, head_total):
    levels = level_count(head_total)
    rows = partial.shape[0]
    width = partial.shape[1] // head_total
    current = partial.reshape((rows,) + (2,) * levels + (width,))
    for level in range(levels):
        bit = 1 << level
        axis = levels - level
        mine = (head_id >> level) & 1
        keep = lax.dynamic_index_in_dim(current, mine, axis, keepdims=False)
        give = lax.dynamic_index_in_dim(current, 1 - mine, axis, keepdims=False)
        got = lax.ppermute(
            give.astype(jnp.bfloat16), "heads", [(i, i ^ bit) for i in range(head_total)]
        )
        current = keep + got.astype(jnp.float32)
    return current.reshape(rows, width)


def gather_heads(piece, head_id, head_total):
    levels = level_count(head_total)
    rows, width = piece.shape
    current = piece
    for level in reversed(range(levels)):
        bit = 1 << level
        mine = (head_id >> level) & 1
        got = lax.ppermute(current, "heads", [(i, i ^ bit) for i in range(head_total)])
        low = jnp.where(mine == 0, current, got)
        high = jnp.where(mine == 0, got, current)
        current = jnp.stack([low, high], axis=current.ndim - 1)
    return current.reshape(rows, head_total * width)


def gather_levels(current, head_id, head_total, level_list):
    for level in level_list:
        bit = 1 << level
        mine = (head_id >> level) & 1
        got = lax.ppermute(current, "heads", [(i, i ^ bit) for i in range(head_total)])
        low = jnp.where(mine == 0, current, got)
        high = jnp.where(mine == 0, got, current)
        current = jnp.stack([low, high], axis=current.ndim - 1)
    return current


def absorb_block(state, query_heads, key_block, value_block, linked, head_count, brick_rows):
    row_max, row_mass, weighted = state
    key_rows = key_block.reshape(-1, head_count, HEAD_DIM)
    value_rows = value_block.reshape(-1, head_count, HEAD_DIM)
    scores = (
        jnp.einsum("bqhd,khd->bhqk", query_heads, key_rows, preferred_element_type=jnp.float32)
        * HEAD_DIM ** (-0.5)
    )
    keep = jnp.repeat(linked, brick_rows, axis=1, total_repeat_length=key_rows.shape[0])
    scores = jnp.where(keep[:, None, None, :], scores, -1e30)
    max_new = jnp.maximum(row_max, jnp.max(scores, axis=-1))
    factor = jnp.exp(row_max - max_new)
    weights = jnp.exp(scores - max_new[..., None])
    mass_new = row_mass * factor + jnp.sum(weights, axis=-1)
    sum_new = weighted * jnp.transpose(factor, (0, 2, 1))[..., None] + jnp.einsum(
        "bhqk,khd->bqhd", weights.astype(jnp.bfloat16), value_rows,
        preferred_element_type=jnp.float32,
    )
    return max_new, mass_new, sum_new


def shards(
    voxel_feats,
    face_open,
    pattern,
    conv_weight,
    conv_bias,
    gain_one,
    query_weight,
    key_weight,
    value_weight,
    out_weight,
    gain_two,
    up_weight,
    down_weight,
):
    row_count = voxel_feats.shape[0]
    local_width = voxel_feats.shape[1]
    face_rows = EDGE * EDGE
    brick_rows = EDGE * face_rows
    local_bricks = row_count // brick_rows
    brick_total = pattern.shape[0]
    first_brick = lax.axis_index("bricks") * local_bricks
    extended = extended_2(voxel_feats, (("bricks", 0),), face_rows)
    brick_vals = extended[face_rows : face_rows + row_count].astype(jnp.float32)
    brick_vals = brick_vals.reshape(local_bricks, EDGE, face_rows, local_width)
    lower_face = jnp.concatenate(
        [extended[:face_rows].astype(jnp.float32)[None], brick_vals[:-1, EDGE - 1]], axis=0
    )
    upper_face = jnp.concatenate(
        [brick_vals[1:, 0], extended[face_rows + row_count :].astype(jnp.float32)[None]], axis=0
    )
    brick_ids = first_brick + jnp.arange(local_bricks, dtype=jnp.int32)
    lower_open = jnp.where(brick_ids >= 1, jnp.take(face_open, brick_ids), 0)
    upper_open = jnp.where(
        brick_ids + 1 < brick_total,
        jnp.take(face_open, jnp.minimum(brick_ids + 1, brick_total - 1)),
        0,
    )
    lower_face = lower_face * lower_open.astype(jnp.float32)[:, None, None]
    upper_face = upper_face * upper_open.astype(jnp.float32)[:, None, None]
    conv_out = depthwise(brick_vals, lower_face, upper_face, conv_weight, conv_bias)
    stream = (voxel_feats.astype(jnp.float32) + conv_out).astype(jnp.bfloat16)
    head_total = lax.axis_size("heads")
    head_id = lax.axis_index("heads")
    head_count = local_width // HEAD_DIM
    brick_dev = lax.axis_index("bricks")
    dev_total = lax.axis_size("bricks")
    ring = [(i, (i + 1) % dev_total) for i in range(dev_total)]
    linked_rows = lax.dynamic_slice_in_dim(pattern, first_brick, local_bricks, 0)
    state = (
        jnp.full((local_bricks, head_count, brick_rows), -1e30, jnp.float32),
        jnp.zeros((local_bricks, head_count, brick_rows), jnp.float32),
        jnp.zeros((local_bricks, brick_rows, head_count, HEAD_DIM), jnp.float32),
    )
    chunk_count = 2 if row_count % 16 == 0 else 1
    chunk_rows = row_count // chunk_count
    split_last = local_bricks == 1 and chunk_count == 2
    levels = level_count(head_total)
    cross_levels = list(reversed(range(1, levels)))
    chip_levels = list(range(min(levels, 1)))
    ringed = {0: stream}
    crossed = {}
    gathered = {}
    query_heads = None
    for slot in range(dev_total + 2):
        made = []
        if 1 <= slot + 1 < dev_total:
            ringed[slot + 1] = lax.ppermute(ringed[slot], "bricks", ring)
            made.append((ringed, slot + 1))
        if slot < dev_total:
            crossed[slot] = gather_levels(ringed[slot], head_id, head_total, cross_levels)
            made.append((crossed, slot))
        if 0 <= slot - 1 < dev_total:
            gathered[slot - 1] = gather_levels(
                crossed[slot - 1], head_id, head_total, chip_levels
            ).reshape(row_count, head_total * local_width)
            made.append((gathered, slot - 1))
        step = slot - 2
        if 0 <= step < dev_total:
            normed_now = layer_norm(gathered[step], gain_one).astype(jnp.bfloat16)
            if step == 0:
                queries = jnp.dot(
                    normed_now, query_weight, preferred_element_type=jnp.float32
                ).astype(jnp.bfloat16)
                query_heads = queries.reshape(local_bricks, brick_rows, head_count, HEAD_DIM)
            key_block = jnp.dot(
                normed_now, key_weight, preferred_element_type=jnp.float32
            ).astype(jnp.bfloat16)
            value_block = jnp.dot(
                normed_now, value_weight, preferred_element_type=jnp.float32
            ).astype(jnp.bfloat16)
            source = (brick_dev - step) % dev_total
            key_ids = source * local_bricks + jnp.arange(local_bricks, dtype=jnp.int32)
            linked = jnp.take(linked_rows, key_ids, axis=1) > 0
            if step == dev_total - 1 and split_last:
                parts = []
                for half in range(chunk_count):
                    cut = slice(half * chunk_rows, (half + 1) * chunk_rows)
                    part = (state[0][:, :, cut], state[1][:, :, cut], state[2][:, cut])
                    parts.append(absorb_block(
                        part, query_heads[:, cut], key_block, value_block, linked, head_count,
                        brick_rows,
                    ))
                state = parts
            else:
                state = absorb_block(
                    state, query_heads, key_block, value_block, linked, head_count, brick_rows
                )
        if slot < dev_total + 1:
            packed = lax.optimization_barrier((state, [table[key] for table, key in made]))
            state = packed[0]
            for (table, key), value in zip(made, packed[1]):
                table[key] = value
    if not split_last:
        state = [state]
    attended_parts = []
    for row_max, row_mass, weighted in state:
        attended = weighted / jnp.transpose(row_mass, (0, 2, 1))[:, :, :, None]
        attended_parts.append(attended.astype(jnp.bfloat16).reshape(-1, local_width))
    attended = jnp.concatenate(attended_parts, axis=0) if not split_last else None
    outputs = []
    for chunk in range(chunk_count):
        rows = slice(chunk * chunk_rows, (chunk + 1) * chunk_rows)
        attended_rows = attended_parts[chunk] if split_last else attended[rows]
        partial_out = jnp.dot(attended_rows, out_weight, preferred_element_type=jnp.float32)
        out_sum = scatter_heads(partial_out, head_id, head_total)
        stream_two = (stream[rows].astype(jnp.float32) + out_sum).astype(jnp.bfloat16)
        stream_two_full = gather_heads(stream_two, head_id, head_total)
        normed_two = layer_norm(stream_two_full, gain_two).astype(jnp.bfloat16)
        hidden = jax.nn.gelu(
            jnp.dot(normed_two, up_weight, preferred_element_type=jnp.float32), approximate=True
        ).astype(jnp.bfloat16)
        lowered = jnp.dot(hidden, down_weight, preferred_element_type=jnp.float32)
        mixed = scatter_heads(lowered, head_id, head_total)
        outputs.append((stream_two.astype(jnp.float32) + mixed).astype(jnp.bfloat16))
    return jnp.concatenate(outputs, axis=0)

def solution(mesh):
    return jax.shard_map(
        shards,
        mesh=mesh,
        in_specs=(
            P(("groups", "bricks"), "heads"),
            P("groups"),
            P("groups", None),
            P(None, "heads"),
            P("heads"),
            P(),
            P(None, "heads"),
            P(None, "heads"),
            P(None, "heads"),
            P("heads", None),
            P(),
            P(None, "heads"),
            P("heads", None),
        ),
        out_specs=P(("groups", "bricks"), "heads"),
        check_vma=False,
    )
```

```python
import jax
import jax.numpy as jnp
from jax import lax
from jax.sharding import PartitionSpec as P

EDGE = 8
HEAD_DIM = 64


epsilon = 1e-05


def extended_2(value, sides, width):
    for axis, dim in sides:
        size, length = (lax.axis_size(axis), value.shape[dim])
        up = [(i, (i + 1) % size) for i in range(size - 1)]
        down = [(j, i) for i, j in up]
        last = lax.slice_in_dim(value, length - width, length, axis=dim)
        first = lax.slice_in_dim(value, 0, width, axis=dim)
        before = lax.ppermute(last, axis, up)
        after = lax.ppermute(first, axis, down)
        value = jnp.concatenate([before, value, after], axis=dim)
    return value


def layer_norm(inputs, gain_vec):
    values = inputs.astype(jnp.float32)
    center = values - jnp.mean(values, axis=-1, keepdims=True)
    spread = jnp.mean(center * center, axis=-1, keepdims=True)
    return center * lax.rsqrt(spread + epsilon) * gain_vec.astype(jnp.float32)


def depthwise(brick_vals, lower_face, upper_face, conv_weight, conv_bias):
    brick_count = brick_vals.shape[0]
    edge_len = brick_vals.shape[1]
    channels = brick_vals.shape[3]
    layers = jnp.concatenate([lower_face[:, None], brick_vals, upper_face[:, None]], axis=1)
    layers = layers.reshape(brick_count, edge_len + 2, edge_len, edge_len, channels)
    padded = jnp.pad(layers, ((0, 0), (0, 0), (1, 1), (1, 1), (0, 0)))
    weights = conv_weight.astype(jnp.float32)
    summed = jnp.zeros((brick_count, edge_len, edge_len, edge_len, channels), jnp.float32)
    for step_x in range(3):
        for step_y in range(3):
            for step_z in range(3):
                window = padded[
                    :,
                    step_x : step_x + edge_len,
                    step_y : step_y + edge_len,
                    step_z : step_z + edge_len,
                ]
                summed = summed + weights[step_x * 9 + step_y * 3 + step_z] * window
    return summed.reshape(brick_count * edge_len**3, channels) + conv_bias.astype(jnp.float32)


def level_count(total):
    levels = total.bit_length() - 1
    assert 1 << levels == total
    return levels


def scatter_heads(partial, head_id, head_total):
    levels = level_count(head_total)
    rows = partial.shape[0]
    width = partial.shape[1] // head_total
    current = partial.reshape((rows,) + (2,) * levels + (width,))
    for level in range(levels):
        bit = 1 << level
        axis = levels - level
        mine = (head_id >> level) & 1
        keep = lax.dynamic_index_in_dim(current, mine, axis, keepdims=False)
        give = lax.dynamic_index_in_dim(current, 1 - mine, axis, keepdims=False)
        got = lax.ppermute(
            give.astype(jnp.bfloat16), "heads", [(i, i ^ bit) for i in range(head_total)]
        )
        current = keep + got.astype(jnp.float32)
    return current.reshape(rows, width)


def gather_heads(piece, head_id, head_total):
    levels = level_count(head_total)
    rows, width = piece.shape
    current = piece
    for level in reversed(range(levels)):
        bit = 1 << level
        mine = (head_id >> level) & 1
        got = lax.ppermute(current, "heads", [(i, i ^ bit) for i in range(head_total)])
        low = jnp.where(mine == 0, current, got)
        high = jnp.where(mine == 0, got, current)
        current = jnp.stack([low, high], axis=current.ndim - 1)
    return current.reshape(rows, head_total * width)


def gather_levels(current, head_id, head_total, level_list):
    for level in level_list:
        bit = 1 << level
        mine = (head_id >> level) & 1
        got = lax.ppermute(current, "heads", [(i, i ^ bit) for i in range(head_total)])
        low = jnp.where(mine == 0, current, got)
        high = jnp.where(mine == 0, got, current)
        current = jnp.stack([low, high], axis=current.ndim - 1)
    return current


def absorb_block(state, query_heads, key_block, value_block, linked, head_count, brick_rows):
    row_max, row_mass, weighted = state
    key_rows = key_block.reshape(-1, head_count, HEAD_DIM)
    value_rows = value_block.reshape(-1, head_count, HEAD_DIM)
    scores = (
        jnp.einsum("bqhd,khd->bhqk", query_heads, key_rows, preferred_element_type=jnp.float32)
        * HEAD_DIM ** (-0.5)
    )
    keep = jnp.repeat(linked, brick_rows, axis=1, total_repeat_length=key_rows.shape[0])
    scores = jnp.where(keep[:, None, None, :], scores, -1e30)
    max_new = jnp.maximum(row_max, jnp.max(scores, axis=-1))
    factor = jnp.exp(row_max - max_new)
    weights = jnp.exp(scores - max_new[..., None])
    mass_new = row_mass * factor + jnp.sum(weights, axis=-1)
    sum_new = weighted * jnp.transpose(factor, (0, 2, 1))[..., None] + jnp.einsum(
        "bhqk,khd->bqhd", weights.astype(jnp.bfloat16), value_rows,
        preferred_element_type=jnp.float32,
    )
    return max_new, mass_new, sum_new


def shards(
    voxel_feats,
    face_open,
    pattern,
    conv_weight,
    conv_bias,
    gain_one,
    query_weight,
    key_weight,
    value_weight,
    out_weight,
    gain_two,
    up_weight,
    down_weight,
):
    row_count = voxel_feats.shape[0]
    local_width = voxel_feats.shape[1]
    face_rows = EDGE * EDGE
    brick_rows = EDGE * face_rows
    local_bricks = row_count // brick_rows
    brick_total = pattern.shape[0]
    first_brick = lax.axis_index("bricks") * local_bricks
    extended = extended_2(voxel_feats, (("bricks", 0),), face_rows)
    brick_vals = extended[face_rows : face_rows + row_count].astype(jnp.float32)
    brick_vals = brick_vals.reshape(local_bricks, EDGE, face_rows, local_width)
    lower_face = jnp.concatenate(
        [extended[:face_rows].astype(jnp.float32)[None], brick_vals[:-1, EDGE - 1]], axis=0
    )
    upper_face = jnp.concatenate(
        [brick_vals[1:, 0], extended[face_rows + row_count :].astype(jnp.float32)[None]], axis=0
    )
    brick_ids = first_brick + jnp.arange(local_bricks, dtype=jnp.int32)
    lower_open = jnp.where(brick_ids >= 1, jnp.take(face_open, brick_ids), 0)
    upper_open = jnp.where(
        brick_ids + 1 < brick_total,
        jnp.take(face_open, jnp.minimum(brick_ids + 1, brick_total - 1)),
        0,
    )
    lower_face = lower_face * lower_open.astype(jnp.float32)[:, None, None]
    upper_face = upper_face * upper_open.astype(jnp.float32)[:, None, None]
    conv_out = depthwise(brick_vals, lower_face, upper_face, conv_weight, conv_bias)
    stream = (voxel_feats.astype(jnp.float32) + conv_out).astype(jnp.bfloat16)
    head_total = lax.axis_size("heads")
    head_id = lax.axis_index("heads")
    head_count = local_width // HEAD_DIM
    brick_dev = lax.axis_index("bricks")
    dev_total = lax.axis_size("bricks")
    ring = [(i, (i + 1) % dev_total) for i in range(dev_total)]
    linked_rows = lax.dynamic_slice_in_dim(pattern, first_brick, local_bricks, 0)
    state = (
        jnp.full((local_bricks, head_count, brick_rows), -1e30, jnp.float32),
        jnp.zeros((local_bricks, head_count, brick_rows), jnp.float32),
        jnp.zeros((local_bricks, brick_rows, head_count, HEAD_DIM), jnp.float32),
    )
    chunk_count = 2 if row_count % 16 == 0 else 1
    chunk_rows = row_count // chunk_count
    split_last = local_bricks == 1 and chunk_count == 2
    levels = level_count(head_total)
    cross_levels = list(reversed(range(1, levels)))
    chip_levels = list(range(min(levels, 1)))
    ringed = {0: stream}
    crossed = {}
    gathered = {}
    query_heads = None
    for slot in range(dev_total + 2):
        made = []
        if 1 <= slot + 1 < dev_total:
            ringed[slot + 1] = lax.ppermute(ringed[slot], "bricks", ring)
            made.append((ringed, slot + 1))
        if slot < dev_total:
            crossed[slot] = gather_levels(ringed[slot], head_id, head_total, cross_levels)
            made.append((crossed, slot))
        if 0 <= slot - 1 < dev_total:
            gathered[slot - 1] = gather_levels(
                crossed[slot - 1], head_id, head_total, chip_levels
            ).reshape(row_count, head_total * local_width)
            made.append((gathered, slot - 1))
        step = slot - 2
        if 0 <= step < dev_total:
            normed_now = layer_norm(gathered[step], gain_one).astype(jnp.bfloat16)
            if step == 0:
                queries = jnp.dot(
                    normed_now, query_weight, preferred_element_type=jnp.float32
                ).astype(jnp.bfloat16)
                query_heads = queries.reshape(local_bricks, brick_rows, head_count, HEAD_DIM)
            key_block = jnp.dot(
                normed_now, key_weight, preferred_element_type=jnp.float32
            ).astype(jnp.bfloat16)
            value_block = jnp.dot(
                normed_now, value_weight, preferred_element_type=jnp.float32
            ).astype(jnp.bfloat16)
            source = (brick_dev - step) % dev_total
            key_ids = source * local_bricks + jnp.arange(local_bricks, dtype=jnp.int32)
            linked = jnp.take(linked_rows, key_ids, axis=1) > 0
            if step == dev_total - 1 and split_last:
                parts = []
                for half in range(chunk_count):
                    cut = slice(half * chunk_rows, (half + 1) * chunk_rows)
                    part = (state[0][:, :, cut], state[1][:, :, cut], state[2][:, cut])
                    parts.append(absorb_block(
                        part, query_heads[:, cut], key_block, value_block, linked, head_count,
                        brick_rows,
                    ))
                state = parts
            else:
                state = absorb_block(
                    state, query_heads, key_block, value_block, linked, head_count, brick_rows
                )
        if slot < dev_total + 1:
            packed = lax.optimization_barrier((state, [table[key] for table, key in made]))
            state = packed[0]
            for (table, key), value in zip(made, packed[1]):
                table[key] = value
    if not split_last:
        state = [state]
    attended_parts = []
    for row_max, row_mass, weighted in state:
        attended = weighted / jnp.transpose(row_mass, (0, 2, 1))[:, :, :, None]
        attended_parts.append(attended.astype(jnp.bfloat16).reshape(-1, local_width))
    attended = jnp.concatenate(attended_parts, axis=0) if not split_last else None
    held = [{} for _ in range(chunk_count)]
    for slot in range(chunk_count + 3):
        made = []
        for chunk in range(chunk_count):
            stage = slot - chunk
            rows = slice(chunk * chunk_rows, (chunk + 1) * chunk_rows)
            box = held[chunk]
            if stage == 0:
                attended_rows = attended_parts[chunk] if split_last else attended[rows]
                partial_out = jnp.dot(
                    attended_rows, out_weight, preferred_element_type=jnp.float32
                )
                out_sum = scatter_heads(partial_out, head_id, head_total)
                box["two"] = (stream[rows].astype(jnp.float32) + out_sum).astype(jnp.bfloat16)
                made.append((box, "two"))
            elif stage == 1:
                box["full"] = gather_heads(box["two"], head_id, head_total)
                made.append((box, "full"))
            elif stage == 2:
                normed_two = layer_norm(box["full"], gain_two).astype(jnp.bfloat16)
                hidden = jax.nn.gelu(
                    jnp.dot(normed_two, up_weight, preferred_element_type=jnp.float32),
                    approximate=True,
                ).astype(jnp.bfloat16)
                box["low"] = jnp.dot(hidden, down_weight, preferred_element_type=jnp.float32)
                made.append((box, "low"))
            elif stage == 3:
                mixed = scatter_heads(box["low"], head_id, head_total)
                box["out"] = (box["two"].astype(jnp.float32) + mixed).astype(jnp.bfloat16)
        if made and slot < chunk_count + 2:
            packed = lax.optimization_barrier([table[key] for table, key in made])
            for (table, key), value in zip(made, packed):
                table[key] = value
    outputs = [box["out"] for box in held]
    return jnp.concatenate(outputs, axis=0)

def solution(mesh):
    return jax.shard_map(
        shards,
        mesh=mesh,
        in_specs=(
            P(("groups", "bricks"), "heads"),
            P("groups"),
            P("groups", None),
            P(None, "heads"),
            P("heads"),
            P(),
            P(None, "heads"),
            P(None, "heads"),
            P(None, "heads"),
            P("heads", None),
            P(),
            P(None, "heads"),
            P("heads", None),
        ),
        out_specs=P(("groups", "bricks"), "heads"),
        check_vma=False,
    )
```

```python
import jax
import jax.numpy as jnp
from jax import lax
from jax.sharding import PartitionSpec as P

EDGE = 8
HEAD_DIM = 64


epsilon = 1e-05


def extended_2(value, sides, width):
    for axis, dim in sides:
        size, length = (lax.axis_size(axis), value.shape[dim])
        up = [(i, (i + 1) % size) for i in range(size - 1)]
        down = [(j, i) for i, j in up]
        last = lax.slice_in_dim(value, length - width, length, axis=dim)
        first = lax.slice_in_dim(value, 0, width, axis=dim)
        before = lax.ppermute(last, axis, up)
        after = lax.ppermute(first, axis, down)
        value = jnp.concatenate([before, value, after], axis=dim)
    return value


def layer_norm(inputs, gain_vec):
    values = inputs.astype(jnp.float32)
    center = values - jnp.mean(values, axis=-1, keepdims=True)
    spread = jnp.mean(center * center, axis=-1, keepdims=True)
    return center * lax.rsqrt(spread + epsilon) * gain_vec.astype(jnp.float32)


def depthwise(brick_vals, lower_face, upper_face, conv_weight, conv_bias):
    brick_count = brick_vals.shape[0]
    edge_len = brick_vals.shape[1]
    channels = brick_vals.shape[3]
    layers = jnp.concatenate([lower_face[:, None], brick_vals, upper_face[:, None]], axis=1)
    layers = layers.reshape(brick_count, edge_len + 2, edge_len, edge_len, channels)
    padded = jnp.pad(layers, ((0, 0), (0, 0), (1, 1), (1, 1), (0, 0)))
    weights = conv_weight.astype(jnp.float32)
    summed = jnp.zeros((brick_count, edge_len, edge_len, edge_len, channels), jnp.float32)
    for step_x in range(3):
        for step_y in range(3):
            for step_z in range(3):
                window = padded[
                    :,
                    step_x : step_x + edge_len,
                    step_y : step_y + edge_len,
                    step_z : step_z + edge_len,
                ]
                summed = summed + weights[step_x * 9 + step_y * 3 + step_z] * window
    return summed.reshape(brick_count * edge_len**3, channels) + conv_bias.astype(jnp.float32)


def level_count(total):
    levels = total.bit_length() - 1
    assert 1 << levels == total
    return levels


def scatter_heads(partial, head_id, head_total):
    levels = level_count(head_total)
    rows = partial.shape[0]
    width = partial.shape[1] // head_total
    current = partial.reshape((rows,) + (2,) * levels + (width,))
    for level in range(levels):
        bit = 1 << level
        axis = levels - level
        mine = (head_id >> level) & 1
        keep = lax.dynamic_index_in_dim(current, mine, axis, keepdims=False)
        give = lax.dynamic_index_in_dim(current, 1 - mine, axis, keepdims=False)
        got = lax.ppermute(
            give.astype(jnp.bfloat16), "heads", [(i, i ^ bit) for i in range(head_total)]
        )
        current = keep + got.astype(jnp.float32)
    return current.reshape(rows, width)


def gather_heads(piece, head_id, head_total):
    levels = level_count(head_total)
    rows, width = piece.shape
    current = piece
    for level in reversed(range(levels)):
        bit = 1 << level
        mine = (head_id >> level) & 1
        got = lax.ppermute(current, "heads", [(i, i ^ bit) for i in range(head_total)])
        low = jnp.where(mine == 0, current, got)
        high = jnp.where(mine == 0, got, current)
        current = jnp.stack([low, high], axis=current.ndim - 1)
    return current.reshape(rows, head_total * width)


def gather_levels(current, head_id, head_total, level_list):
    for level in level_list:
        bit = 1 << level
        mine = (head_id >> level) & 1
        got = lax.ppermute(current, "heads", [(i, i ^ bit) for i in range(head_total)])
        low = jnp.where(mine == 0, current, got)
        high = jnp.where(mine == 0, got, current)
        current = jnp.stack([low, high], axis=current.ndim - 1)
    return current


def absorb_block(state, query_heads, key_block, value_block, linked, head_count, brick_rows):
    row_max, row_mass, weighted = state
    key_rows = key_block.reshape(-1, head_count, HEAD_DIM)
    value_rows = value_block.reshape(-1, head_count, HEAD_DIM)
    scores = (
        jnp.einsum("bqhd,khd->bhqk", query_heads, key_rows, preferred_element_type=jnp.float32)
        * HEAD_DIM ** (-0.5)
    )
    keep = jnp.repeat(linked, brick_rows, axis=1, total_repeat_length=key_rows.shape[0])
    scores = jnp.where(keep[:, None, None, :], scores, -1e30)
    max_new = jnp.maximum(row_max, jnp.max(scores, axis=-1))
    factor = jnp.exp(row_max - max_new)
    weights = jnp.exp(scores - max_new[..., None])
    mass_new = row_mass * factor + jnp.sum(weights, axis=-1)
    sum_new = weighted * jnp.transpose(factor, (0, 2, 1))[..., None] + jnp.einsum(
        "bhqk,khd->bqhd", weights.astype(jnp.bfloat16), value_rows,
        preferred_element_type=jnp.float32,
    )
    return max_new, mass_new, sum_new


def shards(
    voxel_feats,
    face_open,
    pattern,
    conv_weight,
    conv_bias,
    gain_one,
    query_weight,
    key_weight,
    value_weight,
    out_weight,
    gain_two,
    up_weight,
    down_weight,
):
    row_count = voxel_feats.shape[0]
    local_width = voxel_feats.shape[1]
    face_rows = EDGE * EDGE
    brick_rows = EDGE * face_rows
    local_bricks = row_count // brick_rows
    brick_total = pattern.shape[0]
    first_brick = lax.axis_index("bricks") * local_bricks
    extended = extended_2(voxel_feats, (("bricks", 0),), face_rows)
    brick_vals = extended[face_rows : face_rows + row_count].astype(jnp.float32)
    brick_vals = brick_vals.reshape(local_bricks, EDGE, face_rows, local_width)
    lower_face = jnp.concatenate(
        [extended[:face_rows].astype(jnp.float32)[None], brick_vals[:-1, EDGE - 1]], axis=0
    )
    upper_face = jnp.concatenate(
        [brick_vals[1:, 0], extended[face_rows + row_count :].astype(jnp.float32)[None]], axis=0
    )
    brick_ids = first_brick + jnp.arange(local_bricks, dtype=jnp.int32)
    lower_open = jnp.where(brick_ids >= 1, jnp.take(face_open, brick_ids), 0)
    upper_open = jnp.where(
        brick_ids + 1 < brick_total,
        jnp.take(face_open, jnp.minimum(brick_ids + 1, brick_total - 1)),
        0,
    )
    lower_face = lower_face * lower_open.astype(jnp.float32)[:, None, None]
    upper_face = upper_face * upper_open.astype(jnp.float32)[:, None, None]
    conv_out = depthwise(brick_vals, lower_face, upper_face, conv_weight, conv_bias)
    stream = (voxel_feats.astype(jnp.float32) + conv_out).astype(jnp.bfloat16)
    head_total = lax.axis_size("heads")
    head_id = lax.axis_index("heads")
    head_count = local_width // HEAD_DIM
    brick_dev = lax.axis_index("bricks")
    dev_total = lax.axis_size("bricks")
    ring = [(i, (i + 1) % dev_total) for i in range(dev_total)]
    linked_rows = lax.dynamic_slice_in_dim(pattern, first_brick, local_bricks, 0)
    state = (
        jnp.full((local_bricks, head_count, brick_rows), -1e30, jnp.float32),
        jnp.zeros((local_bricks, head_count, brick_rows), jnp.float32),
        jnp.zeros((local_bricks, brick_rows, head_count, HEAD_DIM), jnp.float32),
    )
    chunk_count = 2 if row_count % 16 == 0 else 1
    chunk_rows = row_count // chunk_count
    split_last = local_bricks == 1 and chunk_count == 2
    levels = level_count(head_total)
    cross_levels = list(reversed(range(1, levels)))
    chip_levels = list(range(min(levels, 1)))
    ringed = {0: stream}
    crossed = {}
    gathered = {}
    query_heads = None
    for slot in range(dev_total + 2):
        made = []
        if 1 <= slot + 1 < dev_total:
            ringed[slot + 1] = lax.ppermute(ringed[slot], "bricks", ring)
            made.append((ringed, slot + 1))
        if slot < dev_total:
            crossed[slot] = gather_levels(ringed[slot], head_id, head_total, cross_levels)
            made.append((crossed, slot))
        if 0 <= slot - 1 < dev_total:
            gathered[slot - 1] = gather_levels(
                crossed[slot - 1], head_id, head_total, chip_levels
            ).reshape(row_count, head_total * local_width)
            made.append((gathered, slot - 1))
        step = slot - 2
        if 0 <= step < dev_total:
            normed_now = layer_norm(gathered[step], gain_one).astype(jnp.bfloat16)
            if step == 0:
                queries = jnp.dot(
                    normed_now, query_weight, preferred_element_type=jnp.float32
                ).astype(jnp.bfloat16)
                query_heads = queries.reshape(local_bricks, brick_rows, head_count, HEAD_DIM)
            key_block = jnp.dot(
                normed_now, key_weight, preferred_element_type=jnp.float32
            ).astype(jnp.bfloat16)
            value_block = jnp.dot(
                normed_now, value_weight, preferred_element_type=jnp.float32
            ).astype(jnp.bfloat16)
            source = (brick_dev - step) % dev_total
            key_ids = source * local_bricks + jnp.arange(local_bricks, dtype=jnp.int32)
            linked = jnp.take(linked_rows, key_ids, axis=1) > 0
            if step == dev_total - 1 and split_last:
                parts = []
                for half in range(chunk_count):
                    cut = slice(half * chunk_rows, (half + 1) * chunk_rows)
                    part = (state[0][:, :, cut], state[1][:, :, cut], state[2][:, cut])
                    parts.append(absorb_block(
                        part, query_heads[:, cut], key_block, value_block, linked, head_count,
                        brick_rows,
                    ))
                state = parts
            else:
                state = absorb_block(
                    state, query_heads, key_block, value_block, linked, head_count, brick_rows
                )
        if slot < dev_total + 1:
            packed = lax.optimization_barrier((state, [table[key] for table, key in made]))
            state = packed[0]
            for (table, key), value in zip(made, packed[1]):
                table[key] = value
    if not split_last:
        state = [state]
    attended_parts = []
    for row_max, row_mass, weighted in state:
        attended = weighted / jnp.transpose(row_mass, (0, 2, 1))[:, :, :, None]
        attended_parts.append(attended.astype(jnp.bfloat16).reshape(-1, local_width))
    attended = jnp.concatenate(attended_parts, axis=0) if not split_last else None
    outputs = []
    for chunk in range(chunk_count):
        rows = slice(chunk * chunk_rows, (chunk + 1) * chunk_rows)
        attended_rows = attended_parts[chunk] if split_last else attended[rows]
        partial_out = jnp.dot(attended_rows, out_weight, preferred_element_type=jnp.float32)
        out_sum = scatter_heads(partial_out, head_id, head_total)
        stream_two = (stream[rows].astype(jnp.float32) + out_sum).astype(jnp.bfloat16)
        stream_two_full = gather_heads(stream_two, head_id, head_total)
        normed_two = layer_norm(stream_two_full, gain_two).astype(jnp.bfloat16)
        hidden = jax.nn.gelu(
            jnp.dot(normed_two, up_weight, preferred_element_type=jnp.float32), approximate=True
        ).astype(jnp.bfloat16)
        hidden = lax.optimization_barrier(hidden)
        lowered = jnp.dot(hidden, down_weight, preferred_element_type=jnp.float32)
        mixed = scatter_heads(lowered, head_id, head_total)
        outputs.append((stream_two.astype(jnp.float32) + mixed).astype(jnp.bfloat16))
    return jnp.concatenate(outputs, axis=0)

def solution(mesh):
    return jax.shard_map(
        shards,
        mesh=mesh,
        in_specs=(
            P(("groups", "bricks"), "heads"),
            P("groups"),
            P("groups", None),
            P(None, "heads"),
            P("heads"),
            P(),
            P(None, "heads"),
            P(None, "heads"),
            P(None, "heads"),
            P("heads", None),
            P(),
            P(None, "heads"),
            P("heads", None),
        ),
        out_specs=P(("groups", "bricks"), "heads"),
        check_vma=False,
    )
```

```python
import jax
import jax.numpy as jnp
from jax import lax
from jax.sharding import PartitionSpec as P

EDGE = 8
HEAD_DIM = 64


epsilon = 1e-05


def extended_2(value, sides, width):
    for axis, dim in sides:
        size, length = (lax.axis_size(axis), value.shape[dim])
        up = [(i, (i + 1) % size) for i in range(size - 1)]
        down = [(j, i) for i, j in up]
        last = lax.slice_in_dim(value, length - width, length, axis=dim)
        first = lax.slice_in_dim(value, 0, width, axis=dim)
        before = lax.ppermute(last, axis, up)
        after = lax.ppermute(first, axis, down)
        value = jnp.concatenate([before, value, after], axis=dim)
    return value


def layer_norm(inputs, gain_vec):
    values = inputs.astype(jnp.float32)
    center = values - jnp.mean(values, axis=-1, keepdims=True)
    spread = jnp.mean(center * center, axis=-1, keepdims=True)
    return center * lax.rsqrt(spread + epsilon) * gain_vec.astype(jnp.float32)


def depthwise(brick_vals, lower_face, upper_face, conv_weight, conv_bias):
    brick_count = brick_vals.shape[0]
    edge_len = brick_vals.shape[1]
    channels = brick_vals.shape[3]
    layers = jnp.concatenate([lower_face[:, None], brick_vals, upper_face[:, None]], axis=1)
    layers = layers.reshape(brick_count, edge_len + 2, edge_len, edge_len, channels)
    padded = jnp.pad(layers, ((0, 0), (0, 0), (1, 1), (1, 1), (0, 0)))
    weights = conv_weight.astype(jnp.float32)
    summed = jnp.zeros((brick_count, edge_len, edge_len, edge_len, channels), jnp.float32)
    for step_x in range(3):
        for step_y in range(3):
            for step_z in range(3):
                window = padded[
                    :,
                    step_x : step_x + edge_len,
                    step_y : step_y + edge_len,
                    step_z : step_z + edge_len,
                ]
                summed = summed + weights[step_x * 9 + step_y * 3 + step_z] * window
    return summed.reshape(brick_count * edge_len**3, channels) + conv_bias.astype(jnp.float32)


def level_count(total):
    levels = total.bit_length() - 1
    assert 1 << levels == total
    return levels


def scatter_heads(partial, head_id, head_total):
    levels = level_count(head_total)
    rows = partial.shape[0]
    width = partial.shape[1] // head_total
    current = partial.reshape((rows,) + (2,) * levels + (width,))
    for level in range(levels):
        bit = 1 << level
        axis = levels - level
        mine = (head_id >> level) & 1
        keep = lax.dynamic_index_in_dim(current, mine, axis, keepdims=False)
        give = lax.dynamic_index_in_dim(current, 1 - mine, axis, keepdims=False)
        got = lax.ppermute(
            give.astype(jnp.bfloat16), "heads", [(i, i ^ bit) for i in range(head_total)]
        )
        current = keep + got.astype(jnp.float32)
    return current.reshape(rows, width)


def gather_heads(piece, head_id, head_total):
    levels = level_count(head_total)
    rows, width = piece.shape
    current = piece
    for level in reversed(range(levels)):
        bit = 1 << level
        mine = (head_id >> level) & 1
        got = lax.ppermute(current, "heads", [(i, i ^ bit) for i in range(head_total)])
        low = jnp.where(mine == 0, current, got)
        high = jnp.where(mine == 0, got, current)
        current = jnp.stack([low, high], axis=current.ndim - 1)
    return current.reshape(rows, head_total * width)


def gather_levels(current, head_id, head_total, level_list):
    for level in level_list:
        bit = 1 << level
        mine = (head_id >> level) & 1
        got = lax.ppermute(current, "heads", [(i, i ^ bit) for i in range(head_total)])
        low = jnp.where(mine == 0, current, got)
        high = jnp.where(mine == 0, got, current)
        current = jnp.stack([low, high], axis=current.ndim - 1)
    return current


def absorb_block(state, query_heads, key_block, value_block, linked, head_count, brick_rows):
    row_max, row_mass, weighted = state
    key_rows = key_block.reshape(-1, head_count, HEAD_DIM)
    value_rows = value_block.reshape(-1, head_count, HEAD_DIM)
    scores = (
        jnp.einsum("bqhd,khd->bhqk", query_heads, key_rows, preferred_element_type=jnp.float32)
        * HEAD_DIM ** (-0.5)
    )
    keep = jnp.repeat(linked, brick_rows, axis=1, total_repeat_length=key_rows.shape[0])
    scores = jnp.where(keep[:, None, None, :], scores, -1e30)
    max_new = jnp.maximum(row_max, jnp.max(scores, axis=-1))
    factor = jnp.exp(row_max - max_new)
    weights = jnp.exp(scores - max_new[..., None])
    mass_new = row_mass * factor + jnp.sum(weights, axis=-1)
    sum_new = weighted * jnp.transpose(factor, (0, 2, 1))[..., None] + jnp.einsum(
        "bhqk,khd->bqhd", weights.astype(jnp.bfloat16), value_rows,
        preferred_element_type=jnp.float32,
    )
    return max_new, mass_new, sum_new


def shards(
    voxel_feats,
    face_open,
    pattern,
    conv_weight,
    conv_bias,
    gain_one,
    query_weight,
    key_weight,
    value_weight,
    out_weight,
    gain_two,
    up_weight,
    down_weight,
):
    row_count = voxel_feats.shape[0]
    local_width = voxel_feats.shape[1]
    face_rows = EDGE * EDGE
    brick_rows = EDGE * face_rows
    local_bricks = row_count // brick_rows
    brick_total = pattern.shape[0]
    first_brick = lax.axis_index("bricks") * local_bricks
    extended = extended_2(voxel_feats, (("bricks", 0),), face_rows)
    brick_vals = extended[face_rows : face_rows + row_count].astype(jnp.float32)
    brick_vals = brick_vals.reshape(local_bricks, EDGE, face_rows, local_width)
    lower_face = jnp.concatenate(
        [extended[:face_rows].astype(jnp.float32)[None], brick_vals[:-1, EDGE - 1]], axis=0
    )
    upper_face = jnp.concatenate(
        [brick_vals[1:, 0], extended[face_rows + row_count :].astype(jnp.float32)[None]], axis=0
    )
    brick_ids = first_brick + jnp.arange(local_bricks, dtype=jnp.int32)
    lower_open = jnp.where(brick_ids >= 1, jnp.take(face_open, brick_ids), 0)
    upper_open = jnp.where(
        brick_ids + 1 < brick_total,
        jnp.take(face_open, jnp.minimum(brick_ids + 1, brick_total - 1)),
        0,
    )
    lower_face = lower_face * lower_open.astype(jnp.float32)[:, None, None]
    upper_face = upper_face * upper_open.astype(jnp.float32)[:, None, None]
    conv_out = depthwise(brick_vals, lower_face, upper_face, conv_weight, conv_bias)
    stream = (voxel_feats.astype(jnp.float32) + conv_out).astype(jnp.bfloat16)
    head_total = lax.axis_size("heads")
    head_id = lax.axis_index("heads")
    head_count = local_width // HEAD_DIM
    brick_dev = lax.axis_index("bricks")
    dev_total = lax.axis_size("bricks")
    ring = [(i, (i + 1) % dev_total) for i in range(dev_total)]
    linked_rows = lax.dynamic_slice_in_dim(pattern, first_brick, local_bricks, 0)
    state = (
        jnp.full((local_bricks, head_count, brick_rows), -1e30, jnp.float32),
        jnp.zeros((local_bricks, head_count, brick_rows), jnp.float32),
        jnp.zeros((local_bricks, brick_rows, head_count, HEAD_DIM), jnp.float32),
    )
    chunk_count = 2 if row_count % 16 == 0 else 1
    chunk_rows = row_count // chunk_count
    split_last = local_bricks == 1 and chunk_count == 2
    levels = level_count(head_total)
    cross_levels = list(reversed(range(1, levels)))
    chip_levels = list(range(min(levels, 1)))
    ringed = {0: stream}
    crossed = {}
    gathered = {}
    query_heads = None
    for slot in range(dev_total + 2):
        made = []
        if 1 <= slot + 1 < dev_total:
            ringed[slot + 1] = lax.ppermute(ringed[slot], "bricks", ring)
            made.append((ringed, slot + 1))
        if slot < dev_total:
            crossed[slot] = gather_levels(ringed[slot], head_id, head_total, cross_levels)
            made.append((crossed, slot))
        if 0 <= slot - 1 < dev_total:
            gathered[slot - 1] = gather_levels(
                crossed[slot - 1], head_id, head_total, chip_levels
            ).reshape(row_count, head_total * local_width)
            made.append((gathered, slot - 1))
        step = slot - 2
        if 0 <= step < dev_total:
            normed_now = lax.optimization_barrier(
                layer_norm(gathered[step], gain_one).astype(jnp.bfloat16)
            )
            if step == 0:
                queries = jnp.dot(
                    normed_now, query_weight, preferred_element_type=jnp.float32
                ).astype(jnp.bfloat16)
                query_heads = queries.reshape(local_bricks, brick_rows, head_count, HEAD_DIM)
            key_block = jnp.dot(
                normed_now, key_weight, preferred_element_type=jnp.float32
            ).astype(jnp.bfloat16)
            value_block = jnp.dot(
                normed_now, value_weight, preferred_element_type=jnp.float32
            ).astype(jnp.bfloat16)
            source = (brick_dev - step) % dev_total
            key_ids = source * local_bricks + jnp.arange(local_bricks, dtype=jnp.int32)
            linked = jnp.take(linked_rows, key_ids, axis=1) > 0
            if step == dev_total - 1 and split_last:
                parts = []
                for half in range(chunk_count):
                    cut = slice(half * chunk_rows, (half + 1) * chunk_rows)
                    part = (state[0][:, :, cut], state[1][:, :, cut], state[2][:, cut])
                    parts.append(absorb_block(
                        part, query_heads[:, cut], key_block, value_block, linked, head_count,
                        brick_rows,
                    ))
                state = parts
            else:
                state = absorb_block(
                    state, query_heads, key_block, value_block, linked, head_count, brick_rows
                )
        if slot < dev_total + 1:
            packed = lax.optimization_barrier((state, [table[key] for table, key in made]))
            state = packed[0]
            for (table, key), value in zip(made, packed[1]):
                table[key] = value
    if not split_last:
        state = [state]
    attended_parts = []
    for row_max, row_mass, weighted in state:
        attended = weighted / jnp.transpose(row_mass, (0, 2, 1))[:, :, :, None]
        attended_parts.append(attended.astype(jnp.bfloat16).reshape(-1, local_width))
    attended = jnp.concatenate(attended_parts, axis=0) if not split_last else None
    outputs = []
    for chunk in range(chunk_count):
        rows = slice(chunk * chunk_rows, (chunk + 1) * chunk_rows)
        attended_rows = attended_parts[chunk] if split_last else attended[rows]
        partial_out = jnp.dot(attended_rows, out_weight, preferred_element_type=jnp.float32)
        out_sum = scatter_heads(partial_out, head_id, head_total)
        stream_two = (stream[rows].astype(jnp.float32) + out_sum).astype(jnp.bfloat16)
        stream_two_full = gather_heads(stream_two, head_id, head_total)
        normed_two = layer_norm(stream_two_full, gain_two).astype(jnp.bfloat16)
        hidden = jax.nn.gelu(
            jnp.dot(normed_two, up_weight, preferred_element_type=jnp.float32), approximate=True
        ).astype(jnp.bfloat16)
        hidden = lax.optimization_barrier(hidden)
        lowered = jnp.dot(hidden, down_weight, preferred_element_type=jnp.float32)
        mixed = scatter_heads(lowered, head_id, head_total)
        outputs.append((stream_two.astype(jnp.float32) + mixed).astype(jnp.bfloat16))
    return jnp.concatenate(outputs, axis=0)

def solution(mesh):
    return jax.shard_map(
        shards,
        mesh=mesh,
        in_specs=(
            P(("groups", "bricks"), "heads"),
            P("groups"),
            P("groups", None),
            P(None, "heads"),
            P("heads"),
            P(),
            P(None, "heads"),
            P(None, "heads"),
            P(None, "heads"),
            P("heads", None),
            P(),
            P(None, "heads"),
            P("heads", None),
        ),
        out_specs=P(("groups", "bricks"), "heads"),
        check_vma=False,
    )
```

```python
import jax
import jax.numpy as jnp
from jax import lax
from jax.sharding import PartitionSpec as P

EDGE = 8
HEAD_DIM = 64


epsilon = 1e-05


def extended_2(value, sides, width):
    for axis, dim in sides:
        size, length = (lax.axis_size(axis), value.shape[dim])
        up = [(i, (i + 1) % size) for i in range(size - 1)]
        down = [(j, i) for i, j in up]
        last = lax.slice_in_dim(value, length - width, length, axis=dim)
        first = lax.slice_in_dim(value, 0, width, axis=dim)
        before = lax.ppermute(last, axis, up)
        after = lax.ppermute(first, axis, down)
        value = jnp.concatenate([before, value, after], axis=dim)
    return value


def layer_norm(inputs, gain_vec):
    values = inputs.astype(jnp.float32)
    center = values - jnp.mean(values, axis=-1, keepdims=True)
    spread = jnp.mean(center * center, axis=-1, keepdims=True)
    return center * lax.rsqrt(spread + epsilon) * gain_vec.astype(jnp.float32)


def depthwise(brick_vals, lower_face, upper_face, conv_weight, conv_bias):
    brick_count = brick_vals.shape[0]
    edge_len = brick_vals.shape[1]
    channels = brick_vals.shape[3]
    layers = jnp.concatenate([lower_face[:, None], brick_vals, upper_face[:, None]], axis=1)
    layers = layers.reshape(brick_count, edge_len + 2, edge_len, edge_len, channels)
    padded = jnp.pad(layers, ((0, 0), (0, 0), (1, 1), (1, 1), (0, 0)))
    weights = conv_weight.astype(jnp.float32)
    summed = jnp.zeros((brick_count, edge_len, edge_len, edge_len, channels), jnp.float32)
    for step_x in range(3):
        for step_y in range(3):
            for step_z in range(3):
                window = padded[
                    :,
                    step_x : step_x + edge_len,
                    step_y : step_y + edge_len,
                    step_z : step_z + edge_len,
                ]
                summed = summed + weights[step_x * 9 + step_y * 3 + step_z] * window
    return summed.reshape(brick_count * edge_len**3, channels) + conv_bias.astype(jnp.float32)


def level_count(total):
    levels = total.bit_length() - 1
    assert 1 << levels == total
    return levels


def scatter_heads(partial, head_id, head_total):
    levels = level_count(head_total)
    rows = partial.shape[0]
    width = partial.shape[1] // head_total
    current = partial.reshape((rows,) + (2,) * levels + (width,))
    for level in range(levels):
        bit = 1 << level
        axis = levels - level
        mine = (head_id >> level) & 1
        keep = lax.dynamic_index_in_dim(current, mine, axis, keepdims=False)
        give = lax.dynamic_index_in_dim(current, 1 - mine, axis, keepdims=False)
        got = lax.ppermute(
            give.astype(jnp.bfloat16), "heads", [(i, i ^ bit) for i in range(head_total)]
        )
        current = keep + got.astype(jnp.float32)
    return current.reshape(rows, width)


def gather_heads(piece, head_id, head_total):
    levels = level_count(head_total)
    rows, width = piece.shape
    current = piece
    for level in reversed(range(levels)):
        bit = 1 << level
        mine = (head_id >> level) & 1
        got = lax.ppermute(current, "heads", [(i, i ^ bit) for i in range(head_total)])
        low = jnp.where(mine == 0, current, got)
        high = jnp.where(mine == 0, got, current)
        current = jnp.stack([low, high], axis=current.ndim - 1)
    return current.reshape(rows, head_total * width)


def gather_levels(current, head_id, head_total, level_list):
    for level in level_list:
        bit = 1 << level
        mine = (head_id >> level) & 1
        got = lax.ppermute(current, "heads", [(i, i ^ bit) for i in range(head_total)])
        low = jnp.where(mine == 0, current, got)
        high = jnp.where(mine == 0, got, current)
        current = jnp.stack([low, high], axis=current.ndim - 1)
    return current


def absorb_block(state, query_heads, key_block, value_block, linked, head_count, brick_rows):
    row_max, row_mass, weighted = state
    key_rows = key_block.reshape(-1, head_count, HEAD_DIM)
    value_rows = value_block.reshape(-1, head_count, HEAD_DIM)
    scores = (
        jnp.einsum("bqhd,khd->bhqk", query_heads, key_rows, preferred_element_type=jnp.float32)
        * HEAD_DIM ** (-0.5)
    )
    keep = jnp.repeat(linked, brick_rows, axis=1, total_repeat_length=key_rows.shape[0])
    scores = jnp.where(keep[:, None, None, :], scores, -1e30)
    max_new = jnp.maximum(row_max, jnp.max(scores, axis=-1))
    factor = jnp.exp(row_max - max_new)
    weights = jnp.exp(scores - max_new[..., None])
    mass_new = row_mass * factor + jnp.sum(weights, axis=-1)
    sum_new = weighted * jnp.transpose(factor, (0, 2, 1))[..., None] + jnp.einsum(
        "bhqk,khd->bqhd", weights.astype(jnp.bfloat16), value_rows,
        preferred_element_type=jnp.float32,
    )
    return max_new, mass_new, sum_new


def shards(
    voxel_feats,
    face_open,
    pattern,
    conv_weight,
    conv_bias,
    gain_one,
    query_weight,
    key_weight,
    value_weight,
    out_weight,
    gain_two,
    up_weight,
    down_weight,
):
    row_count = voxel_feats.shape[0]
    local_width = voxel_feats.shape[1]
    face_rows = EDGE * EDGE
    brick_rows = EDGE * face_rows
    local_bricks = row_count // brick_rows
    brick_total = pattern.shape[0]
    first_brick = lax.axis_index("bricks") * local_bricks
    extended = extended_2(voxel_feats, (("bricks", 0),), face_rows)
    brick_vals = extended[face_rows : face_rows + row_count].astype(jnp.float32)
    brick_vals = brick_vals.reshape(local_bricks, EDGE, face_rows, local_width)
    lower_face = jnp.concatenate(
        [extended[:face_rows].astype(jnp.float32)[None], brick_vals[:-1, EDGE - 1]], axis=0
    )
    upper_face = jnp.concatenate(
        [brick_vals[1:, 0], extended[face_rows + row_count :].astype(jnp.float32)[None]], axis=0
    )
    brick_ids = first_brick + jnp.arange(local_bricks, dtype=jnp.int32)
    lower_open = jnp.where(brick_ids >= 1, jnp.take(face_open, brick_ids), 0)
    upper_open = jnp.where(
        brick_ids + 1 < brick_total,
        jnp.take(face_open, jnp.minimum(brick_ids + 1, brick_total - 1)),
        0,
    )
    lower_face = lower_face * lower_open.astype(jnp.float32)[:, None, None]
    upper_face = upper_face * upper_open.astype(jnp.float32)[:, None, None]
    conv_out = depthwise(brick_vals, lower_face, upper_face, conv_weight, conv_bias)
    stream = (voxel_feats.astype(jnp.float32) + conv_out).astype(jnp.bfloat16)
    head_total = lax.axis_size("heads")
    head_id = lax.axis_index("heads")
    head_count = local_width // HEAD_DIM
    brick_dev = lax.axis_index("bricks")
    dev_total = lax.axis_size("bricks")
    ring = [(i, (i + 1) % dev_total) for i in range(dev_total)]
    linked_rows = lax.dynamic_slice_in_dim(pattern, first_brick, local_bricks, 0)
    state = (
        jnp.full((local_bricks, head_count, brick_rows), -1e30, jnp.float32),
        jnp.zeros((local_bricks, head_count, brick_rows), jnp.float32),
        jnp.zeros((local_bricks, brick_rows, head_count, HEAD_DIM), jnp.float32),
    )
    chunk_count = 2 if row_count % 16 == 0 else 1
    chunk_rows = row_count // chunk_count
    split_last = local_bricks == 1 and chunk_count == 2
    levels = level_count(head_total)
    cross_levels = list(reversed(range(1, levels)))
    chip_levels = list(range(min(levels, 1)))
    ringed = {0: stream}
    crossed = {}
    gathered = {}
    query_heads = None
    for slot in range(dev_total + 2):
        made = []
        if 1 <= slot + 1 < dev_total:
            ringed[slot + 1] = lax.ppermute(ringed[slot], "bricks", ring)
            made.append((ringed, slot + 1))
        if slot < dev_total:
            crossed[slot] = gather_levels(ringed[slot], head_id, head_total, cross_levels)
            made.append((crossed, slot))
        if 0 <= slot - 1 < dev_total:
            gathered[slot - 1] = gather_levels(
                crossed[slot - 1], head_id, head_total, chip_levels
            ).reshape(row_count, head_total * local_width)
            made.append((gathered, slot - 1))
        step = slot - 2
        if 0 <= step < dev_total:
            normed_now = layer_norm(gathered[step], gain_one).astype(jnp.bfloat16)
            if step == 0:
                queries = jnp.dot(
                    normed_now, query_weight, preferred_element_type=jnp.float32
                ).astype(jnp.bfloat16)
                query_heads = queries.reshape(local_bricks, brick_rows, head_count, HEAD_DIM)
            key_block = jnp.dot(
                normed_now, key_weight, preferred_element_type=jnp.float32
            ).astype(jnp.bfloat16)
            value_block = jnp.dot(
                normed_now, value_weight, preferred_element_type=jnp.float32
            ).astype(jnp.bfloat16)
            source = (brick_dev - step) % dev_total
            key_ids = source * local_bricks + jnp.arange(local_bricks, dtype=jnp.int32)
            linked = jnp.take(linked_rows, key_ids, axis=1) > 0
            if step == dev_total - 1 and split_last:
                parts = []
                for half in range(chunk_count):
                    cut = slice(half * chunk_rows, (half + 1) * chunk_rows)
                    part = (state[0][:, :, cut], state[1][:, :, cut], state[2][:, cut])
                    parts.append(absorb_block(
                        part, query_heads[:, cut], key_block, value_block, linked, head_count,
                        brick_rows,
                    ))
                state = parts
            else:
                state = absorb_block(
                    state, query_heads, key_block, value_block, linked, head_count, brick_rows
                )
        if slot < dev_total + 1:
            packed = lax.optimization_barrier((state, [table[key] for table, key in made]))
            state = packed[0]
            for (table, key), value in zip(made, packed[1]):
                table[key] = value
    if not split_last:
        state = [state]
    attended_parts = []
    for row_max, row_mass, weighted in state:
        attended = weighted / jnp.transpose(row_mass, (0, 2, 1))[:, :, :, None]
        attended_parts.append(attended.astype(jnp.bfloat16).reshape(-1, local_width))
    attended = jnp.concatenate(attended_parts, axis=0) if not split_last else None
    outputs = []
    for chunk in range(chunk_count):
        rows = slice(chunk * chunk_rows, (chunk + 1) * chunk_rows)
        attended_rows = attended_parts[chunk] if split_last else attended[rows]
        partial_out = jnp.dot(attended_rows, out_weight, preferred_element_type=jnp.float32)
        out_sum = scatter_heads(partial_out, head_id, head_total)
        stream_two = (stream[rows].astype(jnp.float32) + out_sum).astype(jnp.bfloat16)
        stream_two_full = gather_heads(stream_two, head_id, head_total)
        normed_two = lax.optimization_barrier(
            layer_norm(stream_two_full, gain_two).astype(jnp.bfloat16)
        )
        hidden = jax.nn.gelu(
            jnp.dot(normed_two, up_weight, preferred_element_type=jnp.float32), approximate=True
        ).astype(jnp.bfloat16)
        hidden = lax.optimization_barrier(hidden)
        lowered = jnp.dot(hidden, down_weight, preferred_element_type=jnp.float32)
        mixed = scatter_heads(lowered, head_id, head_total)
        outputs.append((stream_two.astype(jnp.float32) + mixed).astype(jnp.bfloat16))
    return jnp.concatenate(outputs, axis=0)

def solution(mesh):
    return jax.shard_map(
        shards,
        mesh=mesh,
        in_specs=(
            P(("groups", "bricks"), "heads"),
            P("groups"),
            P("groups", None),
            P(None, "heads"),
            P("heads"),
            P(),
            P(None, "heads"),
            P(None, "heads"),
            P(None, "heads"),
            P("heads", None),
            P(),
            P(None, "heads"),
            P("heads", None),
        ),
        out_specs=P(("groups", "bricks"), "heads"),
        check_vma=False,
    )
```

```python
import jax
import jax.numpy as jnp
from jax import lax
from jax.sharding import PartitionSpec as P

EDGE = 8
HEAD_DIM = 64


epsilon = 1e-05


def extended_2(value, sides, width):
    for axis, dim in sides:
        size, length = (lax.axis_size(axis), value.shape[dim])
        up = [(i, (i + 1) % size) for i in range(size - 1)]
        down = [(j, i) for i, j in up]
        last = lax.slice_in_dim(value, length - width, length, axis=dim)
        first = lax.slice_in_dim(value, 0, width, axis=dim)
        before = lax.ppermute(last, axis, up)
        after = lax.ppermute(first, axis, down)
        value = jnp.concatenate([before, value, after], axis=dim)
    return value


def layer_norm(inputs, gain_vec):
    values = inputs.astype(jnp.float32)
    center = values - jnp.mean(values, axis=-1, keepdims=True)
    spread = jnp.mean(center * center, axis=-1, keepdims=True)
    return center * lax.rsqrt(spread + epsilon) * gain_vec.astype(jnp.float32)


def depthwise(brick_vals, lower_face, upper_face, conv_weight, conv_bias):
    brick_count = brick_vals.shape[0]
    edge_len = brick_vals.shape[1]
    channels = brick_vals.shape[3]
    layers = jnp.concatenate([lower_face[:, None], brick_vals, upper_face[:, None]], axis=1)
    layers = layers.reshape(brick_count, edge_len + 2, edge_len, edge_len, channels)
    padded = jnp.pad(layers, ((0, 0), (0, 0), (1, 1), (1, 1), (0, 0)))
    weights = conv_weight.astype(jnp.float32)
    summed = jnp.zeros((brick_count, edge_len, edge_len, edge_len, channels), jnp.float32)
    for step_x in range(3):
        for step_y in range(3):
            for step_z in range(3):
                window = padded[
                    :,
                    step_x : step_x + edge_len,
                    step_y : step_y + edge_len,
                    step_z : step_z + edge_len,
                ]
                summed = summed + weights[step_x * 9 + step_y * 3 + step_z] * window
    return summed.reshape(brick_count * edge_len**3, channels) + conv_bias.astype(jnp.float32)


def level_count(total):
    levels = total.bit_length() - 1
    assert 1 << levels == total
    return levels


def scatter_heads(partial, head_id, head_total):
    levels = level_count(head_total)
    rows = partial.shape[0]
    width = partial.shape[1] // head_total
    current = partial.reshape((rows,) + (2,) * levels + (width,))
    for level in range(levels):
        bit = 1 << level
        axis = levels - level
        mine = (head_id >> level) & 1
        keep = lax.dynamic_index_in_dim(current, mine, axis, keepdims=False)
        give = lax.dynamic_index_in_dim(current, 1 - mine, axis, keepdims=False)
        got = lax.ppermute(
            give.astype(jnp.bfloat16), "heads", [(i, i ^ bit) for i in range(head_total)]
        )
        current = keep + got.astype(jnp.float32)
    return current.reshape(rows, width)


def gather_heads(piece, head_id, head_total):
    levels = level_count(head_total)
    rows, width = piece.shape
    current = piece
    for level in reversed(range(levels)):
        bit = 1 << level
        mine = (head_id >> level) & 1
        got = lax.ppermute(current, "heads", [(i, i ^ bit) for i in range(head_total)])
        low = jnp.where(mine == 0, current, got)
        high = jnp.where(mine == 0, got, current)
        current = jnp.stack([low, high], axis=current.ndim - 1)
    return current.reshape(rows, head_total * width)


def gather_levels(current, head_id, head_total, level_list):
    for level in level_list:
        bit = 1 << level
        mine = (head_id >> level) & 1
        got = lax.ppermute(current, "heads", [(i, i ^ bit) for i in range(head_total)])
        low = jnp.where(mine == 0, current, got)
        high = jnp.where(mine == 0, got, current)
        current = jnp.stack([low, high], axis=current.ndim - 1)
    return current


def absorb_block(state, query_heads, key_block, value_block, linked, head_count, brick_rows):
    row_max, row_mass, weighted = state
    key_rows = key_block.reshape(-1, head_count, HEAD_DIM)
    value_rows = value_block.reshape(-1, head_count, HEAD_DIM)
    scores = (
        jnp.einsum("bqhd,khd->bhqk", query_heads, key_rows, preferred_element_type=jnp.float32)
        * HEAD_DIM ** (-0.5)
    )
    keep = jnp.repeat(linked, brick_rows, axis=1, total_repeat_length=key_rows.shape[0])
    scores = jnp.where(keep[:, None, None, :], scores, -1e30)
    max_new = jnp.maximum(row_max, jnp.max(scores, axis=-1))
    factor = jnp.exp(row_max - max_new)
    weights = jnp.exp(scores - max_new[..., None])
    mass_new = row_mass * factor + jnp.sum(weights, axis=-1)
    sum_new = weighted * jnp.transpose(factor, (0, 2, 1))[..., None] + jnp.einsum(
        "bhqk,khd->bqhd", weights.astype(jnp.bfloat16), value_rows,
        preferred_element_type=jnp.float32,
    )
    return max_new, mass_new, sum_new


def shards(
    voxel_feats,
    face_open,
    pattern,
    conv_weight,
    conv_bias,
    gain_one,
    query_weight,
    key_weight,
    value_weight,
    out_weight,
    gain_two,
    up_weight,
    down_weight,
):
    row_count = voxel_feats.shape[0]
    local_width = voxel_feats.shape[1]
    face_rows = EDGE * EDGE
    brick_rows = EDGE * face_rows
    local_bricks = row_count // brick_rows
    brick_total = pattern.shape[0]
    first_brick = lax.axis_index("bricks") * local_bricks
    extended = extended_2(voxel_feats, (("bricks", 0),), face_rows)
    brick_vals = extended[face_rows : face_rows + row_count].astype(jnp.float32)
    brick_vals = brick_vals.reshape(local_bricks, EDGE, face_rows, local_width)
    lower_face = jnp.concatenate(
        [extended[:face_rows].astype(jnp.float32)[None], brick_vals[:-1, EDGE - 1]], axis=0
    )
    upper_face = jnp.concatenate(
        [brick_vals[1:, 0], extended[face_rows + row_count :].astype(jnp.float32)[None]], axis=0
    )
    brick_ids = first_brick + jnp.arange(local_bricks, dtype=jnp.int32)
    lower_open = jnp.where(brick_ids >= 1, jnp.take(face_open, brick_ids), 0)
    upper_open = jnp.where(
        brick_ids + 1 < brick_total,
        jnp.take(face_open, jnp.minimum(brick_ids + 1, brick_total - 1)),
        0,
    )
    lower_face = lower_face * lower_open.astype(jnp.float32)[:, None, None]
    upper_face = upper_face * upper_open.astype(jnp.float32)[:, None, None]
    conv_out = depthwise(brick_vals, lower_face, upper_face, conv_weight, conv_bias)
    stream = (voxel_feats.astype(jnp.float32) + conv_out).astype(jnp.bfloat16)
    head_total = lax.axis_size("heads")
    head_id = lax.axis_index("heads")
    head_count = local_width // HEAD_DIM
    brick_dev = lax.axis_index("bricks")
    dev_total = lax.axis_size("bricks")
    ring = [(i, (i + 1) % dev_total) for i in range(dev_total)]
    linked_rows = lax.dynamic_slice_in_dim(pattern, first_brick, local_bricks, 0)
    state = (
        jnp.full((local_bricks, head_count, brick_rows), -1e30, jnp.float32),
        jnp.zeros((local_bricks, head_count, brick_rows), jnp.float32),
        jnp.zeros((local_bricks, brick_rows, head_count, HEAD_DIM), jnp.float32),
    )
    chunk_count = 2 if row_count % 16 == 0 else 1
    chunk_rows = row_count // chunk_count
    split_last = local_bricks == 1 and chunk_count == 2
    levels = level_count(head_total)
    cross_levels = list(reversed(range(1, levels)))
    chip_levels = list(range(min(levels, 1)))
    ringed = {0: stream}
    crossed = {}
    gathered = {}
    query_heads = None
    for slot in range(dev_total + 2):
        made = []
        if 1 <= slot + 1 < dev_total:
            ringed[slot + 1] = lax.ppermute(ringed[slot], "bricks", ring)
            made.append((ringed, slot + 1))
        if slot < dev_total:
            crossed[slot] = gather_levels(ringed[slot], head_id, head_total, cross_levels)
            made.append((crossed, slot))
        if 0 <= slot - 1 < dev_total:
            gathered[slot - 1] = gather_levels(
                crossed[slot - 1], head_id, head_total, chip_levels
            ).reshape(row_count, head_total * local_width)
            made.append((gathered, slot - 1))
        step = slot - 2
        if 0 <= step < dev_total:
            normed_now = layer_norm(gathered[step], gain_one).astype(jnp.bfloat16)
            if step == 0:
                queries = jnp.dot(
                    normed_now, query_weight, preferred_element_type=jnp.float32
                ).astype(jnp.bfloat16)
                query_heads = queries.reshape(local_bricks, brick_rows, head_count, HEAD_DIM)
            key_block = jnp.dot(
                normed_now, key_weight, preferred_element_type=jnp.float32
            ).astype(jnp.bfloat16)
            value_block = jnp.dot(
                normed_now, value_weight, preferred_element_type=jnp.float32
            ).astype(jnp.bfloat16)
            source = (brick_dev - step) % dev_total
            key_ids = source * local_bricks + jnp.arange(local_bricks, dtype=jnp.int32)
            linked = jnp.take(linked_rows, key_ids, axis=1) > 0
            if step == dev_total - 1 and split_last:
                parts = []
                for half in range(chunk_count):
                    cut = slice(half * chunk_rows, (half + 1) * chunk_rows)
                    part = (state[0][:, :, cut], state[1][:, :, cut], state[2][:, cut])
                    parts.append(absorb_block(
                        part, query_heads[:, cut], key_block, value_block, linked, head_count,
                        brick_rows,
                    ))
                state = parts
            else:
                state = absorb_block(
                    state, query_heads, key_block, value_block, linked, head_count, brick_rows
                )
        if slot < dev_total + 1:
            packed = lax.optimization_barrier((state, [table[key] for table, key in made]))
            state = packed[0]
            for (table, key), value in zip(made, packed[1]):
                table[key] = value
    if not split_last:
        state = [state]
    attended_parts = []
    for row_max, row_mass, weighted in state:
        attended = weighted / jnp.transpose(row_mass, (0, 2, 1))[:, :, :, None]
        attended_parts.append(attended.astype(jnp.bfloat16).reshape(-1, local_width))
    attended = jnp.concatenate(attended_parts, axis=0) if not split_last else None
    outputs = []
    for chunk in range(chunk_count):
        rows = slice(chunk * chunk_rows, (chunk + 1) * chunk_rows)
        attended_rows = attended_parts[chunk] if split_last else attended[rows]
        partial_out = jnp.dot(attended_rows, out_weight, preferred_element_type=jnp.float32)
        out_sum = scatter_heads(partial_out, head_id, head_total)
        stream_two = (stream[rows].astype(jnp.float32) + out_sum).astype(jnp.bfloat16)
        stream_two_full = gather_heads(stream_two, head_id, head_total)
        normed_two = layer_norm(stream_two_full, gain_two).astype(jnp.bfloat16)
        hidden = jax.nn.gelu(
            jnp.dot(normed_two, up_weight, preferred_element_type=jnp.float32), approximate=True
        ).astype(jnp.bfloat16)
        hidden = lax.optimization_barrier(hidden)
        lowered = jnp.dot(hidden, down_weight, preferred_element_type=jnp.float32)
        mixed = scatter_heads(lowered, head_id, head_total)
        outputs.append((stream_two, mixed))
    two_rows = jnp.concatenate([two for two, _ in outputs], axis=0)
    mixed_rows = jnp.concatenate([mix for _, mix in outputs], axis=0)
    return (two_rows.astype(jnp.float32) + mixed_rows).astype(jnp.bfloat16)

def solution(mesh):
    return jax.shard_map(
        shards,
        mesh=mesh,
        in_specs=(
            P(("groups", "bricks"), "heads"),
            P("groups"),
            P("groups", None),
            P(None, "heads"),
            P("heads"),
            P(),
            P(None, "heads"),
            P(None, "heads"),
            P(None, "heads"),
            P("heads", None),
            P(),
            P(None, "heads"),
            P("heads", None),
        ),
        out_specs=P(("groups", "bricks"), "heads"),
        check_vma=False,
    )
```

```python
import jax
import jax.numpy as jnp
from jax import lax
from jax.sharding import PartitionSpec as P

EDGE = 8
HEAD_DIM = 64


epsilon = 1e-05


def extended_2(value, sides, width):
    for axis, dim in sides:
        size, length = (lax.axis_size(axis), value.shape[dim])
        up = [(i, (i + 1) % size) for i in range(size - 1)]
        down = [(j, i) for i, j in up]
        last = lax.slice_in_dim(value, length - width, length, axis=dim)
        first = lax.slice_in_dim(value, 0, width, axis=dim)
        before = lax.ppermute(last, axis, up)
        after = lax.ppermute(first, axis, down)
        value = jnp.concatenate([before, value, after], axis=dim)
    return value


def layer_norm(inputs, gain_vec):
    values = inputs.astype(jnp.float32)
    center = values - jnp.mean(values, axis=-1, keepdims=True)
    spread = jnp.mean(center * center, axis=-1, keepdims=True)
    return center * lax.rsqrt(spread + epsilon) * gain_vec.astype(jnp.float32)


def depthwise(brick_vals, lower_face, upper_face, conv_weight, conv_bias):
    brick_count = brick_vals.shape[0]
    edge_len = brick_vals.shape[1]
    channels = brick_vals.shape[3]
    layers = jnp.concatenate([lower_face[:, None], brick_vals, upper_face[:, None]], axis=1)
    layers = layers.reshape(brick_count, edge_len + 2, edge_len, edge_len, channels)
    padded = jnp.pad(layers, ((0, 0), (0, 0), (1, 1), (1, 1), (0, 0)))
    weights = conv_weight.astype(jnp.float32)
    summed = jnp.zeros((brick_count, edge_len, edge_len, edge_len, channels), jnp.float32)
    for step_x in range(3):
        for step_y in range(3):
            for step_z in range(3):
                window = padded[
                    :,
                    step_x : step_x + edge_len,
                    step_y : step_y + edge_len,
                    step_z : step_z + edge_len,
                ]
                summed = summed + weights[step_x * 9 + step_y * 3 + step_z] * window
    return summed.reshape(brick_count * edge_len**3, channels) + conv_bias.astype(jnp.float32)


def level_count(total):
    levels = total.bit_length() - 1
    assert 1 << levels == total
    return levels


def scatter_heads(partial, head_id, head_total):
    levels = level_count(head_total)
    rows = partial.shape[0]
    width = partial.shape[1] // head_total
    current = partial.reshape((rows,) + (2,) * levels + (width,))
    for level in range(levels):
        bit = 1 << level
        axis = levels - level
        mine = (head_id >> level) & 1
        keep = lax.dynamic_index_in_dim(current, mine, axis, keepdims=False)
        give = lax.dynamic_index_in_dim(current, 1 - mine, axis, keepdims=False)
        got = lax.ppermute(
            give.astype(jnp.bfloat16), "heads", [(i, i ^ bit) for i in range(head_total)]
        )
        current = keep + got.astype(jnp.float32)
    return current.reshape(rows, width)


def gather_heads(piece, head_id, head_total):
    levels = level_count(head_total)
    rows, width = piece.shape
    current = piece
    for level in reversed(range(levels)):
        bit = 1 << level
        mine = (head_id >> level) & 1
        got = lax.ppermute(current, "heads", [(i, i ^ bit) for i in range(head_total)])
        low = jnp.where(mine == 0, current, got)
        high = jnp.where(mine == 0, got, current)
        current = jnp.stack([low, high], axis=current.ndim - 1)
    return current.reshape(rows, head_total * width)


def gather_levels(current, head_id, head_total, level_list):
    for level in level_list:
        bit = 1 << level
        mine = (head_id >> level) & 1
        got = lax.ppermute(current, "heads", [(i, i ^ bit) for i in range(head_total)])
        low = jnp.where(mine == 0, current, got)
        high = jnp.where(mine == 0, got, current)
        current = jnp.stack([low, high], axis=current.ndim - 1)
    return current


def absorb_block(state, query_heads, key_block, value_block, linked, head_count, brick_rows):
    row_max, row_mass, weighted = state
    key_rows = key_block.reshape(-1, head_count, HEAD_DIM)
    value_rows = value_block.reshape(-1, head_count, HEAD_DIM)
    scores = (
        jnp.einsum("bqhd,khd->bhqk", query_heads, key_rows, preferred_element_type=jnp.float32)
        * HEAD_DIM ** (-0.5)
    )
    keep = jnp.repeat(linked, brick_rows, axis=1, total_repeat_length=key_rows.shape[0])
    scores = jnp.where(keep[:, None, None, :], scores, -1e30)
    max_new = jnp.maximum(row_max, jnp.max(scores, axis=-1))
    factor = jnp.exp(row_max - max_new)
    weights = jnp.exp(scores - max_new[..., None])
    mass_new = row_mass * factor + jnp.sum(weights, axis=-1)
    sum_new = weighted * jnp.transpose(factor, (0, 2, 1))[..., None] + jnp.einsum(
        "bhqk,khd->bqhd", weights.astype(jnp.bfloat16), value_rows,
        preferred_element_type=jnp.float32,
    )
    return max_new, mass_new, sum_new


def shards(
    voxel_feats,
    face_open,
    pattern,
    conv_weight,
    conv_bias,
    gain_one,
    query_weight,
    key_weight,
    value_weight,
    out_weight,
    gain_two,
    up_weight,
    down_weight,
):
    row_count = voxel_feats.shape[0]
    local_width = voxel_feats.shape[1]
    face_rows = EDGE * EDGE
    brick_rows = EDGE * face_rows
    local_bricks = row_count // brick_rows
    brick_total = pattern.shape[0]
    first_brick = lax.axis_index("bricks") * local_bricks
    extended = extended_2(voxel_feats, (("bricks", 0),), face_rows)
    brick_vals = extended[face_rows : face_rows + row_count].astype(jnp.float32)
    brick_vals = brick_vals.reshape(local_bricks, EDGE, face_rows, local_width)
    lower_face = jnp.concatenate(
        [extended[:face_rows].astype(jnp.float32)[None], brick_vals[:-1, EDGE - 1]], axis=0
    )
    upper_face = jnp.concatenate(
        [brick_vals[1:, 0], extended[face_rows + row_count :].astype(jnp.float32)[None]], axis=0
    )
    brick_ids = first_brick + jnp.arange(local_bricks, dtype=jnp.int32)
    lower_open = jnp.where(brick_ids >= 1, jnp.take(face_open, brick_ids), 0)
    upper_open = jnp.where(
        brick_ids + 1 < brick_total,
        jnp.take(face_open, jnp.minimum(brick_ids + 1, brick_total - 1)),
        0,
    )
    lower_face = lower_face * lower_open.astype(jnp.float32)[:, None, None]
    upper_face = upper_face * upper_open.astype(jnp.float32)[:, None, None]
    conv_out = depthwise(brick_vals, lower_face, upper_face, conv_weight, conv_bias)
    stream = (voxel_feats.astype(jnp.float32) + conv_out).astype(jnp.bfloat16)
    head_total = lax.axis_size("heads")
    head_id = lax.axis_index("heads")
    head_count = local_width // HEAD_DIM
    brick_dev = lax.axis_index("bricks")
    dev_total = lax.axis_size("bricks")
    ring = [(i, (i + 1) % dev_total) for i in range(dev_total)]
    linked_rows = lax.dynamic_slice_in_dim(pattern, first_brick, local_bricks, 0)
    state = (
        jnp.full((local_bricks, head_count, brick_rows), -1e30, jnp.float32),
        jnp.zeros((local_bricks, head_count, brick_rows), jnp.float32),
        jnp.zeros((local_bricks, brick_rows, head_count, HEAD_DIM), jnp.float32),
    )
    chunk_count = 1
    chunk_rows = row_count // chunk_count
    split_last = local_bricks == 1 and chunk_count == 2
    levels = level_count(head_total)
    cross_levels = list(reversed(range(1, levels)))
    chip_levels = list(range(min(levels, 1)))
    ringed = {0: stream}
    crossed = {}
    gathered = {}
    query_heads = None
    for slot in range(dev_total + 2):
        made = []
        if 1 <= slot + 1 < dev_total:
            ringed[slot + 1] = lax.ppermute(ringed[slot], "bricks", ring)
            made.append((ringed, slot + 1))
        if slot < dev_total:
            crossed[slot] = gather_levels(ringed[slot], head_id, head_total, cross_levels)
            made.append((crossed, slot))
        if 0 <= slot - 1 < dev_total:
            gathered[slot - 1] = gather_levels(
                crossed[slot - 1], head_id, head_total, chip_levels
            ).reshape(row_count, head_total * local_width)
            made.append((gathered, slot - 1))
        step = slot - 2
        if 0 <= step < dev_total:
            normed_now = layer_norm(gathered[step], gain_one).astype(jnp.bfloat16)
            if step == 0:
                queries = jnp.dot(
                    normed_now, query_weight, preferred_element_type=jnp.float32
                ).astype(jnp.bfloat16)
                query_heads = queries.reshape(local_bricks, brick_rows, head_count, HEAD_DIM)
            key_block = jnp.dot(
                normed_now, key_weight, preferred_element_type=jnp.float32
            ).astype(jnp.bfloat16)
            value_block = jnp.dot(
                normed_now, value_weight, preferred_element_type=jnp.float32
            ).astype(jnp.bfloat16)
            source = (brick_dev - step) % dev_total
            key_ids = source * local_bricks + jnp.arange(local_bricks, dtype=jnp.int32)
            linked = jnp.take(linked_rows, key_ids, axis=1) > 0
            if step == dev_total - 1 and split_last:
                parts = []
                for half in range(chunk_count):
                    cut = slice(half * chunk_rows, (half + 1) * chunk_rows)
                    part = (state[0][:, :, cut], state[1][:, :, cut], state[2][:, cut])
                    parts.append(absorb_block(
                        part, query_heads[:, cut], key_block, value_block, linked, head_count,
                        brick_rows,
                    ))
                state = parts
            else:
                state = absorb_block(
                    state, query_heads, key_block, value_block, linked, head_count, brick_rows
                )
        if slot < dev_total + 1:
            packed = lax.optimization_barrier((state, [table[key] for table, key in made]))
            state = packed[0]
            for (table, key), value in zip(made, packed[1]):
                table[key] = value
    if not split_last:
        state = [state]
    attended_parts = []
    for row_max, row_mass, weighted in state:
        attended = weighted / jnp.transpose(row_mass, (0, 2, 1))[:, :, :, None]
        attended_parts.append(attended.astype(jnp.bfloat16).reshape(-1, local_width))
    attended = jnp.concatenate(attended_parts, axis=0) if not split_last else None
    outputs = []
    for chunk in range(chunk_count):
        rows = slice(chunk * chunk_rows, (chunk + 1) * chunk_rows)
        attended_rows = attended_parts[chunk] if split_last else attended[rows]
        partial_out = jnp.dot(attended_rows, out_weight, preferred_element_type=jnp.float32)
        out_sum = scatter_heads(partial_out, head_id, head_total)
        stream_two = (stream[rows].astype(jnp.float32) + out_sum).astype(jnp.bfloat16)
        stream_two_full = gather_heads(stream_two, head_id, head_total)
        normed_two = layer_norm(stream_two_full, gain_two).astype(jnp.bfloat16)
        hidden = jax.nn.gelu(
            jnp.dot(normed_two, up_weight, preferred_element_type=jnp.float32), approximate=True
        ).astype(jnp.bfloat16)
        hidden = lax.optimization_barrier(hidden)
        lowered = jnp.dot(hidden, down_weight, preferred_element_type=jnp.float32)
        mixed = scatter_heads(lowered, head_id, head_total)
        outputs.append((stream_two.astype(jnp.float32) + mixed).astype(jnp.bfloat16))
    return jnp.concatenate(outputs, axis=0)

def solution(mesh):
    return jax.shard_map(
        shards,
        mesh=mesh,
        in_specs=(
            P(("groups", "bricks"), "heads"),
            P("groups"),
            P("groups", None),
            P(None, "heads"),
            P("heads"),
            P(),
            P(None, "heads"),
            P(None, "heads"),
            P(None, "heads"),
            P("heads", None),
            P(),
            P(None, "heads"),
            P("heads", None),
        ),
        out_specs=P(("groups", "bricks"), "heads"),
        check_vma=False,
    )
```

```python
import jax
import jax.numpy as jnp
from jax import lax
from jax.sharding import PartitionSpec as P

EDGE = 8
HEAD_DIM = 64


epsilon = 1e-05


def extended_2(value, sides, width):
    for axis, dim in sides:
        size, length = (lax.axis_size(axis), value.shape[dim])
        up = [(i, (i + 1) % size) for i in range(size - 1)]
        down = [(j, i) for i, j in up]
        last = lax.slice_in_dim(value, length - width, length, axis=dim)
        first = lax.slice_in_dim(value, 0, width, axis=dim)
        before = lax.ppermute(last, axis, up)
        after = lax.ppermute(first, axis, down)
        value = jnp.concatenate([before, value, after], axis=dim)
    return value


def layer_norm(inputs, gain_vec):
    values = inputs.astype(jnp.float32)
    center = values - jnp.mean(values, axis=-1, keepdims=True)
    spread = jnp.mean(center * center, axis=-1, keepdims=True)
    return center * lax.rsqrt(spread + epsilon) * gain_vec.astype(jnp.float32)


def depthwise(brick_vals, lower_face, upper_face, conv_weight, conv_bias):
    brick_count = brick_vals.shape[0]
    edge_len = brick_vals.shape[1]
    channels = brick_vals.shape[3]
    layers = jnp.concatenate([lower_face[:, None], brick_vals, upper_face[:, None]], axis=1)
    layers = layers.reshape(brick_count, edge_len + 2, edge_len, edge_len, channels)
    padded = jnp.pad(layers, ((0, 0), (0, 0), (1, 1), (1, 1), (0, 0)))
    weights = conv_weight.astype(jnp.float32)
    summed = jnp.zeros((brick_count, edge_len, edge_len, edge_len, channels), jnp.float32)
    for step_x in range(3):
        for step_y in range(3):
            for step_z in range(3):
                window = padded[
                    :,
                    step_x : step_x + edge_len,
                    step_y : step_y + edge_len,
                    step_z : step_z + edge_len,
                ]
                summed = summed + weights[step_x * 9 + step_y * 3 + step_z] * window
    return summed.reshape(brick_count * edge_len**3, channels) + conv_bias.astype(jnp.float32)


def level_count(total):
    levels = total.bit_length() - 1
    assert 1 << levels == total
    return levels


def scatter_heads(partial, head_id, head_total):
    levels = level_count(head_total)
    rows = partial.shape[0]
    width = partial.shape[1] // head_total
    current = partial.reshape((rows,) + (2,) * levels + (width,))
    for level in range(levels):
        bit = 1 << level
        axis = levels - level
        mine = (head_id >> level) & 1
        keep = lax.dynamic_index_in_dim(current, mine, axis, keepdims=False)
        give = lax.dynamic_index_in_dim(current, 1 - mine, axis, keepdims=False)
        got = lax.ppermute(
            give.astype(jnp.bfloat16), "heads", [(i, i ^ bit) for i in range(head_total)]
        )
        current = keep + got.astype(jnp.float32)
    return current.reshape(rows, width)


def gather_heads(piece, head_id, head_total):
    levels = level_count(head_total)
    rows, width = piece.shape
    current = piece
    for level in reversed(range(levels)):
        bit = 1 << level
        mine = (head_id >> level) & 1
        got = lax.ppermute(current, "heads", [(i, i ^ bit) for i in range(head_total)])
        low = jnp.where(mine == 0, current, got)
        high = jnp.where(mine == 0, got, current)
        current = jnp.stack([low, high], axis=current.ndim - 1)
    return current.reshape(rows, head_total * width)


def gather_levels(current, head_id, head_total, level_list):
    for level in level_list:
        bit = 1 << level
        mine = (head_id >> level) & 1
        got = lax.ppermute(current, "heads", [(i, i ^ bit) for i in range(head_total)])
        low = jnp.where(mine == 0, current, got)
        high = jnp.where(mine == 0, got, current)
        current = jnp.stack([low, high], axis=current.ndim - 1)
    return current


def absorb_block(state, query_heads, key_block, value_block, linked, head_count, brick_rows):
    row_max, row_mass, weighted = state
    key_rows = key_block.reshape(-1, head_count, HEAD_DIM)
    value_rows = value_block.reshape(-1, head_count, HEAD_DIM)
    scores = (
        jnp.einsum("bqhd,khd->bhqk", query_heads, key_rows, preferred_element_type=jnp.float32)
        * HEAD_DIM ** (-0.5)
    )
    keep = jnp.repeat(linked, brick_rows, axis=1, total_repeat_length=key_rows.shape[0])
    scores = jnp.where(keep[:, None, None, :], scores, -1e30)
    max_new = jnp.maximum(row_max, jnp.max(scores, axis=-1))
    factor = jnp.exp(row_max - max_new)
    weights = jnp.exp(scores - max_new[..., None])
    mass_new = row_mass * factor + jnp.sum(weights, axis=-1)
    sum_new = weighted * jnp.transpose(factor, (0, 2, 1))[..., None] + jnp.einsum(
        "bhqk,khd->bqhd", weights.astype(jnp.bfloat16), value_rows,
        preferred_element_type=jnp.float32,
    )
    return max_new, mass_new, sum_new


def shards(
    voxel_feats,
    face_open,
    pattern,
    conv_weight,
    conv_bias,
    gain_one,
    query_weight,
    key_weight,
    value_weight,
    out_weight,
    gain_two,
    up_weight,
    down_weight,
):
    row_count = voxel_feats.shape[0]
    local_width = voxel_feats.shape[1]
    face_rows = EDGE * EDGE
    brick_rows = EDGE * face_rows
    local_bricks = row_count // brick_rows
    brick_total = pattern.shape[0]
    first_brick = lax.axis_index("bricks") * local_bricks
    extended = extended_2(voxel_feats, (("bricks", 0),), face_rows)
    brick_vals = extended[face_rows : face_rows + row_count].astype(jnp.float32)
    brick_vals = brick_vals.reshape(local_bricks, EDGE, face_rows, local_width)
    lower_face = jnp.concatenate(
        [extended[:face_rows].astype(jnp.float32)[None], brick_vals[:-1, EDGE - 1]], axis=0
    )
    upper_face = jnp.concatenate(
        [brick_vals[1:, 0], extended[face_rows + row_count :].astype(jnp.float32)[None]], axis=0
    )
    brick_ids = first_brick + jnp.arange(local_bricks, dtype=jnp.int32)
    lower_open = jnp.where(brick_ids >= 1, jnp.take(face_open, brick_ids), 0)
    upper_open = jnp.where(
        brick_ids + 1 < brick_total,
        jnp.take(face_open, jnp.minimum(brick_ids + 1, brick_total - 1)),
        0,
    )
    lower_face = lower_face * lower_open.astype(jnp.float32)[:, None, None]
    upper_face = upper_face * upper_open.astype(jnp.float32)[:, None, None]
    conv_out = depthwise(brick_vals, lower_face, upper_face, conv_weight, conv_bias)
    stream = (voxel_feats.astype(jnp.float32) + conv_out).astype(jnp.bfloat16)
    head_total = lax.axis_size("heads")
    head_id = lax.axis_index("heads")
    head_count = local_width // HEAD_DIM
    brick_dev = lax.axis_index("bricks")
    dev_total = lax.axis_size("bricks")
    ring = [(i, (i + 1) % dev_total) for i in range(dev_total)]
    linked_rows = lax.dynamic_slice_in_dim(pattern, first_brick, local_bricks, 0)
    state = (
        jnp.full((local_bricks, head_count, brick_rows), -1e30, jnp.float32),
        jnp.zeros((local_bricks, head_count, brick_rows), jnp.float32),
        jnp.zeros((local_bricks, brick_rows, head_count, HEAD_DIM), jnp.float32),
    )
    chunk_count = 2 if row_count % 16 == 0 else 1
    chunk_rows = row_count // chunk_count
    split_last = local_bricks == 1 and chunk_count == 2
    levels = level_count(head_total)
    cross_levels = list(reversed(range(1, levels)))
    chip_levels = list(range(min(levels, 1)))
    ringed = {0: stream}
    crossed = {}
    gathered = {}
    query_heads = None
    for slot in range(dev_total + 2):
        made = []
        if 1 <= slot + 1 < dev_total:
            ringed[slot + 1] = lax.ppermute(ringed[slot], "bricks", ring)
            made.append((ringed, slot + 1))
        if slot < dev_total:
            crossed[slot] = gather_levels(ringed[slot], head_id, head_total, cross_levels)
            made.append((crossed, slot))
        if 0 <= slot - 1 < dev_total:
            gathered[slot - 1] = gather_levels(
                crossed[slot - 1], head_id, head_total, chip_levels
            ).reshape(row_count, head_total * local_width)
            made.append((gathered, slot - 1))
        step = slot - 2
        if 0 <= step < dev_total:
            normed_now = layer_norm(gathered[step], gain_one).astype(jnp.bfloat16)
            if step == 0:
                queries = jnp.dot(
                    normed_now, query_weight, preferred_element_type=jnp.float32
                ).astype(jnp.bfloat16)
                query_heads = queries.reshape(local_bricks, brick_rows, head_count, HEAD_DIM)
            key_block = jnp.dot(
                normed_now, key_weight, preferred_element_type=jnp.float32
            ).astype(jnp.bfloat16)
            value_block = jnp.dot(
                normed_now, value_weight, preferred_element_type=jnp.float32
            ).astype(jnp.bfloat16)
            source = (brick_dev - step) % dev_total
            key_ids = source * local_bricks + jnp.arange(local_bricks, dtype=jnp.int32)
            linked = jnp.take(linked_rows, key_ids, axis=1) > 0
            if step == dev_total - 1 and split_last:
                parts = []
                for half in range(chunk_count):
                    cut = slice(half * chunk_rows, (half + 1) * chunk_rows)
                    part = (state[0][:, :, cut], state[1][:, :, cut], state[2][:, cut])
                    parts.append(absorb_block(
                        part, query_heads[:, cut], key_block, value_block, linked, head_count,
                        brick_rows,
                    ))
                state = parts
            else:
                state = absorb_block(
                    state, query_heads, key_block, value_block, linked, head_count, brick_rows
                )
        if slot < dev_total + 1:
            packed = lax.optimization_barrier((state, [table[key] for table, key in made]))
            state = packed[0]
            for (table, key), value in zip(made, packed[1]):
                table[key] = value
    if not split_last:
        state = [state]
    attended_parts = []
    for row_max, row_mass, weighted in state:
        attended = weighted / jnp.transpose(row_mass, (0, 2, 1))[:, :, :, None]
        attended_parts.append(
            lax.optimization_barrier(attended.astype(jnp.bfloat16).reshape(-1, local_width))
        )
    attended = jnp.concatenate(attended_parts, axis=0) if not split_last else None
    outputs = []
    for chunk in range(chunk_count):
        rows = slice(chunk * chunk_rows, (chunk + 1) * chunk_rows)
        attended_rows = attended_parts[chunk] if split_last else attended[rows]
        partial_out = jnp.dot(attended_rows, out_weight, preferred_element_type=jnp.float32)
        out_sum = scatter_heads(partial_out, head_id, head_total)
        stream_two = (stream[rows].astype(jnp.float32) + out_sum).astype(jnp.bfloat16)
        stream_two_full = gather_heads(stream_two, head_id, head_total)
        normed_two = layer_norm(stream_two_full, gain_two).astype(jnp.bfloat16)
        hidden = jax.nn.gelu(
            jnp.dot(normed_two, up_weight, preferred_element_type=jnp.float32), approximate=True
        ).astype(jnp.bfloat16)
        hidden = lax.optimization_barrier(hidden)
        lowered = jnp.dot(hidden, down_weight, preferred_element_type=jnp.float32)
        mixed = scatter_heads(lowered, head_id, head_total)
        outputs.append((stream_two.astype(jnp.float32) + mixed).astype(jnp.bfloat16))
    return jnp.concatenate(outputs, axis=0)

def solution(mesh):
    return jax.shard_map(
        shards,
        mesh=mesh,
        in_specs=(
            P(("groups", "bricks"), "heads"),
            P("groups"),
            P("groups", None),
            P(None, "heads"),
            P("heads"),
            P(),
            P(None, "heads"),
            P(None, "heads"),
            P(None, "heads"),
            P("heads", None),
            P(),
            P(None, "heads"),
            P("heads", None),
        ),
        out_specs=P(("groups", "bricks"), "heads"),
        check_vma=False,
    )
```
